32 devices in a mesh: group: 2 (over y), head: 4 (over x, core), seq: 4 (over z).
Axes of the slice: x: 2, y: 2, z: 4, core: 2. Of those that a mesh axis runs over, the one named last changes fastest.
Arguments:
- new_queries: bfloat16 [512, 4096], P(('group', 'seq'), 'head'), parts along dimension 0, may hold values from -80 to 80
- new_keys: bfloat16 [512, 1024], P(('group', 'seq'), 'head'), parts along dimension 0, may hold values from -6 to 6
- new_values: bfloat16 [512, 1024], P(('group', 'seq'), 'head'), parts along dimension 0, may hold values from -6 to 6
- cache_keys: bfloat16 [8192, 1024], P(('group', 'seq'), 'head'), parts along dimension 0, may hold values from -5 to 5
- cache_values: bfloat16 [8192, 1024], P(('group', 'seq'), 'head'), parts along dimension 0, may hold values from -6 to 6
- segment_ids: int32 [512], P('group'), parts along dimension 0, may hold values from 0 to 7, as said below
- cache_length: int32 [2], P('group'), parts along dimension 0, may hold values from 512 to 4096
Outputs:
- attended: bfloat16 [512, 4096], P(('group', 'seq'), 'head'), parts along dimension 0
The draws below stay inside these ranges and needn't reach their ends.
There are 2 independent parts, one for each index of `group`. The reference program is written for one: setup_inputs(seed, part) draws one part's arguments, and reference() takes and returns one part's arrays. A program takes and returns all parts, laid end to end along the dimension named above; each array names one. Nothing has to cross between parts.
Inputs may be any that keep to these rules, and one draw needn't show every extreme that they name: `segment_ids`: Non-decreasing along the positions; every number of 0 to 7 appears.
All inputs are finite; a program needn't handle non-finite values.
Results may differ from the reference program's by a relative error of at most 0.0024.
Values may be sent and summed in bfloat16 or wider, within the bound.
No kernel may reach another device: no remote copies, remote signals or barrier semaphores. Data moves between devices by JAX's collectives and lax.ppermute only.
A program may use at most 64 MiB of HBM per device.

```python
import jax
import jax.numpy as jnp
from jax import lax

Q_HEADS = 32
KV_HEADS = 8
HEAD_DIM = 128
SEGMENTS = 8
CACHE_DEV = 1024
JOIN = 256
CACHE = 4096
SUB = 256
N_SEQ = 4


def segment_table(key):
    small_cap = JOIN // (2 * (SEGMENTS - 1))
    small_sizes = jax.random.randint(jax.random.fold_in(key, 1), (SEGMENTS,), 1, small_cap + 1, dtype=jnp.int32)
    longest = jax.random.randint(jax.random.fold_in(key, 2), (), 0, SEGMENTS, dtype=jnp.int32)
    slots = jnp.arange(SEGMENTS, dtype=jnp.int32)
    small_sizes = jnp.where(slots == longest, 0, small_sizes).astype(jnp.int32)
    sizes_all = jnp.where(slots == longest, JOIN - jnp.sum(small_sizes), small_sizes).astype(jnp.int32)
    ends = jnp.cumsum(sizes_all).astype(jnp.int32)[:SEGMENTS - 1]
    positions = jnp.arange(JOIN, dtype=jnp.int32)
    return jnp.sum((positions[:, None] >= ends[None, :]).astype(jnp.int32), axis=1).astype(jnp.int32)


def topic_table(key):
    return 0.7 * jax.random.normal(jax.random.fold_in(key, 12), (SEGMENTS, KV_HEADS, HEAD_DIM), jnp.float32)


def draw_segment_ids(key, part):
    return segment_table(jax.random.fold_in(key, 11))


def draw_new_keys(key, part):
    segment_of = segment_table(jax.random.fold_in(key, 11))
    topics = topic_table(key)
    noise = 0.7 * jax.random.normal(jax.random.fold_in(key, 13), (JOIN, KV_HEADS, HEAD_DIM), jnp.float32)
    keys_drawn = topics[segment_of] + noise
    return jnp.clip(keys_drawn, -6.0, 6.0).reshape(JOIN, KV_HEADS * HEAD_DIM).astype(jnp.bfloat16)


def draw_new_queries(key, part):
    group_size = Q_HEADS // KV_HEADS
    segment_of = segment_table(jax.random.fold_in(key, 11))
    topics = topic_table(key)
    base = topics[segment_of][:, :, None, :]
    spread = jax.random.normal(jax.random.fold_in(key, 16), (JOIN, KV_HEADS, group_size, HEAD_DIM), jnp.float32)
    queries = base + 3.0 * spread
    return jnp.clip(queries, -80.0, 80.0).reshape(JOIN, Q_HEADS * HEAD_DIM).astype(jnp.bfloat16)


def draw_cache_keys(key, part):
    entries = jax.random.normal(jax.random.fold_in(key, 17), (CACHE, KV_HEADS, HEAD_DIM), jnp.float32)
    return jnp.clip(entries, -5.0, 5.0).reshape(CACHE, KV_HEADS * HEAD_DIM).astype(jnp.bfloat16)


def block_levels(own_key, shape, pieces, least, top_value):
    def one(dim, parts):
        steps = jax.random.uniform(jax.random.fold_in(jax.random.fold_in(own_key, 6), dim), (parts,), jnp.float32, least / len(pieces), top_value / len(pieces))
        return jnp.repeat(jnp.exp(steps), shape[dim] // parts).reshape((-1,) + (1,) * (len(shape) - dim - 1))

    level = one(*pieces[0])
    for cut in pieces[1:]:
        level = level * one(*cut)
    return level


def bell_draw(rng, dims, deviation, bound, cuts=(), held_as=jnp.bfloat16):
    drawn = deviation * jax.random.normal(rng, dims, jnp.float32)
    if cuts:
        drawn = drawn * block_levels(rng, dims, cuts, -0.22, 0.18)
    return jnp.clip(drawn, -bound, bound).astype(held_as)


def setup_inputs(seed: int = 0, part: int = 0) -> dict:
    keys = jax.random.split(jax.random.key(seed), 8)
    part_splits = jax.random.split(jax.random.fold_in(keys[7], part), 8)
    return {
        "new_queries": draw_new_queries(jax.random.fold_in(jax.random.fold_in(keys[7], part), 71), part),
        "new_keys": draw_new_keys(jax.random.fold_in(jax.random.fold_in(keys[7], part), 71), part),
        "new_values": bell_draw(part_splits[2], (JOIN, KV_HEADS * HEAD_DIM), 1.0, 6.0, ((0, 4), (1, 4))),
        "cache_keys": draw_cache_keys(jax.random.fold_in(jax.random.fold_in(keys[7], part), 71), part),
        "cache_values": bell_draw(part_splits[4], (CACHE, KV_HEADS * HEAD_DIM), 1.0, 6.0, ((0, 4), (1, 4))),
        "segment_ids": draw_segment_ids(jax.random.fold_in(jax.random.fold_in(keys[7], part), 71), part),
        "cache_length": jax.random.randint(part_splits[6], (1,), CACHE // 8, CACHE + 1).astype(jnp.int32),
    }


NEG_FILL = -1.0e30


def rounded(values):
    return lax.optimization_barrier(values.astype(jnp.bfloat16)).astype(jnp.float32)


def reference(new_queries, new_keys, new_values, cache_keys, cache_values, segment_ids, cache_length):
    group_size = Q_HEADS // KV_HEADS
    score_scale = HEAD_DIM ** -0.5
    limit_rows = cache_length[0]
    tile_total = CACHE_DEV // SUB
    queries = new_queries.astype(jnp.float32).reshape(JOIN, KV_HEADS, group_size, HEAD_DIM)
    fresh_keys = new_keys.astype(jnp.float32).reshape(JOIN, KV_HEADS, HEAD_DIM)
    fresh_values = new_values.astype(jnp.float32).reshape(JOIN, KV_HEADS, HEAD_DIM)
    old_keys = cache_keys.reshape(N_SEQ, CACHE_DEV, KV_HEADS, HEAD_DIM)
    old_values = cache_values.reshape(N_SEQ, CACHE_DEV, KV_HEADS, HEAD_DIM)
    starts = jnp.arange(N_SEQ, dtype=jnp.int32) * CACHE_DEV
    offsets = jnp.arange(CACHE_DEV, dtype=jnp.int32)
    positions = jnp.arange(JOIN, dtype=jnp.int32)
    allowed = (positions[None, :] <= positions[:, None]) & (segment_ids[None, :] == segment_ids[:, None])
    allowed = allowed[:, None, None, :]
    fresh_scores = jnp.einsum("cgrd,tgd->cgrt", queries, fresh_keys) * score_scale
    fresh_max = jnp.max(jnp.where(allowed, fresh_scores, NEG_FILL), axis=-1)

    def tiled(block_keys, start):
        scores = jnp.einsum("cgrd,tgd->cgrt", queries, block_keys.astype(jnp.float32)) * score_scale
        usable = ((start + offsets) < limit_rows).reshape(tile_total, SUB)
        split = scores.reshape(JOIN, KV_HEADS, group_size, tile_total, SUB)
        tile_max = jnp.max(jnp.where(usable, split, NEG_FILL), axis=-1)
        return split, usable, tile_max

    def max_step(best, block):
        block_keys, start = block
        tile_max = tiled(block_keys, start)[2]
        return jnp.maximum(best, jnp.max(tile_max, axis=-1)), None

    row_max = lax.scan(max_step, fresh_max, (old_keys, starts))[0]

    def sum_step(running, block):
        block_keys, block_values, start = block
        split, usable, tile_max = tiled(block_keys, start)
        weights = rounded(jnp.exp(jnp.where(usable, split - tile_max[..., None], NEG_FILL)))
        weights = weights * jnp.exp(tile_max - row_max[..., None])[..., None]
        numer_acc, denom_acc = running
        value_tiles = block_values.astype(jnp.float32).reshape(tile_total, SUB, KV_HEADS, HEAD_DIM)
        numer_acc = numer_acc + jnp.einsum("cgrbt,btgd->cgrd", weights, value_tiles)
        denom_acc = denom_acc + jnp.sum(weights, axis=(-2, -1))
        return (numer_acc, denom_acc), None

    start_state = (jnp.zeros((JOIN, KV_HEADS, group_size, HEAD_DIM), jnp.float32), jnp.zeros((JOIN, KV_HEADS, group_size), jnp.float32))
    cache_numer, cache_denom = lax.scan(sum_step, start_state, (old_keys, old_values, starts))[0]
    fresh_weights = rounded(jnp.exp(jnp.where(allowed, fresh_scores - fresh_max[..., None], NEG_FILL)))
    fresh_weights = fresh_weights * jnp.exp(fresh_max - row_max)[..., None]
    total_numer = cache_numer + jnp.einsum("cgrt,tgd->cgrd", fresh_weights, fresh_values)
    total_denom = cache_denom + jnp.sum(fresh_weights, axis=-1)
    attended = total_numer / total_denom[..., None]
    return attended.reshape(JOIN, Q_HEADS * HEAD_DIM).astype(jnp.bfloat16)
```

```python
import functools

import jax
import jax.numpy as jnp
from jax import lax
from jax.experimental import pallas as pl
from jax.experimental.pallas import tpu as pltpu
from jax.sharding import PartitionSpec as P

HEAD_DIM = 128
SUB = 256
NEG_FILL = -1e30


def cache_kernel(live_ref, q_ref, k_ref, v_ref, out_ref):
    live = live_ref[0]
    rows = q_ref.shape[0]
    heads_q = q_ref.shape[1] // HEAD_DIM
    heads_kv = k_ref.shape[1] // HEAD_DIM
    group = heads_q // heads_kv
    tiles = k_ref.shape[0] // SUB
    scale = HEAD_DIM ** (-0.5)
    col = lax.broadcasted_iota(jnp.int32, (rows, SUB), 1)
    lane = lax.broadcasted_iota(jnp.int32, (rows, 128), 1)
    extra = jnp.zeros((rows, 128), jnp.float32)
    for h in range(heads_q):
        g = h // group
        qh = q_ref[:, h * HEAD_DIM:(h + 1) * HEAD_DIM]
        maxes, numers, denoms = [], [], []
        for b in range(tiles):
            kb = k_ref[b * SUB:(b + 1) * SUB, g * HEAD_DIM:(g + 1) * HEAD_DIM]
            s = lax.dot_general(
                qh, kb, (((1,), (1,)), ((), ())), preferred_element_type=jnp.float32
            ) * scale
            ok = (col + b * SUB) < live
            tm = jnp.max(jnp.where(ok, s, NEG_FILL), axis=1, keepdims=True)
            w = jnp.exp(jnp.where(ok, s - tm, NEG_FILL)).astype(jnp.bfloat16)
            vb = v_ref[b * SUB:(b + 1) * SUB, g * HEAD_DIM:(g + 1) * HEAD_DIM]
            numers.append(jnp.dot(w, vb, preferred_element_type=jnp.float32))
            denoms.append(jnp.sum(w.astype(jnp.float32), axis=1, keepdims=True))
            maxes.append(tm)
        m = maxes[0]
        for tm in maxes[1:]:
            m = jnp.maximum(m, tm)
        numer = jnp.zeros((rows, HEAD_DIM), jnp.float32)
        denom = jnp.zeros((rows, 1), jnp.float32)
        for tm, nb, db in zip(maxes, numers, denoms):
            f = jnp.exp(tm - m)
            numer = numer + nb * f
            denom = denom + db * f
        out_ref[:, h * HEAD_DIM:(h + 1) * HEAD_DIM] = numer
        extra = jnp.where(lane == h, denom, extra)
        extra = jnp.where(lane == heads_q + h, m, extra)
    out_ref[:, heads_q * HEAD_DIM:] = extra


def cache_partials(live, queries, keys, values):
    rows, qcols = queries.shape
    cache_rows, kcols = keys.shape
    block = min(rows, 256)
    out_cols = qcols + 128
    heads_q = qcols // HEAD_DIM
    flops = 4 * rows * cache_rows * qcols
    return pl.pallas_call(
        cache_kernel,
        grid=(rows // block,),
        in_specs=[
            pl.BlockSpec(memory_space=pltpu.SMEM),
            pl.BlockSpec((block, qcols), lambda i: (i, 0)),
            pl.BlockSpec((cache_rows, kcols), lambda i: (0, 0)),
            pl.BlockSpec((cache_rows, kcols), lambda i: (0, 0)),
        ],
        out_specs=pl.BlockSpec((block, out_cols), lambda i: (i, 0)),
        out_shape=jax.ShapeDtypeStruct((rows, out_cols), jnp.float32),
        cost_estimate=pl.CostEstimate(
            flops=flops,
            transcendentals=rows * cache_rows * heads_q,
            bytes_accessed=2 * (rows * qcols + 2 * cache_rows * kcols) + 4 * rows * out_cols,
        ),
    )(live, queries, keys, values)


def on_device(
    new_queries, new_keys, new_values, cache_keys, cache_values, segment_ids, cache_length
):
    head_size = HEAD_DIM
    own_count = new_queries.shape[0]
    join_rows = segment_ids.shape[0]
    cache_rows = cache_keys.shape[0]
    heads_kv = cache_keys.shape[1] // head_size
    heads_q = new_queries.shape[1] // head_size
    group_size = heads_q // heads_kv
    qcols = heads_q * head_size
    kcols = heads_kv * head_size
    seq_count = lax.axis_size("seq")
    seq_rank = lax.axis_index("seq")
    score_scale = head_size ** (-0.5)

    packed = jnp.concatenate([new_queries, new_keys, new_values], axis=1)
    gathered = lax.all_gather(packed, "seq", axis=0, tiled=True)
    all_queries = gathered[:, :qcols]
    all_keys = gathered[:, qcols:qcols + kcols]
    all_values = gathered[:, qcols + kcols:]

    live_rows = jnp.clip(cache_length[0] - seq_rank * cache_rows, 0, cache_rows)
    partial = cache_partials(
        live_rows.reshape(1).astype(jnp.int32), all_queries, cache_keys, cache_values
    )

    if seq_count <= 8:
        chunks = partial.reshape(seq_count, own_count, qcols + 128)
        received = [lax.dynamic_index_in_dim(chunks, seq_rank, 0, keepdims=False)]
        for shift in range(1, seq_count):
            src = lax.rem(seq_rank + shift, seq_count)
            send = lax.dynamic_index_in_dim(chunks, src, 0, keepdims=False)
            received.append(
                lax.ppermute(
                    send, "seq", [(i, (i + shift) % seq_count) for i in range(seq_count)]
                )
            )
        recv = jnp.stack(received, axis=0)
    else:
        recv = lax.all_to_all(partial, "seq", 0, 0, tiled=True).reshape(
            seq_count, own_count, qcols + 128
        )
    part_numer = recv[:, :, :qcols].reshape(seq_count, own_count, heads_q, head_size)
    part_denom = recv[:, :, qcols:qcols + heads_q]
    part_max = recv[:, :, qcols + heads_q:qcols + 2 * heads_q]

    own_queries = new_queries.reshape(own_count, heads_kv, group_size, head_size)
    fresh_scores = (
        jnp.einsum(
            "cgrd,tgd->cgrt",
            own_queries,
            all_keys.reshape(join_rows, heads_kv, head_size),
            preferred_element_type=jnp.float32,
        )
        * score_scale
    )
    start_row = seq_rank * own_count
    own_positions = start_row + jnp.arange(own_count, dtype=jnp.int32)
    own_segments = lax.dynamic_slice_in_dim(segment_ids, start_row, own_count, 0)
    key_positions = jnp.arange(join_rows, dtype=jnp.int32)
    allowed = (key_positions[None, :] <= own_positions[:, None]) & (
        segment_ids[None, :] == own_segments[:, None]
    )
    allowed = allowed[:, None, None, :]
    fresh_max = jnp.max(jnp.where(allowed, fresh_scores, NEG_FILL), axis=-1)
    fresh_weights = jnp.exp(
        jnp.where(allowed, fresh_scores - fresh_max[..., None], NEG_FILL)
    ).astype(jnp.bfloat16)
    fresh_numer = jnp.einsum(
        "cgrt,tgd->cgrd",
        fresh_weights,
        all_values.reshape(join_rows, heads_kv, head_size),
        preferred_element_type=jnp.float32,
    ).reshape(own_count, heads_q, head_size)
    fresh_denom = jnp.sum(fresh_weights.astype(jnp.float32), axis=-1).reshape(own_count, heads_q)
    fresh_max = fresh_max.reshape(own_count, heads_q)

    row_max = jnp.maximum(fresh_max, jnp.max(part_max, axis=0))
    fresh_factor = jnp.exp(fresh_max - row_max)
    part_factor = jnp.exp(part_max - row_max[None])
    total_numer = fresh_numer * fresh_factor[..., None] + jnp.sum(
        part_numer * part_factor[..., None], axis=0
    )
    total_denom = fresh_denom * fresh_factor + jnp.sum(part_denom * part_factor, axis=0)
    attended = total_numer / total_denom[..., None]
    return attended.reshape(own_count, qcols).astype(jnp.bfloat16)


def solution(mesh):
    placed = (
        P(("group", "seq"), "head"),
        P(("group", "seq"), "head"),
        P(("group", "seq"), "head"),
        P(("group", "seq"), "head"),
        P(("group", "seq"), "head"),
        P("group"),
        P("group"),
    )
    return jax.shard_map(
        on_device,
        mesh=mesh,
        in_specs=placed,
        out_specs=P(("group", "seq"), "head"),
        check_vma=False,
    )
```

```python
import functools

import jax
import jax.numpy as jnp
from jax import lax
from jax.experimental import pallas as pl
from jax.experimental.pallas import tpu as pltpu
from jax.sharding import PartitionSpec as P

HEAD_DIM = 128
SUB = 256
NEG_FILL = -1e30


def cache_kernel(live_ref, q_ref, k_ref, v_ref, out_ref):
    live = live_ref[0]
    rows = q_ref.shape[0]
    heads_q = (out_ref.shape[1] - 128) // HEAD_DIM
    heads_kv = k_ref.shape[1] // HEAD_DIM
    group = heads_q // heads_kv
    tiles = k_ref.shape[0] // SUB
    scale = HEAD_DIM ** (-0.5)
    col = lax.broadcasted_iota(jnp.int32, (rows, SUB), 1)
    lane = lax.broadcasted_iota(jnp.int32, (rows, 128), 1)
    extra = jnp.zeros((rows, 128), jnp.float32)
    for h in range(heads_q):
        g = h // group
        qh = q_ref[:, h * HEAD_DIM:(h + 1) * HEAD_DIM]
        maxes, numers, denoms = [], [], []
        for b in range(tiles):
            kb = k_ref[b * SUB:(b + 1) * SUB, g * HEAD_DIM:(g + 1) * HEAD_DIM]
            s = lax.dot_general(
                qh, kb, (((1,), (1,)), ((), ())), preferred_element_type=jnp.float32
            ) * scale
            ok = (col + b * SUB) < live
            tm = jnp.max(jnp.where(ok, s, NEG_FILL), axis=1, keepdims=True)
            w = jnp.exp(jnp.where(ok, s - tm, NEG_FILL)).astype(jnp.bfloat16)
            vb = v_ref[b * SUB:(b + 1) * SUB, g * HEAD_DIM:(g + 1) * HEAD_DIM]
            numers.append(jnp.dot(w, vb, preferred_element_type=jnp.float32))
            denoms.append(jnp.sum(w.astype(jnp.float32), axis=1, keepdims=True))
            maxes.append(tm)
        m = maxes[0]
        for tm in maxes[1:]:
            m = jnp.maximum(m, tm)
        numer = jnp.zeros((rows, HEAD_DIM), jnp.float32)
        denom = jnp.zeros((rows, 1), jnp.float32)
        for tm, nb, db in zip(maxes, numers, denoms):
            f = jnp.exp(tm - m)
            numer = numer + nb * f
            denom = denom + db * f
        out_ref[:, h * HEAD_DIM:(h + 1) * HEAD_DIM] = numer
        extra = jnp.where(lane == h, denom, extra)
        extra = jnp.where(lane == heads_q + h, m, extra)
    out_ref[:, heads_q * HEAD_DIM:] = extra


def cache_partials(scalars, gathered, keys, values, block, chunked, qcols):
    rows, gcols = gathered.shape
    if chunked:
        rows = block
    cache_rows, kcols = keys.shape
    out_cols = qcols + 128
    heads_q = qcols // HEAD_DIM
    flops = 4 * rows * cache_rows * qcols
    if chunked:
        q_map = lambda i, s: (s[1], 0)
    else:
        q_map = lambda i, s: (i, 0)
    return pl.pallas_call(
        cache_kernel,
        grid_spec=pltpu.PrefetchScalarGridSpec(
            num_scalar_prefetch=1,
            grid=(rows // block,),
            in_specs=[
                pl.BlockSpec((block, gcols), q_map),
                pl.BlockSpec((cache_rows, kcols), lambda i, s: (0, 0)),
                pl.BlockSpec((cache_rows, kcols), lambda i, s: (0, 0)),
            ],
            out_specs=pl.BlockSpec((block, out_cols), lambda i, s: (i, 0)),
        ),
        out_shape=jax.ShapeDtypeStruct((rows, out_cols), jnp.float32),
        cost_estimate=pl.CostEstimate(
            flops=flops,
            transcendentals=rows * cache_rows * heads_q,
            bytes_accessed=2 * (rows * gcols + 2 * cache_rows * kcols) + 4 * rows * out_cols,
        ),
    )(scalars, gathered, keys, values)


def on_device(
    new_queries, new_keys, new_values, cache_keys, cache_values, segment_ids, cache_length
):
    head_size = HEAD_DIM
    own_count = new_queries.shape[0]
    join_rows = segment_ids.shape[0]
    cache_rows = cache_keys.shape[0]
    heads_kv = cache_keys.shape[1] // head_size
    heads_q = new_queries.shape[1] // head_size
    group_size = heads_q // heads_kv
    qcols = heads_q * head_size
    kcols = heads_kv * head_size
    seq_count = lax.axis_size("seq")
    seq_rank = lax.axis_index("seq")
    score_scale = head_size ** (-0.5)

    packed = jnp.concatenate([new_queries, new_keys, new_values], axis=1)
    gathered = lax.all_gather(packed, "seq", axis=0, tiled=True)
    all_keys = gathered[:, qcols:qcols + kcols]
    all_values = gathered[:, qcols + kcols:]

    live_rows = jnp.clip(cache_length[0] - seq_rank * cache_rows, 0, cache_rows)
    live_rows = live_rows.astype(jnp.int32)

    if seq_count <= 8:
        parts = []
        for shift in list(range(1, seq_count)) + [0]:
            chunk = lax.rem(seq_rank + shift, seq_count)
            scalars = jnp.stack([live_rows, chunk.astype(jnp.int32)])
            part = cache_partials(
                scalars, gathered, cache_keys, cache_values, own_count, True, qcols
            )
            if shift:
                part = lax.ppermute(
                    part, "seq", [(i, (i + shift) % seq_count) for i in range(seq_count)]
                )
            parts.append(part)
    else:
        scalars = jnp.stack([live_rows, jnp.zeros((), jnp.int32)])
        partial = cache_partials(
            scalars, gathered, cache_keys, cache_values, min(join_rows, 256), False, qcols
        )
        recv = lax.all_to_all(partial, "seq", 0, 0, tiled=True)
        parts = [recv[j * own_count:(j + 1) * own_count] for j in range(seq_count)]
    part_numer = [p[:, :qcols].reshape(own_count, heads_q, head_size) for p in parts]
    part_denom = [p[:, qcols:qcols + heads_q] for p in parts]
    part_max = [p[:, qcols + heads_q:qcols + 2 * heads_q] for p in parts]

    own_queries = new_queries.reshape(own_count, heads_kv, group_size, head_size)
    fresh_scores = (
        jnp.einsum(
            "cgrd,tgd->cgrt",
            own_queries,
            all_keys.reshape(join_rows, heads_kv, head_size),
            preferred_element_type=jnp.float32,
        )
        * score_scale
    )
    start_row = seq_rank * own_count
    own_positions = start_row + jnp.arange(own_count, dtype=jnp.int32)
    own_segments = lax.dynamic_slice_in_dim(segment_ids, start_row, own_count, 0)
    key_positions = jnp.arange(join_rows, dtype=jnp.int32)
    allowed = (key_positions[None, :] <= own_positions[:, None]) & (
        segment_ids[None, :] == own_segments[:, None]
    )
    allowed = allowed[:, None, None, :]
    fresh_max = jnp.max(jnp.where(allowed, fresh_scores, NEG_FILL), axis=-1)
    fresh_weights = jnp.exp(
        jnp.where(allowed, fresh_scores - fresh_max[..., None], NEG_FILL)
    ).astype(jnp.bfloat16)
    fresh_numer = jnp.einsum(
        "cgrt,tgd->cgrd",
        fresh_weights,
        all_values.reshape(join_rows, heads_kv, head_size),
        preferred_element_type=jnp.float32,
    ).reshape(own_count, heads_q, head_size)
    fresh_denom = jnp.sum(fresh_weights.astype(jnp.float32), axis=-1).reshape(own_count, heads_q)
    fresh_max = fresh_max.reshape(own_count, heads_q)

    row_max = fresh_max
    for m in part_max:
        row_max = jnp.maximum(row_max, m)
    fresh_factor = jnp.exp(fresh_max - row_max)
    total_numer = fresh_numer * fresh_factor[..., None]
    total_denom = fresh_denom * fresh_factor
    for n_j, d_j, m_j in zip(part_numer, part_denom, part_max):
        f_j = jnp.exp(m_j - row_max)
        total_numer = total_numer + n_j * f_j[..., None]
        total_denom = total_denom + d_j * f_j
    attended = total_numer / total_denom[..., None]
    return attended.reshape(own_count, qcols).astype(jnp.bfloat16)


def solution(mesh):
    placed = (
        P(("group", "seq"), "head"),
        P(("group", "seq"), "head"),
        P(("group", "seq"), "head"),
        P(("group", "seq"), "head"),
        P(("group", "seq"), "head"),
        P("group"),
        P("group"),
    )
    return jax.shard_map(
        on_device,
        mesh=mesh,
        in_specs=placed,
        out_specs=P(("group", "seq"), "head"),
        check_vma=False,
    )
```

```python
import functools

import jax
import jax.numpy as jnp
from jax import lax
from jax.experimental import pallas as pl
from jax.experimental.pallas import tpu as pltpu
from jax.sharding import PartitionSpec as P

HEAD_DIM = 128
SUB = 256
NEG_FILL = -1e30


def cache_kernel(scalar_ref, q_ref, kt_ref, v_ref, out_ref):
    live = scalar_ref[0]
    rows = q_ref.shape[0]
    heads_q = (out_ref.shape[1] - 128) // HEAD_DIM
    heads_kv = kt_ref.shape[0] // HEAD_DIM
    group = heads_q // heads_kv
    tiles = kt_ref.shape[1] // SUB
    scale = HEAD_DIM ** (-0.5)
    col = lax.broadcasted_iota(jnp.int32, (group * rows, SUB), 1)
    lane = lax.broadcasted_iota(jnp.int32, (rows, 128), 1)
    extra = jnp.zeros((rows, 128), jnp.float32)
    for g in range(heads_kv):
        qg = jnp.concatenate(
            [q_ref[:, (g * group + r) * HEAD_DIM:(g * group + r + 1) * HEAD_DIM] for r in range(group)],
            axis=0,
        )
        maxes, numers, denoms = [], [], []
        for b in range(tiles):
            kb = kt_ref[g * HEAD_DIM:(g + 1) * HEAD_DIM, b * SUB:(b + 1) * SUB]
            s = jnp.dot(qg, kb, preferred_element_type=jnp.float32) * scale
            ok = (col + b * SUB) < live
            tm = jnp.max(jnp.where(ok, s, NEG_FILL), axis=1, keepdims=True)
            w = jnp.exp(jnp.where(ok, s - tm, NEG_FILL)).astype(jnp.bfloat16)
            vb = v_ref[b * SUB:(b + 1) * SUB, g * HEAD_DIM:(g + 1) * HEAD_DIM]
            numers.append(jnp.dot(w, vb, preferred_element_type=jnp.float32))
            denoms.append(jnp.sum(w.astype(jnp.float32), axis=1, keepdims=True))
            maxes.append(tm)
        m = maxes[0]
        for tm in maxes[1:]:
            m = jnp.maximum(m, tm)
        numer = jnp.zeros((group * rows, HEAD_DIM), jnp.float32)
        denom = jnp.zeros((group * rows, 1), jnp.float32)
        for tm, nb, db in zip(maxes, numers, denoms):
            f = jnp.exp(tm - m)
            numer = numer + nb * f
            denom = denom + db * f
        for r in range(group):
            h = g * group + r
            out_ref[:, h * HEAD_DIM:(h + 1) * HEAD_DIM] = numer[r * rows:(r + 1) * rows]
            extra = jnp.where(lane == h, denom[r * rows:(r + 1) * rows], extra)
            extra = jnp.where(lane == heads_q + h, m[r * rows:(r + 1) * rows], extra)
    out_ref[:, heads_q * HEAD_DIM:] = extra


def cache_partials(scalars, gathered, keys, values, block, chunked, qcols):
    rows, gcols = gathered.shape
    if chunked:
        rows = block
    kcols, cache_rows = keys.shape
    out_cols = qcols + 128
    heads_q = qcols // HEAD_DIM
    flops = 4 * rows * cache_rows * qcols
    if chunked:
        q_map = lambda i, s: (s[1], 0)
    else:
        q_map = lambda i, s: (i, 0)
    return pl.pallas_call(
        cache_kernel,
        grid_spec=pltpu.PrefetchScalarGridSpec(
            num_scalar_prefetch=1,
            grid=(rows // block,),
            in_specs=[
                pl.BlockSpec((block, gcols), q_map),
                pl.BlockSpec((kcols, cache_rows), lambda i, s: (0, 0)),
                pl.BlockSpec((cache_rows, kcols), lambda i, s: (0, 0)),
            ],
            out_specs=pl.BlockSpec((block, out_cols), lambda i, s: (i, 0)),
        ),
        out_shape=jax.ShapeDtypeStruct((rows, out_cols), jnp.float32),
        cost_estimate=pl.CostEstimate(
            flops=flops,
            transcendentals=rows * cache_rows * heads_q,
            bytes_accessed=2 * (rows * gcols + 2 * cache_rows * kcols) + 4 * rows * out_cols,
        ),
    )(scalars, gathered, keys, values)


def on_device(
    new_queries, new_keys, new_values, cache_keys, cache_values, segment_ids, cache_length
):
    head_size = HEAD_DIM
    own_count = new_queries.shape[0]
    join_rows = segment_ids.shape[0]
    cache_rows = cache_keys.shape[0]
    heads_kv = cache_keys.shape[1] // head_size
    heads_q = new_queries.shape[1] // head_size
    group_size = heads_q // heads_kv
    qcols = heads_q * head_size
    kcols = heads_kv * head_size
    seq_count = lax.axis_size("seq")
    seq_rank = lax.axis_index("seq")
    score_scale = head_size ** (-0.5)

    packed = jnp.concatenate([new_queries, new_keys, new_values], axis=1)
    gathered = lax.all_gather(packed, "seq", axis=0, tiled=True)
    all_keys = gathered[:, qcols:qcols + kcols]
    all_values = gathered[:, qcols + kcols:]

    live_rows = jnp.clip(cache_length[0] - seq_rank * cache_rows, 0, cache_rows)
    live_rows = live_rows.astype(jnp.int32)
    keys_t = cache_keys.T

    if seq_count <= 8:
        parts = []
        for shift in list(range(1, seq_count)) + [0]:
            chunk = lax.rem(seq_rank + shift, seq_count)
            scalars = jnp.stack([live_rows, chunk.astype(jnp.int32)])
            part = cache_partials(
                scalars, gathered, keys_t, cache_values, own_count, True, qcols
            )
            if shift:
                part = lax.ppermute(
                    part, "seq", [(i, (i + shift) % seq_count) for i in range(seq_count)]
                )
            parts.append(part)
    else:
        scalars = jnp.stack([live_rows, jnp.zeros((), jnp.int32)])
        partial = cache_partials(
            scalars, gathered, keys_t, cache_values, min(join_rows, 256), False, qcols
        )
        recv = lax.all_to_all(partial, "seq", 0, 0, tiled=True)
        parts = [recv[j * own_count:(j + 1) * own_count] for j in range(seq_count)]
    part_numer = [p[:, :qcols].reshape(own_count, heads_q, head_size) for p in parts]
    part_denom = [p[:, qcols:qcols + heads_q] for p in parts]
    part_max = [p[:, qcols + heads_q:qcols + 2 * heads_q] for p in parts]

    own_queries = new_queries.reshape(own_count, heads_kv, group_size, head_size)
    fresh_scores = (
        jnp.einsum(
            "cgrd,tgd->cgrt",
            own_queries,
            all_keys.reshape(join_rows, heads_kv, head_size),
            preferred_element_type=jnp.float32,
        )
        * score_scale
    )
    start_row = seq_rank * own_count
    own_positions = start_row + jnp.arange(own_count, dtype=jnp.int32)
    own_segments = lax.dynamic_slice_in_dim(segment_ids, start_row, own_count, 0)
    key_positions = jnp.arange(join_rows, dtype=jnp.int32)
    allowed = (key_positions[None, :] <= own_positions[:, None]) & (
        segment_ids[None, :] == own_segments[:, None]
    )
    allowed = allowed[:, None, None, :]
    fresh_max = jnp.max(jnp.where(allowed, fresh_scores, NEG_FILL), axis=-1)
    fresh_weights = jnp.exp(
        jnp.where(allowed, fresh_scores - fresh_max[..., None], NEG_FILL)
    ).astype(jnp.bfloat16)
    fresh_numer = jnp.einsum(
        "cgrt,tgd->cgrd",
        fresh_weights,
        all_values.reshape(join_rows, heads_kv, head_size),
        preferred_element_type=jnp.float32,
    ).reshape(own_count, heads_q, head_size)
    fresh_denom = jnp.sum(fresh_weights.astype(jnp.float32), axis=-1).reshape(own_count, heads_q)
    fresh_max = fresh_max.reshape(own_count, heads_q)

    row_max = fresh_max
    for m in part_max:
        row_max = jnp.maximum(row_max, m)
    fresh_factor = jnp.exp(fresh_max - row_max)
    total_numer = fresh_numer * fresh_factor[..., None]
    total_denom = fresh_denom * fresh_factor
    for n_j, d_j, m_j in zip(part_numer, part_denom, part_max):
        f_j = jnp.exp(m_j - row_max)
        total_numer = total_numer + n_j * f_j[..., None]
        total_denom = total_denom + d_j * f_j
    attended = total_numer / total_denom[..., None]
    return attended.reshape(own_count, qcols).astype(jnp.bfloat16)


def solution(mesh):
    placed = (
        P(("group", "seq"), "head"),
        P(("group", "seq"), "head"),
        P(("group", "seq"), "head"),
        P(("group", "seq"), "head"),
        P(("group", "seq"), "head"),
        P("group"),
        P("group"),
    )
    return jax.shard_map(
        on_device,
        mesh=mesh,
        in_specs=placed,
        out_specs=P(("group", "seq"), "head"),
        check_vma=False,
    )
```

```python
import functools

import jax
import jax.numpy as jnp
from jax import lax
from jax.experimental import pallas as pl
from jax.experimental.pallas import tpu as pltpu
from jax.sharding import PartitionSpec as P

HEAD_DIM = 128
SUB = 256
NEG_FILL = -1e30


def cache_kernel(scalar_ref, q_ref, kt_ref, v_ref, out_ref):
    live = scalar_ref[0]
    rows = q_ref.shape[0]
    heads_q = (out_ref.shape[1] - 128) // HEAD_DIM
    heads_kv = kt_ref.shape[0] // HEAD_DIM
    group = heads_q // heads_kv
    tiles = kt_ref.shape[1] // SUB
    scale = HEAD_DIM ** (-0.5)
    col = lax.broadcasted_iota(jnp.int32, (group * rows, SUB), 1)
    lane = lax.broadcasted_iota(jnp.int32, (rows, 128), 1)
    extra = jnp.zeros((rows, 128), jnp.float32)
    for g in range(heads_kv):
        qg = jnp.concatenate(
            [q_ref[:, (g * group + r) * HEAD_DIM:(g * group + r + 1) * HEAD_DIM] for r in range(group)],
            axis=0,
        )
        maxes, numers, denoms = [], [], []
        for b in range(tiles):
            kb = kt_ref[g * HEAD_DIM:(g + 1) * HEAD_DIM, b * SUB:(b + 1) * SUB]
            s = jnp.dot(qg, kb, preferred_element_type=jnp.float32) * scale
            ok = (col + b * SUB) < live
            tm = jnp.max(jnp.where(ok, s, NEG_FILL), axis=1, keepdims=True)
            w = jnp.exp(jnp.where(ok, s - tm, NEG_FILL)).astype(jnp.bfloat16)
            vb = v_ref[b * SUB:(b + 1) * SUB, g * HEAD_DIM:(g + 1) * HEAD_DIM]
            numers.append(jnp.dot(w, vb, preferred_element_type=jnp.float32))
            denoms.append(jnp.sum(w.astype(jnp.float32), axis=1, keepdims=True))
            maxes.append(tm)
        m = maxes[0]
        for tm in maxes[1:]:
            m = jnp.maximum(m, tm)
        numer = jnp.zeros((group * rows, HEAD_DIM), jnp.float32)
        denom = jnp.zeros((group * rows, 1), jnp.float32)
        for tm, nb, db in zip(maxes, numers, denoms):
            f = jnp.exp(tm - m)
            numer = numer + nb * f
            denom = denom + db * f
        top = jnp.floor(jnp.maximum(m, -60000.0) * 0.25 + 0.5) * 4.0
        f = jnp.exp(m - top)
        numer = numer * f
        denom = denom * f
        mean = numer / jnp.where(denom > 0, denom, 1.0)
        for r in range(group):
            h = g * group + r
            rs = slice(r * rows, (r + 1) * rows)
            out_ref[:, h * HEAD_DIM:(h + 1) * HEAD_DIM] = mean[rs]
            extra = jnp.where((lane == h) | (lane == heads_q + h), denom[rs], extra)
            extra = jnp.where(lane == 2 * heads_q + h, top[rs], extra)
    out_ref[:, heads_q * HEAD_DIM:] = extra


def to_half(part, qcols, heads_q):
    extra = part[:, qcols:]
    rounded = extra.astype(jnp.float16)
    rest = (extra - rounded.astype(jnp.float32)).astype(jnp.float16)
    lane = lax.broadcasted_iota(jnp.int32, extra.shape, 1)
    second = (lane >= heads_q) & (lane < 2 * heads_q)
    return jnp.concatenate(
        [part[:, :qcols].astype(jnp.float16), jnp.where(second, rest, rounded)], axis=1
    )


def cache_partials(scalars, gathered, keys, values, block, chunked, qcols, slot):
    rows, gcols = gathered.shape
    if chunked:
        rows = block
    kcols, cache_rows = keys.shape
    out_cols = qcols + 128
    heads_q = qcols // HEAD_DIM
    flops = 4 * rows * cache_rows * qcols
    if chunked:
        q_map = lambda i, s: (s[slot], 0)
    else:
        q_map = lambda i, s: (i, 0)
    return pl.pallas_call(
        cache_kernel,
        grid_spec=pltpu.PrefetchScalarGridSpec(
            num_scalar_prefetch=1,
            grid=(rows // block,),
            in_specs=[
                pl.BlockSpec((block, gcols), q_map),
                pl.BlockSpec((kcols, cache_rows), lambda i, s: (0, 0)),
                pl.BlockSpec((cache_rows, kcols), lambda i, s: (0, 0)),
            ],
            out_specs=pl.BlockSpec((block, out_cols), lambda i, s: (i, 0)),
        ),
        out_shape=jax.ShapeDtypeStruct((rows, out_cols), jnp.float32),
        cost_estimate=pl.CostEstimate(
            flops=flops,
            transcendentals=rows * cache_rows * heads_q,
            bytes_accessed=2 * (rows * gcols + 2 * cache_rows * kcols) + 4 * rows * out_cols,
        ),
    )(scalars, gathered, keys, values)


def on_device(
    new_queries, new_keys, new_values, cache_keys, cache_values, segment_ids, cache_length
):
    head_size = HEAD_DIM
    own_count = new_queries.shape[0]
    join_rows = segment_ids.shape[0]
    cache_rows = cache_keys.shape[0]
    heads_kv = cache_keys.shape[1] // head_size
    heads_q = new_queries.shape[1] // head_size
    group_size = heads_q // heads_kv
    qcols = heads_q * head_size
    kcols = heads_kv * head_size
    seq_count = lax.axis_size("seq")
    seq_rank = lax.axis_index("seq")
    score_scale = head_size ** (-0.5)

    packed = jnp.concatenate([new_queries, new_keys, new_values], axis=1)
    gathered = lax.all_gather(packed, "seq", axis=0, tiled=True)
    all_keys = gathered[:, qcols:qcols + kcols]
    all_values = gathered[:, qcols + kcols:]

    live_rows = jnp.clip(cache_length[0] - seq_rank * cache_rows, 0, cache_rows)
    live_rows = live_rows.astype(jnp.int32)
    keys_t = cache_keys.T

    if seq_count <= 8:
        shifts = list(range(1, seq_count)) + [0]
        scalars = jnp.stack(
            [live_rows] + [lax.rem(seq_rank + s, seq_count).astype(jnp.int32) for s in shifts]
        )
        parts = []
        for slot, shift in enumerate(shifts):
            part = cache_partials(
                scalars, gathered, keys_t, cache_values, own_count, True, qcols, slot + 1
            )
            part = to_half(part, qcols, heads_q)
            if shift:
                part = lax.ppermute(
                    part, "seq", [(i, (i + shift) % seq_count) for i in range(seq_count)]
                )
            parts.append(part)
    else:
        scalars = jnp.stack([live_rows, jnp.zeros((), jnp.int32)])
        partial = cache_partials(
            scalars, gathered, keys_t, cache_values, min(join_rows, 256), False, qcols, 1
        )
        recv = lax.all_to_all(to_half(partial, qcols, heads_q), "seq", 0, 0, tiled=True)
        parts = [recv[j * own_count:(j + 1) * own_count] for j in range(seq_count)]
    parts = [p.astype(jnp.float32) for p in parts]
    part_mean = [p[:, :qcols].reshape(own_count, heads_q, head_size) for p in parts]
    part_denom = [
        p[:, qcols:qcols + heads_q] + p[:, qcols + heads_q:qcols + 2 * heads_q] for p in parts
    ]
    part_max = [p[:, qcols + 2 * heads_q:qcols + 3 * heads_q] for p in parts]

    own_queries = new_queries.reshape(own_count, heads_kv, group_size, head_size)
    fresh_scores = (
        jnp.einsum(
            "cgrd,tgd->cgrt",
            own_queries,
            all_keys.reshape(join_rows, heads_kv, head_size),
            preferred_element_type=jnp.float32,
        )
        * score_scale
    )
    start_row = seq_rank * own_count
    own_positions = start_row + jnp.arange(own_count, dtype=jnp.int32)
    own_segments = lax.dynamic_slice_in_dim(segment_ids, start_row, own_count, 0)
    key_positions = jnp.arange(join_rows, dtype=jnp.int32)
    allowed = (key_positions[None, :] <= own_positions[:, None]) & (
        segment_ids[None, :] == own_segments[:, None]
    )
    allowed = allowed[:, None, None, :]
    fresh_max = jnp.max(jnp.where(allowed, fresh_scores, NEG_FILL), axis=-1)
    fresh_weights = jnp.exp(
        jnp.where(allowed, fresh_scores - fresh_max[..., None], NEG_FILL)
    ).astype(jnp.bfloat16)
    fresh_numer = jnp.einsum(
        "cgrt,tgd->cgrd",
        fresh_weights,
        all_values.reshape(join_rows, heads_kv, head_size),
        preferred_element_type=jnp.float32,
    ).reshape(own_count, heads_q, head_size)
    fresh_denom = jnp.sum(fresh_weights.astype(jnp.float32), axis=-1).reshape(own_count, heads_q)
    fresh_max = fresh_max.reshape(own_count, heads_q)

    row_max = fresh_max
    for m in part_max:
        row_max = jnp.maximum(row_max, m)
    fresh_factor = jnp.exp(fresh_max - row_max)
    total_numer = fresh_numer * fresh_factor[..., None]
    total_denom = fresh_denom * fresh_factor
    for o_j, d_j, m_j in zip(part_mean, part_denom, part_max):
        w_j = jnp.exp(m_j - row_max) * d_j
        total_numer = total_numer + o_j * w_j[..., None]
        total_denom = total_denom + w_j
    attended = total_numer / total_denom[..., None]
    return attended.reshape(own_count, qcols).astype(jnp.bfloat16)


def solution(mesh):
    placed = (
        P(("group", "seq"), "head"),
        P(("group", "seq"), "head"),
        P(("group", "seq"), "head"),
        P(("group", "seq"), "head"),
        P(("group", "seq"), "head"),
        P("group"),
        P("group"),
    )
    return jax.shard_map(
        on_device,
        mesh=mesh,
        in_specs=placed,
        out_specs=P(("group", "seq"), "head"),
        check_vma=False,
    )
```

```python
import functools

import jax
import jax.numpy as jnp
from jax import lax
from jax.experimental import pallas as pl
from jax.experimental.pallas import tpu as pltpu
from jax.sharding import PartitionSpec as P

HEAD_DIM = 128
SUB = 256
NEG_FILL = -1e30


def cache_kernel(scalar_ref, q_ref, k_ref, v_ref, out_ref):
    live = scalar_ref[0]
    rows = q_ref.shape[0]
    heads_q = (out_ref.shape[1] - 128) // HEAD_DIM
    heads_kv = k_ref.shape[1] // HEAD_DIM
    group = heads_q // heads_kv
    tiles = k_ref.shape[0] // SUB
    ones = jnp.ones((SUB, 128), jnp.bfloat16)
    scale = HEAD_DIM ** (-0.5)
    col = lax.broadcasted_iota(jnp.int32, (group * rows, SUB), 1)
    lane = lax.broadcasted_iota(jnp.int32, (rows, 128), 1)
    extra = jnp.zeros((rows, 128), jnp.float32)
    for g in range(heads_kv):
        qg = jnp.concatenate(
            [q_ref[:, (g * group + r) * HEAD_DIM:(g * group + r + 1) * HEAD_DIM] for r in range(group)],
            axis=0,
        )
        maxes, numers, denoms = [], [], []
        for b in range(tiles):
            kb = k_ref[b * SUB:(b + 1) * SUB, g * HEAD_DIM:(g + 1) * HEAD_DIM]
            s = lax.dot_general(
                qg, kb, (((1,), (1,)), ((), ())), preferred_element_type=jnp.float32
            ) * scale
            ok = (col + b * SUB) < live
            tm = jnp.max(jnp.where(ok, s, NEG_FILL), axis=1, keepdims=True)
            w = jnp.exp(jnp.where(ok, s - tm, NEG_FILL)).astype(jnp.bfloat16)
            vb = v_ref[b * SUB:(b + 1) * SUB, g * HEAD_DIM:(g + 1) * HEAD_DIM]
            numers.append(jnp.dot(w, vb, preferred_element_type=jnp.float32))
            denoms.append(jnp.dot(w, ones, preferred_element_type=jnp.float32)[:, :1])
            maxes.append(tm)
        m = maxes[0]
        for tm in maxes[1:]:
            m = jnp.maximum(m, tm)
        numer = jnp.zeros((group * rows, HEAD_DIM), jnp.float32)
        denom = jnp.zeros((group * rows, 1), jnp.float32)
        for tm, nb, db in zip(maxes, numers, denoms):
            f = jnp.exp(tm - m)
            numer = numer + nb * f
            denom = denom + db * f
        top = jnp.floor(jnp.maximum(m, -60000.0) * 0.25 + 0.5) * 4.0
        f = jnp.exp(m - top)
        numer = numer * f
        denom = denom * f
        mean = numer / jnp.where(denom > 0, denom, 1.0)
        for r in range(group):
            h = g * group + r
            rs = slice(r * rows, (r + 1) * rows)
            out_ref[:, h * HEAD_DIM:(h + 1) * HEAD_DIM] = mean[rs]
            extra = jnp.where((lane == h) | (lane == heads_q + h), denom[rs], extra)
            extra = jnp.where(lane == 2 * heads_q + h, top[rs], extra)
    out_ref[:, heads_q * HEAD_DIM:] = extra


def to_half(part, qcols, heads_q):
    extra = part[:, qcols:]
    rounded = extra.astype(jnp.float16)
    rest = (extra - rounded.astype(jnp.float32)).astype(jnp.float16)
    lane = lax.broadcasted_iota(jnp.int32, extra.shape, 1)
    second = (lane >= heads_q) & (lane < 2 * heads_q)
    return jnp.concatenate(
        [part[:, :qcols].astype(jnp.float16), jnp.where(second, rest, rounded)], axis=1
    )


def cache_partials(scalars, gathered, keys, values, block, first_slot, count, qcols):
    gcols = gathered.shape[1]
    rows = block * count
    cache_rows, kcols = keys.shape
    out_cols = qcols + 128
    heads_q = qcols // HEAD_DIM
    flops = 4 * rows * cache_rows * qcols + 2 * rows * cache_rows * 128 * (qcols // HEAD_DIM)
    return pl.pallas_call(
        cache_kernel,
        grid_spec=pltpu.PrefetchScalarGridSpec(
            num_scalar_prefetch=1,
            grid=(count,),
            in_specs=[
                pl.BlockSpec((block, gcols), lambda i, s: (s[first_slot + i], 0)),
                pl.BlockSpec((cache_rows, kcols), lambda i, s: (0, 0)),
                pl.BlockSpec((cache_rows, kcols), lambda i, s: (0, 0)),
            ],
            out_specs=pl.BlockSpec((block, out_cols), lambda i, s: (i, 0)),
        ),
        out_shape=jax.ShapeDtypeStruct((rows, out_cols), jnp.float32),
        cost_estimate=pl.CostEstimate(
            flops=flops,
            transcendentals=rows * cache_rows * heads_q,
            bytes_accessed=2 * (rows * gcols + 2 * cache_rows * kcols) + 4 * rows * out_cols,
        ),
    )(scalars, gathered, keys, values)


def on_device(
    new_queries, new_keys, new_values, cache_keys, cache_values, segment_ids, cache_length
):
    head_size = HEAD_DIM
    own_count = new_queries.shape[0]
    join_rows = segment_ids.shape[0]
    cache_rows = cache_keys.shape[0]
    heads_kv = cache_keys.shape[1] // head_size
    heads_q = new_queries.shape[1] // head_size
    group_size = heads_q // heads_kv
    qcols = heads_q * head_size
    kcols = heads_kv * head_size
    seq_count = lax.axis_size("seq")
    seq_rank = lax.axis_index("seq")
    score_scale = head_size ** (-0.5)

    packed = jnp.concatenate([new_queries, new_keys, new_values], axis=1)
    gathered = lax.all_gather(packed, "seq", axis=0, tiled=True)
    all_keys = gathered[:, qcols:qcols + kcols]
    all_values = gathered[:, qcols + kcols:]

    live_rows = jnp.clip(cache_length[0] - seq_rank * cache_rows, 0, cache_rows)
    live_rows = live_rows.astype(jnp.int32)

    if seq_count <= 8:
        shifts = list(range(1, seq_count))
        scalars = jnp.stack(
            [live_rows]
            + [lax.rem(seq_rank + s, seq_count).astype(jnp.int32) for s in shifts]
            + [seq_rank.astype(jnp.int32)]
        )
        remote = cache_partials(
            scalars, gathered, cache_keys, cache_values, own_count, 1, seq_count - 1, qcols
        )
        parts = []
        for k, shift in enumerate(shifts):
            part = to_half(remote[k * own_count:(k + 1) * own_count], qcols, heads_q)
            parts.append(
                lax.ppermute(
                    part, "seq", [(i, (i + shift) % seq_count) for i in range(seq_count)]
                )
            )
        own = cache_partials(
            scalars, gathered, cache_keys, cache_values, own_count, seq_count, 1, qcols
        )
        parts.append(to_half(own, qcols, heads_q))
    else:
        scalars = jnp.stack([live_rows] + [jnp.int32(j) for j in range(join_rows // 256)])
        partial = cache_partials(
            scalars, gathered, cache_keys, cache_values, 256, 1, join_rows // 256, qcols
        )
        recv = lax.all_to_all(to_half(partial, qcols, heads_q), "seq", 0, 0, tiled=True)
        parts = [recv[j * own_count:(j + 1) * own_count] for j in range(seq_count)]
    parts = [p.astype(jnp.float32) for p in parts]
    part_mean = [p[:, :qcols].reshape(own_count, heads_q, head_size) for p in parts]
    part_denom = [
        p[:, qcols:qcols + heads_q] + p[:, qcols + heads_q:qcols + 2 * heads_q] for p in parts
    ]
    part_max = [p[:, qcols + 2 * heads_q:qcols + 3 * heads_q] for p in parts]

    own_queries = new_queries.reshape(own_count, heads_kv, group_size, head_size)
    fresh_scores = (
        jnp.einsum(
            "cgrd,tgd->cgrt",
            own_queries,
            all_keys.reshape(join_rows, heads_kv, head_size),
            preferred_element_type=jnp.float32,
        )
        * score_scale
    )
    start_row = seq_rank * own_count
    own_positions = start_row + jnp.arange(own_count, dtype=jnp.int32)
    own_segments = lax.dynamic_slice_in_dim(segment_ids, start_row, own_count, 0)
    key_positions = jnp.arange(join_rows, dtype=jnp.int32)
    allowed = (key_positions[None, :] <= own_positions[:, None]) & (
        segment_ids[None, :] == own_segments[:, None]
    )
    allowed = allowed[:, None, None, :]
    fresh_max = jnp.max(jnp.where(allowed, fresh_scores, NEG_FILL), axis=-1)
    fresh_weights = jnp.exp(
        jnp.where(allowed, fresh_scores - fresh_max[..., None], NEG_FILL)
    ).astype(jnp.bfloat16)
    fresh_numer = jnp.einsum(
        "cgrt,tgd->cgrd",
        fresh_weights,
        all_values.reshape(join_rows, heads_kv, head_size),
        preferred_element_type=jnp.float32,
    ).reshape(own_count, heads_q, head_size)
    fresh_denom = jnp.sum(fresh_weights.astype(jnp.float32), axis=-1).reshape(own_count, heads_q)
    fresh_max = fresh_max.reshape(own_count, heads_q)

    row_max = fresh_max
    for m in part_max:
        row_max = jnp.maximum(row_max, m)
    fresh_factor = jnp.exp(fresh_max - row_max)
    total_numer = fresh_numer * fresh_factor[..., None]
    total_denom = fresh_denom * fresh_factor
    for o_j, d_j, m_j in zip(part_mean, part_denom, part_max):
        w_j = jnp.exp(m_j - row_max) * d_j
        total_numer = total_numer + o_j * w_j[..., None]
        total_denom = total_denom + w_j
    attended = total_numer / total_denom[..., None]
    return attended.reshape(own_count, qcols).astype(jnp.bfloat16)


def solution(mesh):
    placed = (
        P(("group", "seq"), "head"),
        P(("group", "seq"), "head"),
        P(("group", "seq"), "head"),
        P(("group", "seq"), "head"),
        P(("group", "seq"), "head"),
        P("group"),
        P("group"),
    )
    return jax.shard_map(
        on_device,
        mesh=mesh,
        in_specs=placed,
        out_specs=P(("group", "seq"), "head"),
        check_vma=False,
    )
```

```python
import functools

import jax
import jax.numpy as jnp
from jax import lax
from jax.experimental import pallas as pl
from jax.experimental.pallas import tpu as pltpu
from jax.sharding import PartitionSpec as P

HEAD_DIM = 128
SUB = 256
NEG_FILL = -1e30


def cache_kernel(pieces, scalar_ref, q_ref, k_ref, v_ref, out_ref):
    live = scalar_ref[0]
    rows = out_ref.shape[0]
    piece = rows // pieces
    heads_q = (out_ref.shape[1] - 128) // HEAD_DIM
    heads_kv = k_ref.shape[1] // HEAD_DIM
    group = heads_q // heads_kv
    tiles = k_ref.shape[0] // SUB
    scale = HEAD_DIM ** (-0.5)
    col = lax.broadcasted_iota(jnp.int32, (rows, SUB), 1)
    lane = lax.broadcasted_iota(jnp.int32, (rows, 128), 1)
    extra = jnp.zeros((rows, 128), jnp.float32)
    for h in range(heads_q):
        g = h // group
        cols = slice(h * HEAD_DIM, (h + 1) * HEAD_DIM)
        if pieces > 1:
            qh = jnp.concatenate(
                [
                    q_ref[pl.ds(pl.multiple_of(scalar_ref[1 + p] * piece, piece), piece), cols]
                    for p in range(pieces)
                ],
                axis=0,
            )
        else:
            qh = q_ref[:, cols]
        maxes, numers, denoms = [], [], []
        for b in range(tiles):
            kb = k_ref[b * SUB:(b + 1) * SUB, g * HEAD_DIM:(g + 1) * HEAD_DIM]
            s = lax.dot_general(
                qh, kb, (((1,), (1,)), ((), ())), preferred_element_type=jnp.float32
            ) * scale
            ok = (col + b * SUB) < live
            tm = jnp.max(jnp.where(ok, s, NEG_FILL), axis=1, keepdims=True)
            w = jnp.exp(jnp.where(ok, s - tm, NEG_FILL)).astype(jnp.bfloat16)
            vb = v_ref[b * SUB:(b + 1) * SUB, g * HEAD_DIM:(g + 1) * HEAD_DIM]
            numers.append(jnp.dot(w, vb, preferred_element_type=jnp.float32))
            denoms.append(jnp.sum(w.astype(jnp.float32), axis=1, keepdims=True))
            maxes.append(tm)
        m = maxes[0]
        for tm in maxes[1:]:
            m = jnp.maximum(m, tm)
        numer = jnp.zeros((rows, HEAD_DIM), jnp.float32)
        denom = jnp.zeros((rows, 1), jnp.float32)
        for tm, nb, db in zip(maxes, numers, denoms):
            f = jnp.exp(tm - m)
            numer = numer + nb * f
            denom = denom + db * f
        top = jnp.floor(jnp.maximum(m, -60000.0) * 0.25 + 0.5) * 4.0
        f = jnp.exp(m - top)
        numer = numer * f
        denom = denom * f
        out_ref[:, cols] = numer / jnp.where(denom > 0, denom, 1.0)
        extra = jnp.where((lane == h) | (lane == heads_q + h), denom, extra)
        extra = jnp.where(lane == 2 * heads_q + h, top, extra)
    out_ref[:, heads_q * HEAD_DIM:] = extra


def to_half(part, qcols, heads_q):
    extra = part[:, qcols:]
    rounded = extra.astype(jnp.float16)
    rest = (extra - rounded.astype(jnp.float32)).astype(jnp.float16)
    lane = lax.broadcasted_iota(jnp.int32, extra.shape, 1)
    second = (lane >= heads_q) & (lane < 2 * heads_q)
    return jnp.concatenate(
        [part[:, :qcols].astype(jnp.float16), jnp.where(second, rest, rounded)], axis=1
    )


def cache_partials(scalars, gathered, keys, values, block, pieces, qcols):
    rows, gcols = gathered.shape
    cache_rows, kcols = keys.shape
    out_cols = qcols + 128
    heads_q = qcols // HEAD_DIM
    if pieces > 1:
        q_spec = pl.BlockSpec((rows, gcols), lambda i, s: (0, 0))
    else:
        q_spec = pl.BlockSpec((block, gcols), lambda i, s: (i, 0))
    return pl.pallas_call(
        functools.partial(cache_kernel, pieces),
        grid_spec=pltpu.PrefetchScalarGridSpec(
            num_scalar_prefetch=1,
            grid=(rows // block,),
            in_specs=[
                q_spec,
                pl.BlockSpec((cache_rows, kcols), lambda i, s: (0, 0)),
                pl.BlockSpec((cache_rows, kcols), lambda i, s: (0, 0)),
            ],
            out_specs=pl.BlockSpec((block, out_cols), lambda i, s: (i, 0)),
        ),
        out_shape=jax.ShapeDtypeStruct((rows, out_cols), jnp.float32),
        cost_estimate=pl.CostEstimate(
            flops=4 * rows * cache_rows * qcols,
            transcendentals=rows * cache_rows * heads_q,
            bytes_accessed=2 * (rows * gcols + 2 * cache_rows * kcols) + 4 * rows * out_cols,
        ),
    )(scalars, gathered, keys, values)


def on_device(
    new_queries, new_keys, new_values, cache_keys, cache_values, segment_ids, cache_length
):
    head_size = HEAD_DIM
    own_count = new_queries.shape[0]
    join_rows = segment_ids.shape[0]
    cache_rows = cache_keys.shape[0]
    heads_kv = cache_keys.shape[1] // head_size
    heads_q = new_queries.shape[1] // head_size
    group_size = heads_q // heads_kv
    qcols = heads_q * head_size
    kcols = heads_kv * head_size
    seq_count = lax.axis_size("seq")
    seq_rank = lax.axis_index("seq")
    score_scale = head_size ** (-0.5)

    packed = jnp.concatenate([new_queries, new_keys, new_values], axis=1)
    gathered = lax.all_gather(packed, "seq", axis=0, tiled=True)
    all_keys = gathered[:, qcols:qcols + kcols]
    all_values = gathered[:, qcols + kcols:]

    live_rows = jnp.clip(cache_length[0] - seq_rank * cache_rows, 0, cache_rows)
    live_rows = live_rows.astype(jnp.int32)

    if seq_count <= 8:
        scalars = jnp.stack(
            [live_rows]
            + [lax.rem(seq_rank + s, seq_count).astype(jnp.int32) for s in range(seq_count)]
        )
        partial = cache_partials(
            scalars, gathered, cache_keys, cache_values, join_rows, seq_count, qcols
        )
        parts = [to_half(partial[:own_count], qcols, heads_q)]
        for shift in range(1, seq_count):
            part = to_half(partial[shift * own_count:(shift + 1) * own_count], qcols, heads_q)
            parts.append(
                lax.ppermute(
                    part, "seq", [(i, (i + shift) % seq_count) for i in range(seq_count)]
                )
            )
    else:
        scalars = jnp.stack([live_rows, jnp.zeros((), jnp.int32)])
        partial = cache_partials(
            scalars, gathered, cache_keys, cache_values, min(join_rows, 256), 1, qcols
        )
        recv = lax.all_to_all(to_half(partial, qcols, heads_q), "seq", 0, 0, tiled=True)
        parts = [recv[j * own_count:(j + 1) * own_count] for j in range(seq_count)]
    parts = [p.astype(jnp.float32) for p in parts]
    part_mean = [p[:, :qcols].reshape(own_count, heads_q, head_size) for p in parts]
    part_denom = [
        p[:, qcols:qcols + heads_q] + p[:, qcols + heads_q:qcols + 2 * heads_q] for p in parts
    ]
    part_max = [p[:, qcols + 2 * heads_q:qcols + 3 * heads_q] for p in parts]

    own_queries = new_queries.reshape(own_count, heads_kv, group_size, head_size)
    fresh_scores = (
        jnp.einsum(
            "cgrd,tgd->cgrt",
            own_queries,
            all_keys.reshape(join_rows, heads_kv, head_size),
            preferred_element_type=jnp.float32,
        )
        * score_scale
    )
    start_row = seq_rank * own_count
    own_positions = start_row + jnp.arange(own_count, dtype=jnp.int32)
    own_segments = lax.dynamic_slice_in_dim(segment_ids, start_row, own_count, 0)
    key_positions = jnp.arange(join_rows, dtype=jnp.int32)
    allowed = (key_positions[None, :] <= own_positions[:, None]) & (
        segment_ids[None, :] == own_segments[:, None]
    )
    allowed = allowed[:, None, None, :]
    fresh_max = jnp.max(jnp.where(allowed, fresh_scores, NEG_FILL), axis=-1)
    fresh_weights = jnp.exp(
        jnp.where(allowed, fresh_scores - fresh_max[..., None], NEG_FILL)
    ).astype(jnp.bfloat16)
    fresh_numer = jnp.einsum(
        "cgrt,tgd->cgrd",
        fresh_weights,
        all_values.reshape(join_rows, heads_kv, head_size),
        preferred_element_type=jnp.float32,
    ).reshape(own_count, heads_q, head_size)
    fresh_denom = jnp.sum(fresh_weights.astype(jnp.float32), axis=-1).reshape(own_count, heads_q)
    fresh_max = fresh_max.reshape(own_count, heads_q)

    row_max = fresh_max
    for m in part_max:
        row_max = jnp.maximum(row_max, m)
    fresh_factor = jnp.exp(fresh_max - row_max)
    total_numer = fresh_numer * fresh_factor[..., None]
    total_denom = fresh_denom * fresh_factor
    for o_j, d_j, m_j in zip(part_mean, part_denom, part_max):
        w_j = jnp.exp(m_j - row_max) * d_j
        total_numer = total_numer + o_j * w_j[..., None]
        total_denom = total_denom + w_j
    attended = total_numer / total_denom[..., None]
    return attended.reshape(own_count, qcols).astype(jnp.bfloat16)


def solution(mesh):
    placed = (
        P(("group", "seq"), "head"),
        P(("group", "seq"), "head"),
        P(("group", "seq"), "head"),
        P(("group", "seq"), "head"),
        P(("group", "seq"), "head"),
        P("group"),
        P("group"),
    )
    return jax.shard_map(
        on_device,
        mesh=mesh,
        in_specs=placed,
        out_specs=P(("group", "seq"), "head"),
        check_vma=False,
    )
```

```python
import functools

import jax
import jax.numpy as jnp
from jax import lax
from jax.experimental import pallas as pl
from jax.experimental.pallas import tpu as pltpu
from jax.sharding import PartitionSpec as P

HEAD_DIM = 128
SUB = 256
NEG_FILL = -1e30


def cache_kernel(seq_count, first, pieces, stack, len_ref, q_ref, k_ref, v_ref, *rest):
    out_ref = rest[-1]
    rank = lax.axis_index("seq")
    cache_rows = k_ref.shape[0]
    live = jnp.clip(len_ref[0] - rank * cache_rows, 0, cache_rows)
    rows = out_ref.shape[0]
    heads_q = (out_ref.shape[1] - 128) // HEAD_DIM
    heads_kv = k_ref.shape[1] // HEAD_DIM
    group = heads_q // heads_kv
    tiles = cache_rows // SUB
    scale = HEAD_DIM ** (-0.5)
    lane = lax.broadcasted_iota(jnp.int32, (rows, 128), 1)
    extra = jnp.zeros((rows, 128), jnp.float32)

    def query_rows(h):
        cols = slice(h * HEAD_DIM, (h + 1) * HEAD_DIM)
        if pieces == 0:
            return q_ref[:, cols]
        piece = rows // pieces
        blocks = []
        for p in range(pieces):
            index = lax.rem(rank + first + p, seq_count)
            blocks.append(q_ref[pl.ds(pl.multiple_of(index * piece, piece), piece), cols])
        return jnp.concatenate(blocks, axis=0)

    if stack > 1:
        units = [list(range(g * group, (g + 1) * group)) for g in range(heads_kv)]
    else:
        units = [[h] for h in range(heads_q)]
    for heads in units:
        g = heads[0] // group
        qx = jnp.concatenate([query_rows(h) for h in heads], axis=0)
        span = qx.shape[0]
        col = lax.broadcasted_iota(jnp.int32, (span, SUB), 1)
        maxes, numers, denoms = [], [], []
        for b in range(tiles):
            kb = k_ref[b * SUB:(b + 1) * SUB, g * HEAD_DIM:(g + 1) * HEAD_DIM]
            s = lax.dot_general(
                qx, kb, (((1,), (1,)), ((), ())), preferred_element_type=jnp.float32
            ) * scale
            ok = (col + b * SUB) < live
            tm = jnp.max(jnp.where(ok, s, NEG_FILL), axis=1, keepdims=True)
            w = jnp.exp(jnp.where(ok, s - tm, NEG_FILL)).astype(jnp.bfloat16)
            vb = v_ref[b * SUB:(b + 1) * SUB, g * HEAD_DIM:(g + 1) * HEAD_DIM]
            numers.append(jnp.dot(w, vb, preferred_element_type=jnp.float32))
            denoms.append(jnp.sum(w.astype(jnp.float32), axis=1, keepdims=True))
            maxes.append(tm)
        m = maxes[0]
        for tm in maxes[1:]:
            m = jnp.maximum(m, tm)
        numer = jnp.zeros((span, HEAD_DIM), jnp.float32)
        denom = jnp.zeros((span, 1), jnp.float32)
        for tm, nb, db in zip(maxes, numers, denoms):
            f = jnp.exp(tm - m)
            numer = numer + nb * f
            denom = denom + db * f
        top = jnp.floor(jnp.maximum(m, -60000.0) * 0.25 + 0.5) * 4.0
        f = jnp.exp(m - top)
        numer = numer * f
        denom = denom * f
        mean = numer / jnp.where(denom > 0, denom, 1.0)
        for i, h in enumerate(heads):
            rs = slice(i * rows, (i + 1) * rows)
            out_ref[:, h * HEAD_DIM:(h + 1) * HEAD_DIM] = mean[rs]
            extra = jnp.where((lane == h) | (lane == heads_q + h), denom[rs], extra)
            extra = jnp.where(lane == 2 * heads_q + h, top[rs], extra)
    out_ref[:, heads_q * HEAD_DIM:] = extra


def to_half(part, qcols, heads_q):
    extra = part[:, qcols:]
    rounded = extra.astype(jnp.float16)
    rest = (extra - rounded.astype(jnp.float32)).astype(jnp.float16)
    lane = lax.broadcasted_iota(jnp.int32, extra.shape, 1)
    second = (lane >= heads_q) & (lane < 2 * heads_q)
    return jnp.concatenate(
        [part[:, :qcols].astype(jnp.float16), jnp.where(second, rest, rounded)], axis=1
    )


def cache_partials(cache_length, queries, keys, values, qcols, rows, block, first, pieces,
                   stack, seq_count, after=None):
    qrows, qcols_in = queries.shape
    cache_rows, kcols = keys.shape
    out_cols = qcols + 128
    heads_q = qcols // HEAD_DIM
    if pieces > 0 or block == qrows:
        q_spec = pl.BlockSpec((qrows, qcols_in), lambda i: (0, 0))
    else:
        q_spec = pl.BlockSpec((block, qcols_in), lambda i: (i, 0))
    in_specs = [
        pl.BlockSpec(memory_space=pltpu.SMEM),
        q_spec,
        pl.BlockSpec((cache_rows, kcols), lambda i: (0, 0)),
        pl.BlockSpec((cache_rows, kcols), lambda i: (0, 0)),
    ]
    operands = [cache_length, queries, keys, values]
    if after is not None:
        in_specs.append(pl.BlockSpec(memory_space=pl.ANY))
        operands.append(after)
    return pl.pallas_call(
        functools.partial(cache_kernel, seq_count, first, pieces, stack),
        grid=(rows // block,),
        in_specs=in_specs,
        out_specs=pl.BlockSpec((block, out_cols), lambda i: (i, 0)),
        out_shape=jax.ShapeDtypeStruct((rows, out_cols), jnp.float32),
        cost_estimate=pl.CostEstimate(
            flops=4 * rows * cache_rows * qcols,
            transcendentals=rows * cache_rows * heads_q,
            bytes_accessed=2 * (rows * qcols_in + 2 * cache_rows * kcols) + 4 * rows * out_cols,
        ),
    )(*operands)


def on_device(
    new_queries, new_keys, new_values, cache_keys, cache_values, segment_ids, cache_length
):
    head_size = HEAD_DIM
    own_count = new_queries.shape[0]
    join_rows = segment_ids.shape[0]
    cache_rows = cache_keys.shape[0]
    heads_kv = cache_keys.shape[1] // head_size
    heads_q = new_queries.shape[1] // head_size
    group_size = heads_q // heads_kv
    qcols = heads_q * head_size
    kcols = heads_kv * head_size
    seq_count = lax.axis_size("seq")
    seq_rank = lax.axis_index("seq")
    score_scale = head_size ** (-0.5)

    packed = jnp.concatenate([new_queries, new_keys, new_values], axis=1)
    gathered = lax.all_gather(packed, "seq", axis=0, tiled=True)
    all_keys = gathered[:, qcols:qcols + kcols]
    all_values = gathered[:, qcols + kcols:]

    if seq_count <= 8:
        remote = cache_partials(
            cache_length, gathered, cache_keys, cache_values, qcols,
            (seq_count - 1) * own_count, (seq_count - 1) * own_count, 1, seq_count - 1, 1,
            seq_count,
        )
        parts = []
        for shift in range(1, seq_count):
            piece = remote[(shift - 1) * own_count:shift * own_count]
            parts.append(
                lax.ppermute(
                    to_half(piece, qcols, heads_q),
                    "seq",
                    [(i, (i + shift) % seq_count) for i in range(seq_count)],
                ).astype(jnp.float32)
            )
        own = cache_partials(
            cache_length, new_queries, cache_keys, cache_values, qcols,
            own_count, own_count, 0, 0, group_size, seq_count, after=remote,
        )
        split_denom = [True] * (seq_count - 1) + [False]
        parts.append(own)
    else:
        partial = cache_partials(
            cache_length, gathered, cache_keys, cache_values, qcols,
            join_rows, min(join_rows, 256), 0, 0, 1, seq_count,
        )
        recv = lax.all_to_all(to_half(partial, qcols, heads_q), "seq", 0, 0, tiled=True)
        recv = recv.astype(jnp.float32)
        parts = [recv[j * own_count:(j + 1) * own_count] for j in range(seq_count)]
        split_denom = [True] * seq_count
    part_mean = [p[:, :qcols].reshape(own_count, heads_q, head_size) for p in parts]
    part_denom = [
        p[:, qcols:qcols + heads_q] + p[:, qcols + heads_q:qcols + 2 * heads_q]
        if two else p[:, qcols:qcols + heads_q]
        for p, two in zip(parts, split_denom)
    ]
    part_max = [p[:, qcols + 2 * heads_q:qcols + 3 * heads_q] for p in parts]

    own_queries = new_queries.reshape(own_count, heads_kv, group_size, head_size)
    fresh_scores = (
        jnp.einsum(
            "cgrd,tgd->cgrt",
            own_queries,
            all_keys.reshape(join_rows, heads_kv, head_size),
            preferred_element_type=jnp.float32,
        )
        * score_scale
    )
    start_row = seq_rank * own_count
    own_positions = start_row + jnp.arange(own_count, dtype=jnp.int32)
    own_segments = lax.dynamic_slice_in_dim(segment_ids, start_row, own_count, 0)
    key_positions = jnp.arange(join_rows, dtype=jnp.int32)
    allowed = (key_positions[None, :] <= own_positions[:, None]) & (
        segment_ids[None, :] == own_segments[:, None]
    )
    allowed = allowed[:, None, None, :]
    fresh_max = jnp.max(jnp.where(allowed, fresh_scores, NEG_FILL), axis=-1)
    fresh_weights = jnp.exp(
        jnp.where(allowed, fresh_scores - fresh_max[..., None], NEG_FILL)
    ).astype(jnp.bfloat16)
    fresh_numer = jnp.einsum(
        "cgrt,tgd->cgrd",
        fresh_weights,
        all_values.reshape(join_rows, heads_kv, head_size),
        preferred_element_type=jnp.float32,
    ).reshape(own_count, heads_q, head_size)
    fresh_denom = jnp.sum(fresh_weights.astype(jnp.float32), axis=-1).reshape(own_count, heads_q)
    fresh_max = fresh_max.reshape(own_count, heads_q)

    row_max = fresh_max
    for m in part_max:
        row_max = jnp.maximum(row_max, m)
    fresh_factor = jnp.exp(fresh_max - row_max)
    total_numer = fresh_numer * fresh_factor[..., None]
    total_denom = fresh_denom * fresh_factor
    for o_j, d_j, m_j in zip(part_mean, part_denom, part_max):
        w_j = jnp.exp(m_j - row_max) * d_j
        total_numer = total_numer + o_j * w_j[..., None]
        total_denom = total_denom + w_j
    attended = total_numer / total_denom[..., None]
    return attended.reshape(own_count, qcols).astype(jnp.bfloat16)


def solution(mesh):
    placed = (
        P(("group", "seq"), "head"),
        P(("group", "seq"), "head"),
        P(("group", "seq"), "head"),
        P(("group", "seq"), "head"),
        P(("group", "seq"), "head"),
        P("group"),
        P("group"),
    )
    return jax.shard_map(
        on_device,
        mesh=mesh,
        in_specs=placed,
        out_specs=P(("group", "seq"), "head"),
        check_vma=False,
    )
```

```python
import functools

import jax
import jax.numpy as jnp
from jax import lax
from jax.experimental import pallas as pl
from jax.experimental.pallas import tpu as pltpu
from jax.sharding import PartitionSpec as P

HEAD_DIM = 128
SUB = 256
NEG_FILL = -1e30


def cache_kernel(seq_count, first, pieces, stack, len_ref, q_ref, k_ref, v_ref, *rest):
    out_ref = rest[-1]
    rank = lax.axis_index("seq")
    cache_rows = k_ref.shape[0]
    live = jnp.clip(len_ref[0] - rank * cache_rows, 0, cache_rows)
    rows = out_ref.shape[0]
    heads_q = (out_ref.shape[1] - 128) // HEAD_DIM
    heads_kv = k_ref.shape[1] // HEAD_DIM
    group = heads_q // heads_kv
    tiles = cache_rows // SUB
    scale = HEAD_DIM ** (-0.5)
    lane = lax.broadcasted_iota(jnp.int32, (rows, 128), 1)
    position = lax.broadcasted_iota(jnp.int32, (1, cache_rows), 1)
    ones = jnp.ones((SUB, 128), jnp.bfloat16)
    extra = jnp.zeros((rows, 128), jnp.float32)

    def query_rows(h):
        cols = slice(h * HEAD_DIM, (h + 1) * HEAD_DIM)
        if pieces == 0:
            return q_ref[:, cols]
        piece = rows // pieces
        blocks = []
        for p in range(pieces):
            index = lax.rem(rank + first + p, seq_count)
            blocks.append(q_ref[pl.ds(pl.multiple_of(index * piece, piece), piece), cols])
        return jnp.concatenate(blocks, axis=0)

    if stack > 1:
        units = [list(range(g * group, (g + 1) * group)) for g in range(heads_kv)]
    else:
        units = [[h] for h in range(heads_q)]
    for heads in units:
        g = heads[0] // group
        qx = jnp.concatenate([query_rows(h) for h in heads], axis=0)
        span = qx.shape[0]
        maxes, numers, denoms = [], [], []
        for b in range(tiles):
            kb = k_ref[b * SUB:(b + 1) * SUB, g * HEAD_DIM:(g + 1) * HEAD_DIM]
            bias = jnp.where(position[:, b * SUB:(b + 1) * SUB] < live, 0.0, NEG_FILL)
            s = lax.dot_general(
                qx, kb, (((1,), (1,)), ((), ())), preferred_element_type=jnp.float32
            ) * scale + bias
            tm = jnp.max(s, axis=1, keepdims=True)
            w = jnp.exp(s - tm).astype(jnp.bfloat16)
            vb = v_ref[b * SUB:(b + 1) * SUB, g * HEAD_DIM:(g + 1) * HEAD_DIM]
            numers.append(jnp.dot(w, vb, preferred_element_type=jnp.float32))
            denoms.append(jnp.dot(w, ones, preferred_element_type=jnp.float32)[:, :1])
            maxes.append(tm)
        m = maxes[0]
        for tm in maxes[1:]:
            m = jnp.maximum(m, tm)
        numer = jnp.zeros((span, HEAD_DIM), jnp.float32)
        denom = jnp.zeros((span, 1), jnp.float32)
        for tm, nb, db in zip(maxes, numers, denoms):
            f = jnp.exp(tm - m)
            numer = numer + nb * f
            denom = denom + db * f
        top = jnp.floor(jnp.maximum(m, -60000.0) * 0.25 + 0.5) * 4.0
        f = jnp.exp(m - top)
        numer = numer * f
        denom = denom * f
        mean = numer / jnp.where(denom > 0, denom, 1.0)
        ulp = jnp.exp2(jnp.floor(jnp.log2(jnp.where(denom > 0, denom, 1.0))) - 10.0)
        hi = jnp.where(denom > 0, jnp.round(denom / ulp) * ulp, 0.0)
        for i, h in enumerate(heads):
            rs = slice(i * rows, (i + 1) * rows)
            out_ref[:, h * HEAD_DIM:(h + 1) * HEAD_DIM] = mean[rs]
            extra = jnp.where(lane == h, hi[rs], extra)
            extra = jnp.where(lane == heads_q + h, denom[rs] - hi[rs], extra)
            extra = jnp.where(lane == 2 * heads_q + h, top[rs], extra)
    out_ref[:, heads_q * HEAD_DIM:] = extra


def to_half(part, qcols, heads_q):
    return part.astype(jnp.float16)


def cache_partials(cache_length, queries, keys, values, qcols, rows, block, first, pieces,
                   stack, seq_count, after=None):
    qrows, qcols_in = queries.shape
    cache_rows, kcols = keys.shape
    out_cols = qcols + 128
    heads_q = qcols // HEAD_DIM
    if pieces > 0 or block == qrows:
        q_spec = pl.BlockSpec((qrows, qcols_in), lambda i: (0, 0))
    else:
        q_spec = pl.BlockSpec((block, qcols_in), lambda i: (i, 0))
    in_specs = [
        pl.BlockSpec(memory_space=pltpu.SMEM),
        q_spec,
        pl.BlockSpec((cache_rows, kcols), lambda i: (0, 0)),
        pl.BlockSpec((cache_rows, kcols), lambda i: (0, 0)),
    ]
    operands = [cache_length, queries, keys, values]
    if after is not None:
        in_specs.append(pl.BlockSpec(memory_space=pl.ANY))
        operands.append(after)
    return pl.pallas_call(
        functools.partial(cache_kernel, seq_count, first, pieces, stack),
        grid=(rows // block,),
        in_specs=in_specs,
        out_specs=pl.BlockSpec((block, out_cols), lambda i: (i, 0)),
        out_shape=jax.ShapeDtypeStruct((rows, out_cols), jnp.float32),
        cost_estimate=pl.CostEstimate(
            flops=4 * rows * cache_rows * qcols,
            transcendentals=rows * cache_rows * heads_q,
            bytes_accessed=2 * (rows * qcols_in + 2 * cache_rows * kcols) + 4 * rows * out_cols,
        ),
    )(*operands)


def on_device(
    new_queries, new_keys, new_values, cache_keys, cache_values, segment_ids, cache_length
):
    head_size = HEAD_DIM
    own_count = new_queries.shape[0]
    join_rows = segment_ids.shape[0]
    cache_rows = cache_keys.shape[0]
    heads_kv = cache_keys.shape[1] // head_size
    heads_q = new_queries.shape[1] // head_size
    group_size = heads_q // heads_kv
    qcols = heads_q * head_size
    kcols = heads_kv * head_size
    seq_count = lax.axis_size("seq")
    seq_rank = lax.axis_index("seq")
    score_scale = head_size ** (-0.5)

    packed = jnp.concatenate([new_queries, new_keys, new_values], axis=1)
    gathered = lax.all_gather(packed, "seq", axis=0, tiled=True)
    all_keys = gathered[:, qcols:qcols + kcols]
    all_values = gathered[:, qcols + kcols:]

    if seq_count <= 8:
        remote = cache_partials(
            cache_length, gathered, cache_keys, cache_values, qcols,
            (seq_count - 1) * own_count, (seq_count - 1) * own_count, 1, seq_count - 1, 1,
            seq_count,
        )
        parts = []
        for shift in range(1, seq_count):
            piece = remote[(shift - 1) * own_count:shift * own_count]
            parts.append(
                lax.ppermute(
                    to_half(piece, qcols, heads_q),
                    "seq",
                    [(i, (i + shift) % seq_count) for i in range(seq_count)],
                ).astype(jnp.float32)
            )
        own = cache_partials(
            cache_length, new_queries, cache_keys, cache_values, qcols,
            own_count, own_count, 0, 0, group_size, seq_count, after=remote,
        )
        parts.append(own)
    else:
        partial = cache_partials(
            cache_length, gathered, cache_keys, cache_values, qcols,
            join_rows, min(join_rows, 256), 0, 0, 1, seq_count,
        )
        recv = lax.all_to_all(to_half(partial, qcols, heads_q), "seq", 0, 0, tiled=True)
        recv = recv.astype(jnp.float32)
        parts = [recv[j * own_count:(j + 1) * own_count] for j in range(seq_count)]
    part_mean = [p[:, :qcols].reshape(own_count, heads_q, head_size) for p in parts]
    part_denom = [
        p[:, qcols:qcols + heads_q] + p[:, qcols + heads_q:qcols + 2 * heads_q] for p in parts
    ]
    part_max = [p[:, qcols + 2 * heads_q:qcols + 3 * heads_q] for p in parts]

    own_queries = new_queries.reshape(own_count, heads_kv, group_size, head_size)
    fresh_scores = (
        jnp.einsum(
            "cgrd,tgd->cgrt",
            own_queries,
            all_keys.reshape(join_rows, heads_kv, head_size),
            preferred_element_type=jnp.float32,
        )
        * score_scale
    )
    start_row = seq_rank * own_count
    own_positions = start_row + jnp.arange(own_count, dtype=jnp.int32)
    own_segments = lax.dynamic_slice_in_dim(segment_ids, start_row, own_count, 0)
    key_positions = jnp.arange(join_rows, dtype=jnp.int32)
    allowed = (key_positions[None, :] <= own_positions[:, None]) & (
        segment_ids[None, :] == own_segments[:, None]
    )
    allowed = allowed[:, None, None, :]
    fresh_max = jnp.max(jnp.where(allowed, fresh_scores, NEG_FILL), axis=-1)
    fresh_weights = jnp.exp(
        jnp.where(allowed, fresh_scores - fresh_max[..., None], NEG_FILL)
    ).astype(jnp.bfloat16)
    fresh_numer = jnp.einsum(
        "cgrt,tgd->cgrd",
        fresh_weights,
        all_values.reshape(join_rows, heads_kv, head_size),
        preferred_element_type=jnp.float32,
    ).reshape(own_count, heads_q, head_size)
    fresh_denom = jnp.sum(fresh_weights.astype(jnp.float32), axis=-1).reshape(own_count, heads_q)
    fresh_max = fresh_max.reshape(own_count, heads_q)

    row_max = fresh_max
    for m in part_max:
        row_max = jnp.maximum(row_max, m)
    fresh_factor = jnp.exp(fresh_max - row_max)
    total_numer = fresh_numer * fresh_factor[..., None]
    total_denom = fresh_denom * fresh_factor
    for o_j, d_j, m_j in zip(part_mean, part_denom, part_max):
        w_j = jnp.exp(m_j - row_max) * d_j
        total_numer = total_numer + o_j * w_j[..., None]
        total_denom = total_denom + w_j
    attended = total_numer / total_denom[..., None]
    return attended.reshape(own_count, qcols).astype(jnp.bfloat16)


def solution(mesh):
    placed = (
        P(("group", "seq"), "head"),
        P(("group", "seq"), "head"),
        P(("group", "seq"), "head"),
        P(("group", "seq"), "head"),
        P(("group", "seq"), "head"),
        P("group"),
        P("group"),
    )
    return jax.shard_map(
        on_device,
        mesh=mesh,
        in_specs=placed,
        out_specs=P(("group", "seq"), "head"),
        check_vma=False,
    )
```

```python
import functools

import jax
import jax.numpy as jnp
from jax import lax
from jax.experimental import pallas as pl
from jax.experimental.pallas import tpu as pltpu
from jax.sharding import PartitionSpec as P

HEAD_DIM = 128
SUB = 256
NEG_FILL = -1e30


def cache_kernel(seq_count, first, pieces, stack, len_ref, q_ref, k_ref, v_ref, *rest):
    out_ref = rest[-1]
    rank = lax.axis_index("seq")
    cache_rows = k_ref.shape[0]
    live = jnp.clip(len_ref[0] - rank * cache_rows, 0, cache_rows)
    rows = out_ref.shape[0]
    heads_q = (out_ref.shape[1] - 128) // HEAD_DIM
    heads_kv = k_ref.shape[1] // HEAD_DIM
    group = heads_q // heads_kv
    tiles = cache_rows // SUB
    scale = HEAD_DIM ** (-0.5)
    lane = lax.broadcasted_iota(jnp.int32, (rows, 128), 1)
    position = lax.broadcasted_iota(jnp.int32, (1, cache_rows), 1)
    extra = jnp.zeros((rows, 128), jnp.float32)

    def query_rows(h):
        cols = slice(h * HEAD_DIM, (h + 1) * HEAD_DIM)
        if pieces == 0:
            return q_ref[:, cols]
        piece = rows // pieces
        blocks = []
        for p in range(pieces):
            index = lax.rem(rank + first + p, seq_count)
            blocks.append(q_ref[pl.ds(pl.multiple_of(index * piece, piece), piece), cols])
        return jnp.concatenate(blocks, axis=0)

    if stack > 1:
        units = [list(range(g * group, (g + 1) * group)) for g in range(heads_kv)]
    else:
        units = [[h] for h in range(heads_q)]
    for heads in units:
        g = heads[0] // group
        qx = jnp.concatenate([query_rows(h) for h in heads], axis=0)
        span = qx.shape[0]
        maxes, numers, denoms = [], [], []
        for b in range(tiles):
            kb = k_ref[b * SUB:(b + 1) * SUB, g * HEAD_DIM:(g + 1) * HEAD_DIM]
            bias = jnp.where(position[:, b * SUB:(b + 1) * SUB] < live, 0.0, NEG_FILL)
            s = lax.dot_general(
                qx, kb, (((1,), (1,)), ((), ())), preferred_element_type=jnp.float32
            ) * scale + bias
            tm = jnp.max(s, axis=1, keepdims=True)
            w = jnp.exp(s - tm).astype(jnp.bfloat16)
            vb = v_ref[b * SUB:(b + 1) * SUB, g * HEAD_DIM:(g + 1) * HEAD_DIM]
            numers.append(jnp.dot(w, vb, preferred_element_type=jnp.float32))
            denoms.append(jnp.sum(w.astype(jnp.float32), axis=1, keepdims=True))
            maxes.append(tm)
        m = maxes[0]
        for tm in maxes[1:]:
            m = jnp.maximum(m, tm)
        numer = jnp.zeros((span, HEAD_DIM), jnp.float32)
        denom = jnp.zeros((span, 1), jnp.float32)
        for tm, nb, db in zip(maxes, numers, denoms):
            f = jnp.exp(tm - m)
            numer = numer + nb * f
            denom = denom + db * f
        top = jnp.floor(jnp.maximum(m, -60000.0) * 0.25 + 0.5) * 4.0
        f = jnp.exp(m - top)
        numer = numer * f
        denom = denom * f
        mean = numer / jnp.where(denom > 0, denom, 1.0)
        ulp = jnp.exp2(jnp.floor(jnp.log2(jnp.where(denom > 0, denom, 1.0))) - 10.0)
        hi = jnp.where(denom > 0, jnp.round(denom / ulp) * ulp, 0.0)
        for i, h in enumerate(heads):
            rs = slice(i * rows, (i + 1) * rows)
            out_ref[:, h * HEAD_DIM:(h + 1) * HEAD_DIM] = mean[rs]
            extra = jnp.where(lane == h, hi[rs], extra)
            extra = jnp.where(lane == heads_q + h, denom[rs] - hi[rs], extra)
            extra = jnp.where(lane == 2 * heads_q + h, top[rs], extra)
    out_ref[:, heads_q * HEAD_DIM:] = extra


def to_half(part, qcols, heads_q):
    return part.astype(jnp.float16)


def cache_partials(cache_length, queries, keys, values, qcols, rows, block, first, pieces,
                   stack, seq_count, after=None):
    qrows, qcols_in = queries.shape
    cache_rows, kcols = keys.shape
    out_cols = qcols + 128
    heads_q = qcols // HEAD_DIM
    if pieces > 0 or block == qrows:
        q_spec = pl.BlockSpec((qrows, qcols_in), lambda i: (0, 0))
    else:
        q_spec = pl.BlockSpec((block, qcols_in), lambda i: (i, 0))
    in_specs = [
        pl.BlockSpec(memory_space=pltpu.SMEM),
        q_spec,
        pl.BlockSpec((cache_rows, kcols), lambda i: (0, 0)),
        pl.BlockSpec((cache_rows, kcols), lambda i: (0, 0)),
    ]
    operands = [cache_length, queries, keys, values]
    if after is not None:
        in_specs.append(pl.BlockSpec(memory_space=pl.ANY))
        operands.append(after)
    return pl.pallas_call(
        functools.partial(cache_kernel, seq_count, first, pieces, stack),
        grid=(rows // block,),
        in_specs=in_specs,
        out_specs=pl.BlockSpec((block, out_cols), lambda i: (i, 0)),
        out_shape=jax.ShapeDtypeStruct((rows, out_cols), jnp.float32),
        cost_estimate=pl.CostEstimate(
            flops=4 * rows * cache_rows * qcols,
            transcendentals=rows * cache_rows * heads_q,
            bytes_accessed=2 * (rows * qcols_in + 2 * cache_rows * kcols) + 4 * rows * out_cols,
        ),
    )(*operands)


def on_device(
    new_queries, new_keys, new_values, cache_keys, cache_values, segment_ids, cache_length
):
    head_size = HEAD_DIM
    own_count = new_queries.shape[0]
    join_rows = segment_ids.shape[0]
    cache_rows = cache_keys.shape[0]
    heads_kv = cache_keys.shape[1] // head_size
    heads_q = new_queries.shape[1] // head_size
    group_size = heads_q // heads_kv
    qcols = heads_q * head_size
    kcols = heads_kv * head_size
    seq_count = lax.axis_size("seq")
    seq_rank = lax.axis_index("seq")
    score_scale = head_size ** (-0.5)

    packed = jnp.concatenate([new_queries, new_keys, new_values], axis=1)
    gathered = lax.all_gather(packed, "seq", axis=0, tiled=True)
    all_keys = gathered[:, qcols:qcols + kcols]
    all_values = gathered[:, qcols + kcols:]

    if seq_count <= 8:
        remote = cache_partials(
            cache_length, gathered, cache_keys, cache_values, qcols,
            (seq_count - 1) * own_count, (seq_count - 1) * own_count, 1, seq_count - 1, 1,
            seq_count,
        )
        parts = []
        for shift in range(1, seq_count):
            piece = remote[(shift - 1) * own_count:shift * own_count]
            parts.append(
                lax.ppermute(
                    to_half(piece, qcols, heads_q),
                    "seq",
                    [(i, (i + shift) % seq_count) for i in range(seq_count)],
                ).astype(jnp.float32)
            )
        own = cache_partials(
            cache_length, new_queries, cache_keys, cache_values, qcols,
            own_count, own_count, 0, 0, group_size, seq_count, after=remote,
        )
        parts.append(own)
    else:
        partial = cache_partials(
            cache_length, gathered, cache_keys, cache_values, qcols,
            join_rows, min(join_rows, 256), 0, 0, 1, seq_count,
        )
        recv = lax.all_to_all(to_half(partial, qcols, heads_q), "seq", 0, 0, tiled=True)
        recv = recv.astype(jnp.float32)
        parts = [recv[j * own_count:(j + 1) * own_count] for j in range(seq_count)]
    part_mean = [p[:, :qcols].reshape(own_count, heads_q, head_size) for p in parts]
    part_denom = [
        p[:, qcols:qcols + heads_q] + p[:, qcols + heads_q:qcols + 2 * heads_q] for p in parts
    ]
    part_max = [p[:, qcols + 2 * heads_q:qcols + 3 * heads_q] for p in parts]

    own_queries = new_queries.reshape(own_count, heads_kv, group_size, head_size)
    fresh_scores = (
        jnp.einsum(
            "cgrd,tgd->cgrt",
            own_queries,
            all_keys.reshape(join_rows, heads_kv, head_size),
            preferred_element_type=jnp.float32,
        )
        * score_scale
    )
    start_row = seq_rank * own_count
    own_positions = start_row + jnp.arange(own_count, dtype=jnp.int32)
    own_segments = lax.dynamic_slice_in_dim(segment_ids, start_row, own_count, 0)
    key_positions = jnp.arange(join_rows, dtype=jnp.int32)
    allowed = (key_positions[None, :] <= own_positions[:, None]) & (
        segment_ids[None, :] == own_segments[:, None]
    )
    allowed = allowed[:, None, None, :]
    fresh_max = jnp.max(jnp.where(allowed, fresh_scores, NEG_FILL), axis=-1)
    fresh_weights = jnp.exp(
        jnp.where(allowed, fresh_scores - fresh_max[..., None], NEG_FILL)
    ).astype(jnp.bfloat16)
    fresh_numer = jnp.einsum(
        "cgrt,tgd->cgrd",
        fresh_weights,
        all_values.reshape(join_rows, heads_kv, head_size),
        preferred_element_type=jnp.float32,
    ).reshape(own_count, heads_q, head_size)
    fresh_denom = jnp.sum(fresh_weights.astype(jnp.float32), axis=-1).reshape(own_count, heads_q)
    fresh_max = fresh_max.reshape(own_count, heads_q)

    row_max = fresh_max
    for m in part_max:
        row_max = jnp.maximum(row_max, m)
    fresh_factor = jnp.exp(fresh_max - row_max)
    total_numer = fresh_numer * fresh_factor[..., None]
    total_denom = fresh_denom * fresh_factor
    for o_j, d_j, m_j in zip(part_mean, part_denom, part_max):
        w_j = jnp.exp(m_j - row_max) * d_j
        total_numer = total_numer + o_j * w_j[..., None]
        total_denom = total_denom + w_j
    attended = total_numer / total_denom[..., None]
    return attended.reshape(own_count, qcols).astype(jnp.bfloat16)


def solution(mesh):
    placed = (
        P(("group", "seq"), "head"),
        P(("group", "seq"), "head"),
        P(("group", "seq"), "head"),
        P(("group", "seq"), "head"),
        P(("group", "seq"), "head"),
        P("group"),
        P("group"),
    )
    return jax.shard_map(
        on_device,
        mesh=mesh,
        in_specs=placed,
        out_specs=P(("group", "seq"), "head"),
        check_vma=False,
    )
```

```python
import functools

import jax
import jax.numpy as jnp
from jax import lax
from jax.experimental import pallas as pl
from jax.experimental.pallas import tpu as pltpu
from jax.sharding import PartitionSpec as P

HEAD_DIM = 128
SUB = 256
NEG_FILL = -1e30


def cache_kernel(seq_count, first, pieces, stack, len_ref, q_ref, k_ref, v_ref, *rest):
    out_ref = rest[-1]
    rank = lax.axis_index("seq")
    cache_rows = k_ref.shape[0]
    live = jnp.clip(len_ref[0] - rank * cache_rows, 0, cache_rows)
    rows = out_ref.shape[0]
    heads_q = (out_ref.shape[1] - 128) // HEAD_DIM
    heads_kv = k_ref.shape[1] // HEAD_DIM
    group = heads_q // heads_kv
    tiles = cache_rows // SUB
    scale = HEAD_DIM ** (-0.5)
    lane = lax.broadcasted_iota(jnp.int32, (rows, 128), 1)
    position = lax.broadcasted_iota(jnp.int32, (1, cache_rows), 1)
    extra = jnp.zeros((rows, 128), jnp.float32)

    def query_rows(h):
        cols = slice(h * HEAD_DIM, (h + 1) * HEAD_DIM)
        if pieces == 0:
            return q_ref[:, cols]
        piece = rows // pieces
        blocks = []
        for p in range(pieces):
            index = lax.rem(rank + first + p, seq_count)
            blocks.append(q_ref[pl.ds(pl.multiple_of(index * piece, piece), piece), cols])
        return jnp.concatenate(blocks, axis=0)

    keys_t = [k_ref[:, g * HEAD_DIM:(g + 1) * HEAD_DIM].T for g in range(heads_kv)]
    if stack > 1:
        units = [list(range(g * group, (g + 1) * group)) for g in range(heads_kv)]
    else:
        units = [[h] for h in range(heads_q)]
    for heads in units:
        g = heads[0] // group
        qx = jnp.concatenate([query_rows(h) for h in heads], axis=0)
        span = qx.shape[0]
        maxes, numers, denoms = [], [], []
        for b in range(tiles):
            kb = keys_t[g][:, b * SUB:(b + 1) * SUB]
            bias = jnp.where(position[:, b * SUB:(b + 1) * SUB] < live, 0.0, NEG_FILL)
            s = jnp.dot(qx, kb, preferred_element_type=jnp.float32) * scale + bias
            tm = jnp.max(s, axis=1, keepdims=True)
            w = jnp.exp(s - tm).astype(jnp.bfloat16)
            vb = v_ref[b * SUB:(b + 1) * SUB, g * HEAD_DIM:(g + 1) * HEAD_DIM]
            numers.append(jnp.dot(w, vb, preferred_element_type=jnp.float32))
            denoms.append(jnp.sum(w.astype(jnp.float32), axis=1, keepdims=True))
            maxes.append(tm)
        m = maxes[0]
        for tm in maxes[1:]:
            m = jnp.maximum(m, tm)
        numer = jnp.zeros((span, HEAD_DIM), jnp.float32)
        denom = jnp.zeros((span, 1), jnp.float32)
        for tm, nb, db in zip(maxes, numers, denoms):
            f = jnp.exp(tm - m)
            numer = numer + nb * f
            denom = denom + db * f
        top = jnp.floor(jnp.maximum(m, -60000.0) * 0.25 + 0.5) * 4.0
        f = jnp.exp(m - top)
        numer = numer * f
        denom = denom * f
        mean = numer / jnp.where(denom > 0, denom, 1.0)
        ulp = jnp.exp2(jnp.floor(jnp.log2(jnp.where(denom > 0, denom, 1.0))) - 10.0)
        hi = jnp.where(denom > 0, jnp.round(denom / ulp) * ulp, 0.0)
        for i, h in enumerate(heads):
            rs = slice(i * rows, (i + 1) * rows)
            out_ref[:, h * HEAD_DIM:(h + 1) * HEAD_DIM] = mean[rs]
            extra = jnp.where(lane == h, hi[rs], extra)
            extra = jnp.where(lane == heads_q + h, denom[rs] - hi[rs], extra)
            extra = jnp.where(lane == 2 * heads_q + h, top[rs], extra)
    out_ref[:, heads_q * HEAD_DIM:] = extra


def to_half(part, qcols, heads_q):
    return part.astype(jnp.float16)


def cache_partials(cache_length, queries, keys, values, qcols, rows, block, first, pieces,
                   stack, seq_count, after=None):
    qrows, qcols_in = queries.shape
    cache_rows, kcols = keys.shape
    out_cols = qcols + 128
    heads_q = qcols // HEAD_DIM
    if pieces > 0 or block == qrows:
        q_spec = pl.BlockSpec((qrows, qcols_in), lambda i: (0, 0))
    else:
        q_spec = pl.BlockSpec((block, qcols_in), lambda i: (i, 0))
    in_specs = [
        pl.BlockSpec(memory_space=pltpu.SMEM),
        q_spec,
        pl.BlockSpec((cache_rows, kcols), lambda i: (0, 0)),
        pl.BlockSpec((cache_rows, kcols), lambda i: (0, 0)),
    ]
    operands = [cache_length, queries, keys, values]
    if after is not None:
        in_specs.append(pl.BlockSpec(memory_space=pl.ANY))
        operands.append(after)
    return pl.pallas_call(
        functools.partial(cache_kernel, seq_count, first, pieces, stack),
        grid=(rows // block,),
        in_specs=in_specs,
        out_specs=pl.BlockSpec((block, out_cols), lambda i: (i, 0)),
        out_shape=jax.ShapeDtypeStruct((rows, out_cols), jnp.float32),
        cost_estimate=pl.CostEstimate(
            flops=4 * rows * cache_rows * qcols,
            transcendentals=rows * cache_rows * heads_q,
            bytes_accessed=2 * (rows * qcols_in + 2 * cache_rows * kcols) + 4 * rows * out_cols,
        ),
    )(*operands)


def on_device(
    new_queries, new_keys, new_values, cache_keys, cache_values, segment_ids, cache_length
):
    head_size = HEAD_DIM
    own_count = new_queries.shape[0]
    join_rows = segment_ids.shape[0]
    cache_rows = cache_keys.shape[0]
    heads_kv = cache_keys.shape[1] // head_size
    heads_q = new_queries.shape[1] // head_size
    group_size = heads_q // heads_kv
    qcols = heads_q * head_size
    kcols = heads_kv * head_size
    seq_count = lax.axis_size("seq")
    seq_rank = lax.axis_index("seq")
    score_scale = head_size ** (-0.5)

    packed = jnp.concatenate([new_queries, new_keys, new_values], axis=1)
    gathered = lax.all_gather(packed, "seq", axis=0, tiled=True)
    all_keys = gathered[:, qcols:qcols + kcols]
    all_values = gathered[:, qcols + kcols:]

    if seq_count <= 8:
        remote = cache_partials(
            cache_length, gathered, cache_keys, cache_values, qcols,
            (seq_count - 1) * own_count, (seq_count - 1) * own_count, 1, seq_count - 1, 1,
            seq_count,
        )
        parts = []
        for shift in range(1, seq_count):
            piece = remote[(shift - 1) * own_count:shift * own_count]
            parts.append(
                lax.ppermute(
                    to_half(piece, qcols, heads_q),
                    "seq",
                    [(i, (i + shift) % seq_count) for i in range(seq_count)],
                ).astype(jnp.float32)
            )
        own = cache_partials(
            cache_length, new_queries, cache_keys, cache_values, qcols,
            own_count, own_count, 0, 0, group_size, seq_count, after=remote,
        )
        parts.append(own)
    else:
        partial = cache_partials(
            cache_length, gathered, cache_keys, cache_values, qcols,
            join_rows, min(join_rows, 256), 0, 0, 1, seq_count,
        )
        recv = lax.all_to_all(to_half(partial, qcols, heads_q), "seq", 0, 0, tiled=True)
        recv = recv.astype(jnp.float32)
        parts = [recv[j * own_count:(j + 1) * own_count] for j in range(seq_count)]
    part_mean = [p[:, :qcols].reshape(own_count, heads_q, head_size) for p in parts]
    part_denom = [
        p[:, qcols:qcols + heads_q] + p[:, qcols + heads_q:qcols + 2 * heads_q] for p in parts
    ]
    part_max = [p[:, qcols + 2 * heads_q:qcols + 3 * heads_q] for p in parts]

    own_queries = new_queries.reshape(own_count, heads_kv, group_size, head_size)
    fresh_scores = (
        jnp.einsum(
            "cgrd,tgd->cgrt",
            own_queries,
            all_keys.reshape(join_rows, heads_kv, head_size),
            preferred_element_type=jnp.float32,
        )
        * score_scale
    )
    start_row = seq_rank * own_count
    own_positions = start_row + jnp.arange(own_count, dtype=jnp.int32)
    own_segments = lax.dynamic_slice_in_dim(segment_ids, start_row, own_count, 0)
    key_positions = jnp.arange(join_rows, dtype=jnp.int32)
    allowed = (key_positions[None, :] <= own_positions[:, None]) & (
        segment_ids[None, :] == own_segments[:, None]
    )
    allowed = allowed[:, None, None, :]
    fresh_max = jnp.max(jnp.where(allowed, fresh_scores, NEG_FILL), axis=-1)
    fresh_weights = jnp.exp(
        jnp.where(allowed, fresh_scores - fresh_max[..., None], NEG_FILL)
    ).astype(jnp.bfloat16)
    fresh_numer = jnp.einsum(
        "cgrt,tgd->cgrd",
        fresh_weights,
        all_values.reshape(join_rows, heads_kv, head_size),
        preferred_element_type=jnp.float32,
    ).reshape(own_count, heads_q, head_size)
    fresh_denom = jnp.sum(fresh_weights.astype(jnp.float32), axis=-1).reshape(own_count, heads_q)
    fresh_max = fresh_max.reshape(own_count, heads_q)

    row_max = fresh_max
    for m in part_max:
        row_max = jnp.maximum(row_max, m)
    fresh_factor = jnp.exp(fresh_max - row_max)
    total_numer = fresh_numer * fresh_factor[..., None]
    total_denom = fresh_denom * fresh_factor
    for o_j, d_j, m_j in zip(part_mean, part_denom, part_max):
        w_j = jnp.exp(m_j - row_max) * d_j
        total_numer = total_numer + o_j * w_j[..., None]
        total_denom = total_denom + w_j
    attended = total_numer / total_denom[..., None]
    return attended.reshape(own_count, qcols).astype(jnp.bfloat16)


def solution(mesh):
    placed = (
        P(("group", "seq"), "head"),
        P(("group", "seq"), "head"),
        P(("group", "seq"), "head"),
        P(("group", "seq"), "head"),
        P(("group", "seq"), "head"),
        P("group"),
        P("group"),
    )
    return jax.shard_map(
        on_device,
        mesh=mesh,
        in_specs=placed,
        out_specs=P(("group", "seq"), "head"),
        check_vma=False,
    )
```

```python
import functools

import jax
import jax.numpy as jnp
from jax import lax
from jax.experimental import pallas as pl
from jax.experimental.pallas import tpu as pltpu
from jax.sharding import PartitionSpec as P

HEAD_DIM = 128
SUB = 256
NEG_FILL = -1e30


def cache_kernel(seq_count, first, pieces, stack, len_ref, q_ref, k_ref, v_ref, *rest):
    out_ref = rest[-1]
    rank = lax.axis_index("seq")
    cache_rows = k_ref.shape[0]
    live = jnp.clip(len_ref[0] - rank * cache_rows, 0, cache_rows)
    rows = out_ref.shape[0]
    heads_q = (out_ref.shape[1] - 128) // HEAD_DIM
    heads_kv = k_ref.shape[1] // HEAD_DIM
    group = heads_q // heads_kv
    tiles = cache_rows // SUB
    scale = HEAD_DIM ** (-0.5)
    lane = lax.broadcasted_iota(jnp.int32, (rows, 128), 1)
    position = lax.broadcasted_iota(jnp.int32, (1, cache_rows), 1)
    extra = jnp.zeros((rows, 128), jnp.float32)

    def query_rows(h):
        cols = slice(h * HEAD_DIM, (h + 1) * HEAD_DIM)
        if pieces == 0:
            return q_ref[:, cols]
        piece = rows // pieces
        blocks = []
        for p in range(pieces):
            index = lax.rem(rank + first + p, seq_count)
            blocks.append(q_ref[pl.ds(pl.multiple_of(index * piece, piece), piece), cols])
        return jnp.concatenate(blocks, axis=0)

    keys_t = [k_ref[:, g * HEAD_DIM:(g + 1) * HEAD_DIM].T for g in range(heads_kv)]
    if stack > 1:
        units = [list(range(g * group, (g + 1) * group)) for g in range(heads_kv)]
    else:
        units = [[h] for h in range(heads_q)]
    for heads in units:
        g = heads[0] // group
        qx = jnp.concatenate([query_rows(h) for h in heads], axis=0)
        span = qx.shape[0]
        maxes, numers, denoms = [], [], []
        for b in range(tiles):
            kb = keys_t[g][:, b * SUB:(b + 1) * SUB]
            bias = jnp.where(position[:, b * SUB:(b + 1) * SUB] < live, 0.0, NEG_FILL)
            s = jnp.dot(qx, kb, preferred_element_type=jnp.float32) * scale + bias
            tm = jnp.max(s, axis=1, keepdims=True)
            w = jnp.exp(s - tm).astype(jnp.bfloat16)
            vb = v_ref[b * SUB:(b + 1) * SUB, g * HEAD_DIM:(g + 1) * HEAD_DIM]
            numers.append(jnp.dot(w, vb, preferred_element_type=jnp.float32))
            denoms.append(jnp.sum(w.astype(jnp.float32), axis=1, keepdims=True))
            maxes.append(tm)
        m = maxes[0]
        for tm in maxes[1:]:
            m = jnp.maximum(m, tm)
        numer = jnp.zeros((span, HEAD_DIM), jnp.float32)
        denom = jnp.zeros((span, 1), jnp.float32)
        for tm, nb, db in zip(maxes, numers, denoms):
            f = jnp.exp(tm - m)
            numer = numer + nb * f
            denom = denom + db * f
        top = jnp.floor(jnp.maximum(m, -60000.0) * 0.25 + 0.5) * 4.0
        f = jnp.exp(m - top)
        numer = numer * f
        denom = denom * f
        mean = numer / jnp.where(denom > 0, denom, 1.0)
        ulp = jnp.exp2(jnp.floor(jnp.log2(jnp.where(denom > 0, denom, 1.0))) - 10.0)
        hi = jnp.where(denom > 0, jnp.round(denom / ulp) * ulp, 0.0)
        for i, h in enumerate(heads):
            rs = slice(i * rows, (i + 1) * rows)
            out_ref[:, h * HEAD_DIM:(h + 1) * HEAD_DIM] = mean[rs]
            extra = jnp.where(lane == h, hi[rs], extra)
            extra = jnp.where(lane == heads_q + h, denom[rs] - hi[rs], extra)
            extra = jnp.where(lane == 2 * heads_q + h, top[rs], extra)
    out_ref[:, heads_q * HEAD_DIM:] = extra


def to_half(part, qcols, heads_q):
    return part.astype(jnp.float16)


def cache_partials(cache_length, queries, keys, values, qcols, rows, block, first, pieces,
                   stack, seq_count, after=None):
    qrows, qcols_in = queries.shape
    cache_rows, kcols = keys.shape
    out_cols = qcols + 128
    heads_q = qcols // HEAD_DIM
    if pieces > 0 or block == qrows:
        q_spec = pl.BlockSpec((qrows, qcols_in), lambda i: (0, 0))
    else:
        q_spec = pl.BlockSpec((block, qcols_in), lambda i: (i, 0))
    in_specs = [
        pl.BlockSpec(memory_space=pltpu.SMEM),
        q_spec,
        pl.BlockSpec((cache_rows, kcols), lambda i: (0, 0)),
        pl.BlockSpec((cache_rows, kcols), lambda i: (0, 0)),
    ]
    operands = [cache_length, queries, keys, values]
    if after is not None:
        in_specs.append(pl.BlockSpec(memory_space=pl.ANY))
        operands.append(after)
    return pl.pallas_call(
        functools.partial(cache_kernel, seq_count, first, pieces, stack),
        grid=(rows // block,),
        in_specs=in_specs,
        out_specs=pl.BlockSpec((block, out_cols), lambda i: (i, 0)),
        out_shape=jax.ShapeDtypeStruct((rows, out_cols), jnp.float32),
        cost_estimate=pl.CostEstimate(
            flops=4 * rows * cache_rows * qcols,
            transcendentals=rows * cache_rows * heads_q,
            bytes_accessed=2 * (rows * qcols_in + 2 * cache_rows * kcols) + 4 * rows * out_cols,
        ),
    )(*operands)


def on_device(
    new_queries, new_keys, new_values, cache_keys, cache_values, segment_ids, cache_length
):
    head_size = HEAD_DIM
    own_count = new_queries.shape[0]
    join_rows = segment_ids.shape[0]
    cache_rows = cache_keys.shape[0]
    heads_kv = cache_keys.shape[1] // head_size
    heads_q = new_queries.shape[1] // head_size
    group_size = heads_q // heads_kv
    qcols = heads_q * head_size
    kcols = heads_kv * head_size
    seq_count = lax.axis_size("seq")
    seq_rank = lax.axis_index("seq")
    score_scale = head_size ** (-0.5)

    packed = jnp.concatenate([new_queries, new_keys, new_values], axis=1)
    gathered = lax.all_gather(packed, "seq", axis=0, tiled=True)
    all_keys = gathered[:, qcols:qcols + kcols]
    all_values = gathered[:, qcols + kcols:]

    if seq_count <= 8:
        remote = cache_partials(
            cache_length, gathered, cache_keys, cache_values, qcols,
            (seq_count - 1) * own_count, (seq_count - 1) * own_count, 1, seq_count - 1, 1,
            seq_count,
        )
        parts = []
        for shift in range(1, seq_count):
            piece = remote[(shift - 1) * own_count:shift * own_count]
            parts.append(
                lax.ppermute(
                    to_half(piece, qcols, heads_q),
                    "seq",
                    [(i, (i + shift) % seq_count) for i in range(seq_count)],
                ).astype(jnp.float32)
            )
        own = cache_partials(
            cache_length, new_queries, cache_keys, cache_values, qcols,
            own_count, own_count, 0, 0, group_size, seq_count, after=remote,
        )
        parts.append(own)
    else:
        partial = cache_partials(
            cache_length, gathered, cache_keys, cache_values, qcols,
            join_rows, min(join_rows, 256), 0, 0, 1, seq_count,
        )
        recv = lax.all_to_all(to_half(partial, qcols, heads_q), "seq", 0, 0, tiled=True)
        recv = recv.astype(jnp.float32)
        parts = [recv[j * own_count:(j + 1) * own_count] for j in range(seq_count)]
    part_mean = [p[:, :qcols] for p in parts]
    part_denom = [
        p[:, qcols:qcols + heads_q] + p[:, qcols + heads_q:qcols + 2 * heads_q] for p in parts
    ]
    part_max = [p[:, qcols + 2 * heads_q:qcols + 3 * heads_q] for p in parts]

    own_queries = new_queries.reshape(own_count, heads_kv, group_size, head_size)
    fresh_scores = (
        jnp.einsum(
            "cgrd,tgd->cgrt",
            own_queries,
            all_keys.reshape(join_rows, heads_kv, head_size),
            preferred_element_type=jnp.float32,
        )
        * score_scale
    )
    start_row = seq_rank * own_count
    own_positions = start_row + jnp.arange(own_count, dtype=jnp.int32)
    own_segments = lax.dynamic_slice_in_dim(segment_ids, start_row, own_count, 0)
    key_positions = jnp.arange(join_rows, dtype=jnp.int32)
    allowed = (key_positions[None, :] <= own_positions[:, None]) & (
        segment_ids[None, :] == own_segments[:, None]
    )
    allowed = allowed[:, None, None, :]
    fresh_max = jnp.max(jnp.where(allowed, fresh_scores, NEG_FILL), axis=-1)
    fresh_weights = jnp.exp(
        jnp.where(allowed, fresh_scores - fresh_max[..., None], NEG_FILL)
    ).astype(jnp.bfloat16)
    fresh_numer = jnp.einsum(
        "cgrt,tgd->cgrd",
        fresh_weights,
        all_values.reshape(join_rows, heads_kv, head_size),
        preferred_element_type=jnp.float32,
    ).reshape(own_count, qcols)
    fresh_denom = jnp.sum(fresh_weights.astype(jnp.float32), axis=-1).reshape(own_count, heads_q)
    fresh_max = fresh_max.reshape(own_count, heads_q)


    def spread(x):
        return jnp.broadcast_to(x[:, :, None], (own_count, heads_q, head_size)).reshape(
            own_count, qcols
        )

    own_mean, own_denom, own_max = part_mean[-1], part_denom[-1], part_max[-1]
    local_max = jnp.maximum(fresh_max, own_max)
    fresh_factor = jnp.exp(fresh_max - local_max)
    own_weight = jnp.exp(own_max - local_max) * own_denom
    local_numer = fresh_numer * spread(fresh_factor) + own_mean * spread(own_weight)
    local_denom = fresh_denom * fresh_factor + own_weight

    row_max = local_max
    for m in part_max[:-1]:
        row_max = jnp.maximum(row_max, m)
    local_factor = jnp.exp(local_max - row_max)
    total_numer = local_numer * spread(local_factor)
    total_denom = local_denom * local_factor
    for o_j, d_j, m_j in zip(part_mean[:-1], part_denom[:-1], part_max[:-1]):
        w_j = jnp.exp(m_j - row_max) * d_j
        total_numer = total_numer + o_j * spread(w_j)
        total_denom = total_denom + w_j
    attended = total_numer / spread(total_denom)
    return attended.astype(jnp.bfloat16)


def solution(mesh):
    placed = (
        P(("group", "seq"), "head"),
        P(("group", "seq"), "head"),
        P(("group", "seq"), "head"),
        P(("group", "seq"), "head"),
        P(("group", "seq"), "head"),
        P("group"),
        P("group"),
    )
    return jax.shard_map(
        on_device,
        mesh=mesh,
        in_specs=placed,
        out_specs=P(("group", "seq"), "head"),
        check_vma=False,
    )
```

```python
import functools

import jax
import jax.numpy as jnp
from jax import lax
from jax.experimental import pallas as pl
from jax.experimental.pallas import tpu as pltpu
from jax.sharding import PartitionSpec as P

HEAD_DIM = 128
SUB = 256
NEG_FILL = -1e30


def cache_kernel(seq_count, first, pieces, stack, len_ref, q_ref, k_ref, v_ref, *rest):
    out_ref = rest[-1]
    rank = lax.axis_index("seq")
    cache_rows = k_ref.shape[0]
    live = jnp.clip(len_ref[0] - rank * cache_rows, 0, cache_rows)
    rows = out_ref.shape[0]
    heads_q = (out_ref.shape[1] - 128) // HEAD_DIM
    heads_kv = k_ref.shape[1] // HEAD_DIM
    group = heads_q // heads_kv
    tiles = cache_rows // SUB
    scale = HEAD_DIM ** (-0.5)
    lane = lax.broadcasted_iota(jnp.int32, (rows, 128), 1)
    position = lax.broadcasted_iota(jnp.int32, (1, cache_rows), 1)
    extra = jnp.zeros((rows, 128), jnp.float32)

    def query_rows(h):
        cols = slice(h * HEAD_DIM, (h + 1) * HEAD_DIM)
        if pieces == 0:
            return q_ref[:, cols]
        piece = rows // pieces
        blocks = []
        for p in range(pieces):
            index = lax.rem(rank + first + p, seq_count)
            blocks.append(q_ref[pl.ds(pl.multiple_of(index * piece, piece), piece), cols])
        return jnp.concatenate(blocks, axis=0)

    keys_t = [k_ref[:, g * HEAD_DIM:(g + 1) * HEAD_DIM].T for g in range(heads_kv)]
    if stack > 1:
        units = [list(range(g * group, (g + 1) * group)) for g in range(heads_kv)]
    else:
        units = [[h] for h in range(heads_q)]
    for heads in units:
        g = heads[0] // group
        qx = jnp.concatenate([query_rows(h) for h in heads], axis=0)
        span = qx.shape[0]
        maxes, numers, denoms = [], [], []
        for b in range(tiles):
            kb = keys_t[g][:, b * SUB:(b + 1) * SUB]
            bias = jnp.where(position[:, b * SUB:(b + 1) * SUB] < live, 0.0, NEG_FILL)
            s = jnp.dot(qx, kb, preferred_element_type=jnp.float32) * scale + bias
            tm = jnp.max(s, axis=1, keepdims=True)
            w = jnp.exp(s - tm).astype(jnp.bfloat16)
            vb = v_ref[b * SUB:(b + 1) * SUB, g * HEAD_DIM:(g + 1) * HEAD_DIM]
            numers.append(jnp.dot(w, vb, preferred_element_type=jnp.float32))
            denoms.append(jnp.sum(w.astype(jnp.float32), axis=1, keepdims=True))
            maxes.append(tm)
        m = maxes[0]
        for tm in maxes[1:]:
            m = jnp.maximum(m, tm)
        numer = jnp.zeros((span, HEAD_DIM), jnp.float32)
        denom = jnp.zeros((span, 1), jnp.float32)
        for tm, nb, db in zip(maxes, numers, denoms):
            f = jnp.exp(tm - m)
            numer = numer + nb * f
            denom = denom + db * f
        top = jnp.floor(jnp.maximum(m, -60000.0) * 0.25 + 0.5) * 4.0
        f = jnp.exp(m - top)
        numer = numer * f
        denom = denom * f
        mean = numer / jnp.where(denom > 0, denom, 1.0)
        ulp = jnp.exp2(jnp.floor(jnp.log2(jnp.where(denom > 0, denom, 1.0))) - 10.0)
        hi = jnp.where(denom > 0, jnp.round(denom / ulp) * ulp, 0.0)
        for i, h in enumerate(heads):
            rs = slice(i * rows, (i + 1) * rows)
            out_ref[:, h * HEAD_DIM:(h + 1) * HEAD_DIM] = mean[rs]
            extra = jnp.where(lane == h, hi[rs], extra)
            extra = jnp.where(lane == heads_q + h, denom[rs] - hi[rs], extra)
            extra = jnp.where(lane == 2 * heads_q + h, top[rs], extra)
    out_ref[:, heads_q * HEAD_DIM:] = extra


def to_half(part, qcols, heads_q):
    return part.astype(jnp.float16)


def cache_partials(cache_length, queries, keys, values, qcols, rows, block, first, pieces,
                   stack, seq_count, after=None):
    qrows, qcols_in = queries.shape
    cache_rows, kcols = keys.shape
    out_cols = qcols + 128
    heads_q = qcols // HEAD_DIM
    if pieces > 0 or block == qrows:
        q_spec = pl.BlockSpec((qrows, qcols_in), lambda i: (0, 0))
    else:
        q_spec = pl.BlockSpec((block, qcols_in), lambda i: (i, 0))
    in_specs = [
        pl.BlockSpec(memory_space=pltpu.SMEM),
        q_spec,
        pl.BlockSpec((cache_rows, kcols), lambda i: (0, 0)),
        pl.BlockSpec((cache_rows, kcols), lambda i: (0, 0)),
    ]
    operands = [cache_length, queries, keys, values]
    if after is not None:
        in_specs.append(pl.BlockSpec(memory_space=pl.ANY))
        operands.append(after)
    return pl.pallas_call(
        functools.partial(cache_kernel, seq_count, first, pieces, stack),
        grid=(rows // block,),
        in_specs=in_specs,
        out_specs=pl.BlockSpec((block, out_cols), lambda i: (i, 0)),
        out_shape=jax.ShapeDtypeStruct((rows, out_cols), jnp.float32),
        cost_estimate=pl.CostEstimate(
            flops=4 * rows * cache_rows * qcols,
            transcendentals=rows * cache_rows * heads_q,
            bytes_accessed=2 * (rows * qcols_in + 2 * cache_rows * kcols) + 4 * rows * out_cols,
        ),
    )(*operands)


def combine_kernel(heads_q, fnum_ref, fmax_ref, fden_ref, *refs):
    out_ref = refs[-1]
    part_refs = refs[:-1]
    qcols = heads_q * HEAD_DIM
    for h in range(heads_q):
        cols = slice(h * HEAD_DIM, (h + 1) * HEAD_DIM)
        tops = [fmax_ref[:, h:h + 1]]
        sums = [fden_ref[:, h:h + 1]]
        for p in part_refs:
            tops.append(p[:, qcols + 2 * heads_q + h:qcols + 2 * heads_q + h + 1])
            sums.append(p[:, qcols + h:qcols + h + 1] + p[:, qcols + heads_q + h:qcols + heads_q + h + 1])
        top = tops[0]
        for t in tops[1:]:
            top = jnp.maximum(top, t)
        weights = [jnp.exp(t - top) * s for t, s in zip(tops, sums)]
        numer = fnum_ref[:, cols] * jnp.exp(tops[0] - top)
        for p, w in zip(part_refs, weights[1:]):
            numer = numer + p[:, cols] * w
        denom = weights[0]
        for w in weights[1:]:
            denom = denom + w
        out_ref[:, cols] = (numer / denom).astype(out_ref.dtype)


def on_device(
    new_queries, new_keys, new_values, cache_keys, cache_values, segment_ids, cache_length
):
    head_size = HEAD_DIM
    own_count = new_queries.shape[0]
    join_rows = segment_ids.shape[0]
    cache_rows = cache_keys.shape[0]
    heads_kv = cache_keys.shape[1] // head_size
    heads_q = new_queries.shape[1] // head_size
    group_size = heads_q // heads_kv
    qcols = heads_q * head_size
    kcols = heads_kv * head_size
    seq_count = lax.axis_size("seq")
    seq_rank = lax.axis_index("seq")
    score_scale = head_size ** (-0.5)

    packed = jnp.concatenate([new_queries, new_keys, new_values], axis=1)
    gathered = lax.all_gather(packed, "seq", axis=0, tiled=True)
    all_keys = gathered[:, qcols:qcols + kcols]
    all_values = gathered[:, qcols + kcols:]

    if seq_count <= 8:
        remote = cache_partials(
            cache_length, gathered, cache_keys, cache_values, qcols,
            (seq_count - 1) * own_count, (seq_count - 1) * own_count, 1, seq_count - 1, 1,
            seq_count,
        )
        parts = []
        for shift in range(1, seq_count):
            piece = remote[(shift - 1) * own_count:shift * own_count]
            parts.append(
                lax.ppermute(
                    to_half(piece, qcols, heads_q),
                    "seq",
                    [(i, (i + shift) % seq_count) for i in range(seq_count)],
                ).astype(jnp.float32)
            )
        own = cache_partials(
            cache_length, new_queries, cache_keys, cache_values, qcols,
            own_count, own_count, 0, 0, group_size, seq_count, after=remote,
        )
        parts.append(own)
    else:
        partial = cache_partials(
            cache_length, gathered, cache_keys, cache_values, qcols,
            join_rows, min(join_rows, 256), 0, 0, 1, seq_count,
        )
        recv = lax.all_to_all(to_half(partial, qcols, heads_q), "seq", 0, 0, tiled=True)
        recv = recv.astype(jnp.float32)
        parts = [recv[j * own_count:(j + 1) * own_count] for j in range(seq_count)]
    own_queries = new_queries.reshape(own_count, heads_kv, group_size, head_size)
    fresh_scores = (
        jnp.einsum(
            "cgrd,tgd->cgrt",
            own_queries,
            all_keys.reshape(join_rows, heads_kv, head_size),
            preferred_element_type=jnp.float32,
        )
        * score_scale
    )
    start_row = seq_rank * own_count
    own_positions = start_row + jnp.arange(own_count, dtype=jnp.int32)
    own_segments = lax.dynamic_slice_in_dim(segment_ids, start_row, own_count, 0)
    key_positions = jnp.arange(join_rows, dtype=jnp.int32)
    allowed = (key_positions[None, :] <= own_positions[:, None]) & (
        segment_ids[None, :] == own_segments[:, None]
    )
    allowed = allowed[:, None, None, :]
    fresh_max = jnp.max(jnp.where(allowed, fresh_scores, NEG_FILL), axis=-1)
    fresh_weights = jnp.exp(
        jnp.where(allowed, fresh_scores - fresh_max[..., None], NEG_FILL)
    ).astype(jnp.bfloat16)
    fresh_numer = jnp.einsum(
        "cgrt,tgd->cgrd",
        fresh_weights,
        all_values.reshape(join_rows, heads_kv, head_size),
        preferred_element_type=jnp.float32,
    ).reshape(own_count, qcols)
    fresh_denom = jnp.sum(fresh_weights.astype(jnp.float32), axis=-1).reshape(own_count, heads_q)
    fresh_max = fresh_max.reshape(own_count, heads_q)


    return pl.pallas_call(
        functools.partial(combine_kernel, heads_q),
        out_shape=jax.ShapeDtypeStruct((own_count, qcols), jnp.bfloat16),
    )(fresh_numer, fresh_max, fresh_denom, *parts)


def solution(mesh):
    placed = (
        P(("group", "seq"), "head"),
        P(("group", "seq"), "head"),
        P(("group", "seq"), "head"),
        P(("group", "seq"), "head"),
        P(("group", "seq"), "head"),
        P("group"),
        P("group"),
    )
    return jax.shard_map(
        on_device,
        mesh=mesh,
        in_specs=placed,
        out_specs=P(("group", "seq"), "head"),
        check_vma=False,
    )
```

```python
import functools

import jax
import jax.numpy as jnp
from jax import lax
from jax.experimental import pallas as pl
from jax.experimental.pallas import tpu as pltpu
from jax.sharding import PartitionSpec as P

HEAD_DIM = 128
SUB = 256
NEG_FILL = -1e30


def cache_kernel(seq_count, first, pieces, stack, len_ref, q_ref, k_ref, v_ref, *rest):
    out_ref = rest[-1]
    rank = lax.axis_index("seq")
    cache_rows = k_ref.shape[0]
    live = jnp.clip(len_ref[0] - rank * cache_rows, 0, cache_rows)
    rows = out_ref.shape[0]
    heads_q = (out_ref.shape[1] - 128) // HEAD_DIM
    heads_kv = k_ref.shape[1] // HEAD_DIM
    group = heads_q // heads_kv
    tiles = cache_rows // SUB
    scale = HEAD_DIM ** (-0.5)
    lane = lax.broadcasted_iota(jnp.int32, (rows, 128), 1)
    position = lax.broadcasted_iota(jnp.int32, (1, cache_rows), 1)
    extra = jnp.zeros((rows, 128), jnp.float32)

    def query_rows(h):
        cols = slice(h * HEAD_DIM, (h + 1) * HEAD_DIM)
        if pieces == 0:
            return q_ref[:, cols]
        piece = rows // pieces
        blocks = []
        for p in range(pieces):
            index = lax.rem(rank + first + p, seq_count)
            blocks.append(q_ref[pl.ds(pl.multiple_of(index * piece, piece), piece), cols])
        return jnp.concatenate(blocks, axis=0)

    keys_t = [k_ref[:, g * HEAD_DIM:(g + 1) * HEAD_DIM].T for g in range(heads_kv)]
    if stack > 1:
        units = [list(range(g * group, (g + 1) * group)) for g in range(heads_kv)]
    else:
        units = [[h] for h in range(heads_q)]
    for heads in units:
        g = heads[0] // group
        qx = jnp.concatenate([query_rows(h) for h in heads], axis=0)
        span = qx.shape[0]
        maxes, numers, denoms = [], [], []
        for b in range(tiles):
            kb = keys_t[g][:, b * SUB:(b + 1) * SUB]
            bias = jnp.where(position[:, b * SUB:(b + 1) * SUB] < live, 0.0, NEG_FILL)
            s = jnp.dot(qx, kb, preferred_element_type=jnp.float32) * scale + bias
            tm = jnp.max(s, axis=1, keepdims=True)
            w = jnp.exp(s - tm).astype(jnp.bfloat16)
            vb = v_ref[b * SUB:(b + 1) * SUB, g * HEAD_DIM:(g + 1) * HEAD_DIM]
            numers.append(jnp.dot(w, vb, preferred_element_type=jnp.float32))
            denoms.append(jnp.sum(w.astype(jnp.float32), axis=1, keepdims=True))
            maxes.append(tm)
        m = maxes[0]
        for tm in maxes[1:]:
            m = jnp.maximum(m, tm)
        top = jnp.floor(jnp.maximum(m, -60000.0) * 0.25 + 0.5) * 4.0
        numer = jnp.zeros((span, HEAD_DIM), jnp.float32)
        denom = jnp.zeros((span, 1), jnp.float32)
        for tm, nb, db in zip(maxes, numers, denoms):
            f = jnp.exp(tm - top)
            numer = numer + nb * f
            denom = denom + db * f
        mean = numer / jnp.where(denom > 0, denom, 1.0)
        ulp = jnp.exp2(jnp.floor(jnp.log2(jnp.where(denom > 0, denom, 1.0))) - 10.0)
        hi = jnp.where(denom > 0, jnp.round(denom / ulp) * ulp, 0.0)
        for i, h in enumerate(heads):
            rs = slice(i * rows, (i + 1) * rows)
            out_ref[:, h * HEAD_DIM:(h + 1) * HEAD_DIM] = mean[rs]
            extra = jnp.where(lane == h, hi[rs], extra)
            extra = jnp.where(lane == heads_q + h, denom[rs] - hi[rs], extra)
            extra = jnp.where(lane == 2 * heads_q + h, top[rs], extra)
    out_ref[:, heads_q * HEAD_DIM:] = extra


def to_half(part, qcols, heads_q):
    return part.astype(jnp.float16)


def cache_partials(cache_length, queries, keys, values, qcols, rows, block, first, pieces,
                   stack, seq_count, after=None):
    qrows, qcols_in = queries.shape
    cache_rows, kcols = keys.shape
    out_cols = qcols + 128
    heads_q = qcols // HEAD_DIM
    if pieces > 0 or block == qrows:
        q_spec = pl.BlockSpec((qrows, qcols_in), lambda i: (0, 0))
    else:
        q_spec = pl.BlockSpec((block, qcols_in), lambda i: (i, 0))
    in_specs = [
        pl.BlockSpec(memory_space=pltpu.SMEM),
        q_spec,
        pl.BlockSpec((cache_rows, kcols), lambda i: (0, 0)),
        pl.BlockSpec((cache_rows, kcols), lambda i: (0, 0)),
    ]
    operands = [cache_length, queries, keys, values]
    if after is not None:
        in_specs.append(pl.BlockSpec(memory_space=pl.ANY))
        operands.append(after)
    return pl.pallas_call(
        functools.partial(cache_kernel, seq_count, first, pieces, stack),
        grid=(rows // block,),
        in_specs=in_specs,
        out_specs=pl.BlockSpec((block, out_cols), lambda i: (i, 0)),
        out_shape=jax.ShapeDtypeStruct((rows, out_cols), jnp.float32),
        cost_estimate=pl.CostEstimate(
            flops=4 * rows * cache_rows * qcols,
            transcendentals=rows * cache_rows * heads_q,
            bytes_accessed=2 * (rows * qcols_in + 2 * cache_rows * kcols) + 4 * rows * out_cols,
        ),
    )(*operands)


def on_device(
    new_queries, new_keys, new_values, cache_keys, cache_values, segment_ids, cache_length
):
    head_size = HEAD_DIM
    own_count = new_queries.shape[0]
    join_rows = segment_ids.shape[0]
    cache_rows = cache_keys.shape[0]
    heads_kv = cache_keys.shape[1] // head_size
    heads_q = new_queries.shape[1] // head_size
    group_size = heads_q // heads_kv
    qcols = heads_q * head_size
    kcols = heads_kv * head_size
    seq_count = lax.axis_size("seq")
    seq_rank = lax.axis_index("seq")
    score_scale = head_size ** (-0.5)

    packed = jnp.concatenate([new_queries, new_keys, new_values], axis=1)
    gathered = lax.all_gather(packed, "seq", axis=0, tiled=True)
    all_keys = gathered[:, qcols:qcols + kcols]
    all_values = gathered[:, qcols + kcols:]

    if seq_count <= 8:
        remote = cache_partials(
            cache_length, gathered, cache_keys, cache_values, qcols,
            (seq_count - 1) * own_count, (seq_count - 1) * own_count, 1, seq_count - 1, 1,
            seq_count,
        )
        parts = []
        for shift in range(1, seq_count):
            piece = remote[(shift - 1) * own_count:shift * own_count]
            parts.append(
                lax.ppermute(
                    to_half(piece, qcols, heads_q),
                    "seq",
                    [(i, (i + shift) % seq_count) for i in range(seq_count)],
                ).astype(jnp.float32)
            )
        own = cache_partials(
            cache_length, new_queries, cache_keys, cache_values, qcols,
            own_count, own_count, 0, 0, group_size, seq_count, after=remote,
        )
        parts.append(own)
    else:
        partial = cache_partials(
            cache_length, gathered, cache_keys, cache_values, qcols,
            join_rows, min(join_rows, 256), 0, 0, 1, seq_count,
        )
        recv = lax.all_to_all(to_half(partial, qcols, heads_q), "seq", 0, 0, tiled=True)
        recv = recv.astype(jnp.float32)
        parts = [recv[j * own_count:(j + 1) * own_count] for j in range(seq_count)]
    part_mean = [p[:, :qcols] for p in parts]
    part_denom = [
        p[:, qcols:qcols + heads_q] + p[:, qcols + heads_q:qcols + 2 * heads_q] for p in parts
    ]
    part_max = [p[:, qcols + 2 * heads_q:qcols + 3 * heads_q] for p in parts]

    own_queries = new_queries.reshape(own_count, heads_kv, group_size, head_size)
    fresh_scores = (
        jnp.einsum(
            "cgrd,tgd->cgrt",
            own_queries,
            all_keys.reshape(join_rows, heads_kv, head_size),
            preferred_element_type=jnp.float32,
        )
        * score_scale
    )
    start_row = seq_rank * own_count
    own_positions = start_row + jnp.arange(own_count, dtype=jnp.int32)
    own_segments = lax.dynamic_slice_in_dim(segment_ids, start_row, own_count, 0)
    key_positions = jnp.arange(join_rows, dtype=jnp.int32)
    allowed = (key_positions[None, :] <= own_positions[:, None]) & (
        segment_ids[None, :] == own_segments[:, None]
    )
    allowed = allowed[:, None, None, :]
    fresh_max = jnp.max(jnp.where(allowed, fresh_scores, NEG_FILL), axis=-1)
    fresh_weights = jnp.exp(
        jnp.where(allowed, fresh_scores - fresh_max[..., None], NEG_FILL)
    ).astype(jnp.bfloat16)
    fresh_numer = jnp.einsum(
        "cgrt,tgd->cgrd",
        fresh_weights,
        all_values.reshape(join_rows, heads_kv, head_size),
        preferred_element_type=jnp.float32,
    ).reshape(own_count, qcols)
    fresh_denom = jnp.sum(fresh_weights.astype(jnp.float32), axis=-1).reshape(own_count, heads_q)
    fresh_max = fresh_max.reshape(own_count, heads_q)


    def spread(x):
        return jnp.broadcast_to(x[:, :, None], (own_count, heads_q, head_size)).reshape(
            own_count, qcols
        )

    own_mean, own_denom, own_max = part_mean[-1], part_denom[-1], part_max[-1]
    local_max = jnp.maximum(fresh_max, own_max)
    fresh_factor = jnp.exp(fresh_max - local_max)
    own_weight = jnp.exp(own_max - local_max) * own_denom
    local_numer = fresh_numer * spread(fresh_factor) + own_mean * spread(own_weight)
    local_denom = fresh_denom * fresh_factor + own_weight

    row_max = local_max
    for m in part_max[:-1]:
        row_max = jnp.maximum(row_max, m)
    local_factor = jnp.exp(local_max - row_max)
    total_numer = local_numer * spread(local_factor)
    total_denom = local_denom * local_factor
    for o_j, d_j, m_j in zip(part_mean[:-1], part_denom[:-1], part_max[:-1]):
        w_j = jnp.exp(m_j - row_max) * d_j
        total_numer = total_numer + o_j * spread(w_j)
        total_denom = total_denom + w_j
    attended = total_numer / spread(total_denom)
    return attended.astype(jnp.bfloat16)


def solution(mesh):
    placed = (
        P(("group", "seq"), "head"),
        P(("group", "seq"), "head"),
        P(("group", "seq"), "head"),
        P(("group", "seq"), "head"),
        P(("group", "seq"), "head"),
        P("group"),
        P("group"),
    )
    return jax.shard_map(
        on_device,
        mesh=mesh,
        in_specs=placed,
        out_specs=P(("group", "seq"), "head"),
        check_vma=False,
    )
```

```python
import functools

import jax
import jax.numpy as jnp
from jax import lax
from jax.experimental import pallas as pl
from jax.experimental.pallas import tpu as pltpu
from jax.sharding import PartitionSpec as P

HEAD_DIM = 128
SUB = 256
NEG_FILL = -1e30
LOG2E = 1.4426950408889634
LN2 = 0.6931471805599453


def cache_kernel(seq_count, first, pieces, stack, len_ref, q_ref, k_ref, v_ref, *rest):
    out_ref = rest[-1]
    rank = lax.axis_index("seq")
    cache_rows = k_ref.shape[0]
    live = jnp.clip(len_ref[0] - rank * cache_rows, 0, cache_rows)
    rows = out_ref.shape[0]
    heads_q = (out_ref.shape[1] - 128) // HEAD_DIM
    heads_kv = k_ref.shape[1] // HEAD_DIM
    group = heads_q // heads_kv
    tiles = cache_rows // SUB
    scale2 = HEAD_DIM ** (-0.5) * LOG2E
    lane = lax.broadcasted_iota(jnp.int32, (rows, 128), 1)
    position = lax.broadcasted_iota(jnp.int32, (1, cache_rows), 1)
    extra = jnp.zeros((rows, 128), jnp.float32)

    def query_rows(h):
        cols = slice(h * HEAD_DIM, (h + 1) * HEAD_DIM)
        if pieces == 0:
            return q_ref[:, cols]
        piece = rows // pieces
        blocks = []
        for p in range(pieces):
            index = lax.rem(rank + first + p, seq_count)
            blocks.append(q_ref[pl.ds(pl.multiple_of(index * piece, piece), piece), cols])
        return jnp.concatenate(blocks, axis=0)

    keys_t = [k_ref[:, g * HEAD_DIM:(g + 1) * HEAD_DIM].T for g in range(heads_kv)]
    if stack > 1:
        units = [list(range(g * group, (g + 1) * group)) for g in range(heads_kv)]
    else:
        units = [[h] for h in range(heads_q)]
    for heads in units:
        g = heads[0] // group
        qx = jnp.concatenate([query_rows(h) for h in heads], axis=0)
        span = qx.shape[0]
        maxes, numers, denoms = [], [], []
        for b in range(tiles):
            kb = keys_t[g][:, b * SUB:(b + 1) * SUB]
            bias = jnp.where(position[:, b * SUB:(b + 1) * SUB] < live, 0.0, NEG_FILL)
            s2 = jnp.dot(qx, kb, preferred_element_type=jnp.float32) * scale2 + bias
            tm2 = jnp.max(s2, axis=1, keepdims=True)
            w = jnp.exp2(s2 - tm2).astype(jnp.bfloat16)
            tm = tm2 * LN2
            vb = v_ref[b * SUB:(b + 1) * SUB, g * HEAD_DIM:(g + 1) * HEAD_DIM]
            numers.append(jnp.dot(w, vb, preferred_element_type=jnp.float32))
            denoms.append(jnp.sum(w.astype(jnp.float32), axis=1, keepdims=True))
            maxes.append(tm)
        m = maxes[0]
        for tm in maxes[1:]:
            m = jnp.maximum(m, tm)
        top = jnp.floor(jnp.maximum(m, -60000.0) * 0.25 + 0.5) * 4.0
        numer = jnp.zeros((span, HEAD_DIM), jnp.float32)
        denom = jnp.zeros((span, 1), jnp.float32)
        for tm, nb, db in zip(maxes, numers, denoms):
            f = jnp.exp(tm - top)
            numer = numer + nb * f
            denom = denom + db * f
        mean = numer / jnp.where(denom > 0, denom, 1.0)
        ulp = jnp.exp2(jnp.floor(jnp.log2(jnp.where(denom > 0, denom, 1.0))) - 10.0)
        hi = jnp.where(denom > 0, jnp.round(denom / ulp) * ulp, 0.0)
        for i, h in enumerate(heads):
            rs = slice(i * rows, (i + 1) * rows)
            out_ref[:, h * HEAD_DIM:(h + 1) * HEAD_DIM] = mean[rs]
            extra = jnp.where(lane == h, hi[rs], extra)
            extra = jnp.where(lane == heads_q + h, denom[rs] - hi[rs], extra)
            extra = jnp.where(lane == 2 * heads_q + h, top[rs], extra)
    out_ref[:, heads_q * HEAD_DIM:] = extra


def to_half(part, qcols, heads_q):
    return part.astype(jnp.float16)


def cache_partials(cache_length, queries, keys, values, qcols, rows, block, first, pieces,
                   stack, seq_count, after=None):
    qrows, qcols_in = queries.shape
    cache_rows, kcols = keys.shape
    out_cols = qcols + 128
    heads_q = qcols // HEAD_DIM
    if pieces > 0 or block == qrows:
        q_spec = pl.BlockSpec((qrows, qcols_in), lambda i: (0, 0))
    else:
        q_spec = pl.BlockSpec((block, qcols_in), lambda i: (i, 0))
    in_specs = [
        pl.BlockSpec(memory_space=pltpu.SMEM),
        q_spec,
        pl.BlockSpec((cache_rows, kcols), lambda i: (0, 0)),
        pl.BlockSpec((cache_rows, kcols), lambda i: (0, 0)),
    ]
    operands = [cache_length, queries, keys, values]
    if after is not None:
        in_specs.append(pl.BlockSpec(memory_space=pl.ANY))
        operands.append(after)
    return pl.pallas_call(
        functools.partial(cache_kernel, seq_count, first, pieces, stack),
        grid=(rows // block,),
        in_specs=in_specs,
        out_specs=pl.BlockSpec((block, out_cols), lambda i: (i, 0)),
        out_shape=jax.ShapeDtypeStruct((rows, out_cols), jnp.float32),
        cost_estimate=pl.CostEstimate(
            flops=4 * rows * cache_rows * qcols,
            transcendentals=rows * cache_rows * heads_q,
            bytes_accessed=2 * (rows * qcols_in + 2 * cache_rows * kcols) + 4 * rows * out_cols,
        ),
    )(*operands)


def on_device(
    new_queries, new_keys, new_values, cache_keys, cache_values, segment_ids, cache_length
):
    head_size = HEAD_DIM
    own_count = new_queries.shape[0]
    join_rows = segment_ids.shape[0]
    cache_rows = cache_keys.shape[0]
    heads_kv = cache_keys.shape[1] // head_size
    heads_q = new_queries.shape[1] // head_size
    group_size = heads_q // heads_kv
    qcols = heads_q * head_size
    kcols = heads_kv * head_size
    seq_count = lax.axis_size("seq")
    seq_rank = lax.axis_index("seq")
    score_scale = head_size ** (-0.5)

    packed = jnp.concatenate([new_queries, new_keys, new_values], axis=1)
    gathered = lax.all_gather(packed, "seq", axis=0, tiled=True)
    all_keys = gathered[:, qcols:qcols + kcols]
    all_values = gathered[:, qcols + kcols:]

    if seq_count <= 8:
        remote = cache_partials(
            cache_length, gathered, cache_keys, cache_values, qcols,
            (seq_count - 1) * own_count, (seq_count - 1) * own_count, 1, seq_count - 1, 1,
            seq_count,
        )
        parts = []
        for shift in range(1, seq_count):
            piece = remote[(shift - 1) * own_count:shift * own_count]
            parts.append(
                lax.ppermute(
                    to_half(piece, qcols, heads_q),
                    "seq",
                    [(i, (i + shift) % seq_count) for i in range(seq_count)],
                ).astype(jnp.float32)
            )
        own = cache_partials(
            cache_length, new_queries, cache_keys, cache_values, qcols,
            own_count, own_count, 0, 0, group_size, seq_count, after=remote,
        )
        parts.append(own)
    else:
        partial = cache_partials(
            cache_length, gathered, cache_keys, cache_values, qcols,
            join_rows, min(join_rows, 256), 0, 0, 1, seq_count,
        )
        recv = lax.all_to_all(to_half(partial, qcols, heads_q), "seq", 0, 0, tiled=True)
        recv = recv.astype(jnp.float32)
        parts = [recv[j * own_count:(j + 1) * own_count] for j in range(seq_count)]
    part_mean = [p[:, :qcols] for p in parts]
    part_denom = [
        p[:, qcols:qcols + heads_q] + p[:, qcols + heads_q:qcols + 2 * heads_q] for p in parts
    ]
    part_max = [p[:, qcols + 2 * heads_q:qcols + 3 * heads_q] for p in parts]

    own_queries = new_queries.reshape(own_count, heads_kv, group_size, head_size)
    fresh_scores = (
        jnp.einsum(
            "cgrd,tgd->cgrt",
            own_queries,
            all_keys.reshape(join_rows, heads_kv, head_size),
            preferred_element_type=jnp.float32,
        )
        * score_scale
    )
    start_row = seq_rank * own_count
    own_positions = start_row + jnp.arange(own_count, dtype=jnp.int32)
    own_segments = lax.dynamic_slice_in_dim(segment_ids, start_row, own_count, 0)
    key_positions = jnp.arange(join_rows, dtype=jnp.int32)
    allowed = (key_positions[None, :] <= own_positions[:, None]) & (
        segment_ids[None, :] == own_segments[:, None]
    )
    allowed = allowed[:, None, None, :]
    fresh_max = jnp.max(jnp.where(allowed, fresh_scores, NEG_FILL), axis=-1)
    fresh_weights = jnp.exp(
        jnp.where(allowed, fresh_scores - fresh_max[..., None], NEG_FILL)
    ).astype(jnp.bfloat16)
    fresh_numer = jnp.einsum(
        "cgrt,tgd->cgrd",
        fresh_weights,
        all_values.reshape(join_rows, heads_kv, head_size),
        preferred_element_type=jnp.float32,
    ).reshape(own_count, qcols)
    fresh_denom = jnp.sum(fresh_weights.astype(jnp.float32), axis=-1).reshape(own_count, heads_q)
    fresh_max = fresh_max.reshape(own_count, heads_q)


    def spread(x):
        return jnp.broadcast_to(x[:, :, None], (own_count, heads_q, head_size)).reshape(
            own_count, qcols
        )

    own_mean, own_denom, own_max = part_mean[-1], part_denom[-1], part_max[-1]
    local_max = jnp.maximum(fresh_max, own_max)
    fresh_factor = jnp.exp(fresh_max - local_max)
    own_weight = jnp.exp(own_max - local_max) * own_denom
    local_numer = fresh_numer * spread(fresh_factor) + own_mean * spread(own_weight)
    local_denom = fresh_denom * fresh_factor + own_weight

    row_max = local_max
    for m in part_max[:-1]:
        row_max = jnp.maximum(row_max, m)
    local_factor = jnp.exp(local_max - row_max)
    total_numer = local_numer * spread(local_factor)
    total_denom = local_denom * local_factor
    for o_j, d_j, m_j in zip(part_mean[:-1], part_denom[:-1], part_max[:-1]):
        w_j = jnp.exp(m_j - row_max) * d_j
        total_numer = total_numer + o_j * spread(w_j)
        total_denom = total_denom + w_j
    attended = total_numer / spread(total_denom)
    return attended.astype(jnp.bfloat16)


def solution(mesh):
    placed = (
        P(("group", "seq"), "head"),
        P(("group", "seq"), "head"),
        P(("group", "seq"), "head"),
        P(("group", "seq"), "head"),
        P(("group", "seq"), "head"),
        P("group"),
        P("group"),
    )
    return jax.shard_map(
        on_device,
        mesh=mesh,
        in_specs=placed,
        out_specs=P(("group", "seq"), "head"),
        check_vma=False,
    )
```

```python
import functools

import jax
import jax.numpy as jnp
from jax import lax
from jax.experimental import pallas as pl
from jax.experimental.pallas import tpu as pltpu
from jax.sharding import PartitionSpec as P

HEAD_DIM = 128
SUB = 256
NEG_FILL = -1e30


def cache_kernel(seq_count, first, pieces, stack, len_ref, q_ref, k_ref, v_ref, *rest):
    out_ref = rest[-1]
    rank = lax.axis_index("seq")
    cache_rows = k_ref.shape[0]
    live = jnp.clip(len_ref[0] - rank * cache_rows, 0, cache_rows)
    rows = out_ref.shape[0]
    heads_q = (out_ref.shape[1] - 128) // HEAD_DIM
    heads_kv = k_ref.shape[1] // HEAD_DIM
    group = heads_q // heads_kv
    tiles = cache_rows // SUB
    scale = HEAD_DIM ** (-0.5)
    lane = lax.broadcasted_iota(jnp.int32, (rows, 128), 1)
    position = lax.broadcasted_iota(jnp.int32, (1, cache_rows), 1)
    extra = jnp.zeros((rows, 128), jnp.float32)

    def query_rows(h):
        cols = slice(h * HEAD_DIM, (h + 1) * HEAD_DIM)
        if pieces == 0:
            return q_ref[:, cols]
        piece = rows // pieces
        blocks = []
        for p in range(pieces):
            index = lax.rem(rank + first + p, seq_count)
            blocks.append(q_ref[pl.ds(pl.multiple_of(index * piece, piece), piece), cols])
        return jnp.concatenate(blocks, axis=0)

    keys_t = [k_ref[:, g * HEAD_DIM:(g + 1) * HEAD_DIM].T for g in range(heads_kv)]
    if stack > 1:
        units = [list(range(g * group, (g + 1) * group)) for g in range(heads_kv)]
    else:
        units = [[h] for h in range(heads_q)]
    for heads in units:
        g = heads[0] // group
        qx = jnp.concatenate([query_rows(h) for h in heads], axis=0)
        span = qx.shape[0]
        maxes, numers, denoms = [], [], []
        for b in range(tiles):
            kb = keys_t[g][:, b * SUB:(b + 1) * SUB]
            bias = jnp.where(position[:, b * SUB:(b + 1) * SUB] < live, 0.0, NEG_FILL)
            s = jnp.dot(qx, kb, preferred_element_type=jnp.float32) * scale + bias
            tm = jnp.max(s, axis=1, keepdims=True)
            w = jnp.exp(s - tm).astype(jnp.bfloat16)
            vb = v_ref[b * SUB:(b + 1) * SUB, g * HEAD_DIM:(g + 1) * HEAD_DIM]
            numers.append(jnp.dot(w, vb, preferred_element_type=jnp.float32))
            denoms.append(jnp.sum(w.astype(jnp.float32), axis=1, keepdims=True))
            maxes.append(tm)
        m = maxes[0]
        for tm in maxes[1:]:
            m = jnp.maximum(m, tm)
        top = jnp.floor(jnp.maximum(m, -60000.0) * 0.25 + 0.5) * 4.0
        numer = jnp.zeros((span, HEAD_DIM), jnp.float32)
        denom = jnp.zeros((span, 1), jnp.float32)
        for tm, nb, db in zip(maxes, numers, denoms):
            f = jnp.exp(tm - top)
            numer = numer + nb * f
            denom = denom + db * f
        mean = numer / jnp.where(denom > 0, denom, 1.0)
        ulp = jnp.exp2(jnp.floor(jnp.log2(jnp.where(denom > 0, denom, 1.0))) - 10.0)
        hi = jnp.where(denom > 0, jnp.round(denom / ulp) * ulp, 0.0)
        for i, h in enumerate(heads):
            rs = slice(i * rows, (i + 1) * rows)
            out_ref[:, h * HEAD_DIM:(h + 1) * HEAD_DIM] = mean[rs]
            extra = jnp.where(lane == h, hi[rs], extra)
            extra = jnp.where(lane == heads_q + h, denom[rs] - hi[rs], extra)
            extra = jnp.where(lane == 2 * heads_q + h, top[rs], extra)
    out_ref[:, heads_q * HEAD_DIM:] = extra


def to_half(part, qcols, heads_q):
    return part.astype(jnp.float16)


def cache_partials(cache_length, queries, keys, values, qcols, rows, block, first, pieces,
                   stack, seq_count, after=None):
    qrows, qcols_in = queries.shape
    cache_rows, kcols = keys.shape
    out_cols = qcols + 128
    heads_q = qcols // HEAD_DIM
    if pieces > 0 or block == qrows:
        q_spec = pl.BlockSpec((qrows, qcols), lambda i: (0, 0))
    else:
        q_spec = pl.BlockSpec((block, qcols), lambda i: (i, 0))
    in_specs = [
        pl.BlockSpec(memory_space=pltpu.SMEM),
        q_spec,
        pl.BlockSpec((cache_rows, kcols), lambda i: (0, 0)),
        pl.BlockSpec((cache_rows, kcols), lambda i: (0, 0)),
    ]
    operands = [cache_length, queries, keys, values]
    if after is not None:
        in_specs.append(pl.BlockSpec(memory_space=pl.ANY))
        operands.append(after)
    return pl.pallas_call(
        functools.partial(cache_kernel, seq_count, first, pieces, stack),
        grid=(rows // block,),
        in_specs=in_specs,
        out_specs=pl.BlockSpec((block, out_cols), lambda i: (i, 0)),
        out_shape=jax.ShapeDtypeStruct((rows, out_cols), jnp.float32),
        cost_estimate=pl.CostEstimate(
            flops=4 * rows * cache_rows * qcols,
            transcendentals=rows * cache_rows * heads_q,
            bytes_accessed=2 * (rows * qcols + 2 * cache_rows * kcols) + 4 * rows * out_cols,
        ),
    )(*operands)


def on_device(
    new_queries, new_keys, new_values, cache_keys, cache_values, segment_ids, cache_length
):
    head_size = HEAD_DIM
    own_count = new_queries.shape[0]
    join_rows = segment_ids.shape[0]
    cache_rows = cache_keys.shape[0]
    heads_kv = cache_keys.shape[1] // head_size
    heads_q = new_queries.shape[1] // head_size
    group_size = heads_q // heads_kv
    qcols = heads_q * head_size
    kcols = heads_kv * head_size
    seq_count = lax.axis_size("seq")
    seq_rank = lax.axis_index("seq")
    score_scale = head_size ** (-0.5)

    packed = jnp.concatenate([new_queries, new_keys, new_values], axis=1)
    gathered = lax.all_gather(packed, "seq", axis=0, tiled=True)
    all_keys = gathered[:, qcols:qcols + kcols]
    all_values = gathered[:, qcols + kcols:]

    if seq_count <= 8:
        remote = cache_partials(
            cache_length, gathered, cache_keys, cache_values, qcols,
            (seq_count - 1) * own_count, (seq_count - 1) * own_count, 1, seq_count - 1, 1,
            seq_count,
        )
        parts = []
        for shift in range(1, seq_count):
            piece = remote[(shift - 1) * own_count:shift * own_count]
            parts.append(
                lax.ppermute(
                    to_half(piece, qcols, heads_q),
                    "seq",
                    [(i, (i + shift) % seq_count) for i in range(seq_count)],
                ).astype(jnp.float32)
            )
        own = cache_partials(
            cache_length, new_queries, cache_keys, cache_values, qcols,
            own_count, own_count, 0, 0, group_size, seq_count, after=remote,
        )
        parts.append(own)
    else:
        partial = cache_partials(
            cache_length, gathered, cache_keys, cache_values, qcols,
            join_rows, min(join_rows, 256), 0, 0, 1, seq_count,
        )
        recv = lax.all_to_all(to_half(partial, qcols, heads_q), "seq", 0, 0, tiled=True)
        recv = recv.astype(jnp.float32)
        parts = [recv[j * own_count:(j + 1) * own_count] for j in range(seq_count)]
    part_mean = [p[:, :qcols] for p in parts]
    part_denom = [
        p[:, qcols:qcols + heads_q] + p[:, qcols + heads_q:qcols + 2 * heads_q] for p in parts
    ]
    part_max = [p[:, qcols + 2 * heads_q:qcols + 3 * heads_q] for p in parts]

    own_queries = new_queries.reshape(own_count, heads_kv, group_size, head_size)
    fresh_scores = (
        jnp.einsum(
            "cgrd,tgd->cgrt",
            own_queries,
            all_keys.reshape(join_rows, heads_kv, head_size),
            preferred_element_type=jnp.float32,
        )
        * score_scale
    )
    start_row = seq_rank * own_count
    own_positions = start_row + jnp.arange(own_count, dtype=jnp.int32)
    own_segments = lax.dynamic_slice_in_dim(segment_ids, start_row, own_count, 0)
    key_positions = jnp.arange(join_rows, dtype=jnp.int32)
    allowed = (key_positions[None, :] <= own_positions[:, None]) & (
        segment_ids[None, :] == own_segments[:, None]
    )
    allowed = allowed[:, None, None, :]
    fresh_max = jnp.max(jnp.where(allowed, fresh_scores, NEG_FILL), axis=-1)
    fresh_weights = jnp.exp(
        jnp.where(allowed, fresh_scores - fresh_max[..., None], NEG_FILL)
    ).astype(jnp.bfloat16)
    fresh_numer = jnp.einsum(
        "cgrt,tgd->cgrd",
        fresh_weights,
        all_values.reshape(join_rows, heads_kv, head_size),
        preferred_element_type=jnp.float32,
    ).reshape(own_count, qcols)
    fresh_denom = jnp.sum(fresh_weights.astype(jnp.float32), axis=-1).reshape(own_count, heads_q)
    fresh_max = fresh_max.reshape(own_count, heads_q)


    def spread(x):
        return jnp.broadcast_to(x[:, :, None], (own_count, heads_q, head_size)).reshape(
            own_count, qcols
        )

    own_mean, own_denom, own_max = part_mean[-1], part_denom[-1], part_max[-1]
    local_max = jnp.maximum(fresh_max, own_max)
    fresh_factor = jnp.exp(fresh_max - local_max)
    own_weight = jnp.exp(own_max - local_max) * own_denom
    local_numer = fresh_numer * spread(fresh_factor) + own_mean * spread(own_weight)
    local_denom = fresh_denom * fresh_factor + own_weight

    row_max = local_max
    for m in part_max[:-1]:
        row_max = jnp.maximum(row_max, m)
    local_factor = jnp.exp(local_max - row_max)
    total_numer = local_numer * spread(local_factor)
    total_denom = local_denom * local_factor
    for o_j, d_j, m_j in zip(part_mean[:-1], part_denom[:-1], part_max[:-1]):
        w_j = jnp.exp(m_j - row_max) * d_j
        total_numer = total_numer + o_j * spread(w_j)
        total_denom = total_denom + w_j
    attended = total_numer / spread(total_denom)
    return attended.astype(jnp.bfloat16)


def solution(mesh):
    placed = (
        P(("group", "seq"), "head"),
        P(("group", "seq"), "head"),
        P(("group", "seq"), "head"),
        P(("group", "seq"), "head"),
        P(("group", "seq"), "head"),
        P("group"),
        P("group"),
    )
    return jax.shard_map(
        on_device,
        mesh=mesh,
        in_specs=placed,
        out_specs=P(("group", "seq"), "head"),
        check_vma=False,
    )
```

```python
import functools

import jax
import jax.numpy as jnp
from jax import lax
from jax.experimental import pallas as pl
from jax.experimental.pallas import tpu as pltpu
from jax.sharding import PartitionSpec as P

HEAD_DIM = 128
SUB = 256
NEG_FILL = -1e30


def cache_kernel(seq_count, shifts, stack, len_ref, q_ref, k_ref, v_ref, *rest):
    out_ref = rest[-1]
    rank = lax.axis_index("seq")
    cache_rows = k_ref.shape[0]
    live = jnp.clip(len_ref[0] - rank * cache_rows, 0, cache_rows)
    rows = out_ref.shape[0]
    heads_q = (out_ref.shape[1] - 128) // HEAD_DIM
    heads_kv = k_ref.shape[1] // HEAD_DIM
    group = heads_q // heads_kv
    tiles = cache_rows // SUB
    scale = HEAD_DIM ** (-0.5)
    lane = lax.broadcasted_iota(jnp.int32, (rows, 128), 1)
    position = lax.broadcasted_iota(jnp.int32, (1, cache_rows), 1)
    extra = jnp.zeros((rows, 128), jnp.float32)

    def query_rows(h):
        cols = slice(h * HEAD_DIM, (h + 1) * HEAD_DIM)
        pieces = len(shifts)
        if pieces == 0:
            return q_ref[:, cols]
        piece = rows // pieces
        blocks = []
        for shift in shifts:
            index = lax.rem(rank + shift, seq_count)
            blocks.append(q_ref[pl.ds(pl.multiple_of(index * piece, piece), piece), cols])
        return jnp.concatenate(blocks, axis=0)

    keys_t = [k_ref[:, g * HEAD_DIM:(g + 1) * HEAD_DIM].T for g in range(heads_kv)]
    if stack > 1:
        units = [list(range(g * group, (g + 1) * group)) for g in range(heads_kv)]
    else:
        units = [[h] for h in range(heads_q)]
    for heads in units:
        g = heads[0] // group
        qx = jnp.concatenate([query_rows(h) for h in heads], axis=0)
        span = qx.shape[0]
        maxes, numers, denoms = [], [], []
        for b in range(tiles):
            kb = keys_t[g][:, b * SUB:(b + 1) * SUB]
            bias = jnp.where(position[:, b * SUB:(b + 1) * SUB] < live, 0.0, NEG_FILL)
            s = jnp.dot(qx, kb, preferred_element_type=jnp.float32) * scale + bias
            tm = jnp.max(s, axis=1, keepdims=True)
            w = jnp.exp(s - tm).astype(jnp.bfloat16)
            vb = v_ref[b * SUB:(b + 1) * SUB, g * HEAD_DIM:(g + 1) * HEAD_DIM]
            numers.append(jnp.dot(w, vb, preferred_element_type=jnp.float32))
            denoms.append(jnp.sum(w.astype(jnp.float32), axis=1, keepdims=True))
            maxes.append(tm)
        m = maxes[0]
        for tm in maxes[1:]:
            m = jnp.maximum(m, tm)
        top = jnp.floor(jnp.maximum(m, -60000.0) * 0.25 + 0.5) * 4.0
        numer = jnp.zeros((span, HEAD_DIM), jnp.float32)
        denom = jnp.zeros((span, 1), jnp.float32)
        for tm, nb, db in zip(maxes, numers, denoms):
            f = jnp.exp(tm - top)
            numer = numer + nb * f
            denom = denom + db * f
        mean = numer / jnp.where(denom > 0, denom, 1.0)
        ulp = jnp.exp2(jnp.floor(jnp.log2(jnp.where(denom > 0, denom, 1.0))) - 10.0)
        hi = jnp.where(denom > 0, jnp.round(denom / ulp) * ulp, 0.0)
        for i, h in enumerate(heads):
            rs = slice(i * rows, (i + 1) * rows)
            out_ref[:, h * HEAD_DIM:(h + 1) * HEAD_DIM] = mean[rs]
            extra = jnp.where(lane == h, hi[rs], extra)
            extra = jnp.where(lane == heads_q + h, denom[rs] - hi[rs], extra)
            extra = jnp.where(lane == 2 * heads_q + h, top[rs], extra)
    out_ref[:, heads_q * HEAD_DIM:] = extra


def to_half(part, qcols, heads_q):
    return part.astype(jnp.float16)


def cache_partials(cache_length, queries, keys, values, qcols, rows, block, shifts,
                   stack, seq_count, after=None):
    qrows, qcols_in = queries.shape
    cache_rows, kcols = keys.shape
    out_cols = qcols + 128
    heads_q = qcols // HEAD_DIM
    if shifts or block == qrows:
        q_spec = pl.BlockSpec((qrows, qcols), lambda i: (0, 0))
    else:
        q_spec = pl.BlockSpec((block, qcols), lambda i: (i, 0))
    in_specs = [
        pl.BlockSpec(memory_space=pltpu.SMEM),
        q_spec,
        pl.BlockSpec((cache_rows, kcols), lambda i: (0, 0)),
        pl.BlockSpec((cache_rows, kcols), lambda i: (0, 0)),
    ]
    operands = [cache_length, queries, keys, values]
    if after is not None:
        in_specs.append(pl.BlockSpec(memory_space=pl.ANY))
        operands.append(after)
    return pl.pallas_call(
        functools.partial(cache_kernel, seq_count, shifts, stack),
        grid=(rows // block,),
        in_specs=in_specs,
        out_specs=pl.BlockSpec((block, out_cols), lambda i: (i, 0)),
        out_shape=jax.ShapeDtypeStruct((rows, out_cols), jnp.float32),
        cost_estimate=pl.CostEstimate(
            flops=4 * rows * cache_rows * qcols,
            transcendentals=rows * cache_rows * heads_q,
            bytes_accessed=2 * (rows * qcols + 2 * cache_rows * kcols) + 4 * rows * out_cols,
        ),
    )(*operands)


def on_device(
    new_queries, new_keys, new_values, cache_keys, cache_values, segment_ids, cache_length
):
    head_size = HEAD_DIM
    own_count = new_queries.shape[0]
    join_rows = segment_ids.shape[0]
    cache_rows = cache_keys.shape[0]
    heads_kv = cache_keys.shape[1] // head_size
    heads_q = new_queries.shape[1] // head_size
    group_size = heads_q // heads_kv
    qcols = heads_q * head_size
    kcols = heads_kv * head_size
    seq_count = lax.axis_size("seq")
    seq_rank = lax.axis_index("seq")
    score_scale = head_size ** (-0.5)

    packed = jnp.concatenate([new_queries, new_keys, new_values], axis=1)
    gathered = lax.all_gather(packed, "seq", axis=0, tiled=True)
    all_keys = gathered[:, qcols:qcols + kcols]
    all_values = gathered[:, qcols + kcols:]

    if seq_count <= 8:
        lead = seq_count // 2
        rest_shifts = tuple(s for s in range(1, seq_count) if s != lead)
        pairs = lambda s: [(i, (i + s) % seq_count) for i in range(seq_count)]
        first_part = cache_partials(
            cache_length, gathered, cache_keys, cache_values, qcols,
            own_count, own_count, (lead,), group_size, seq_count,
        )
        parts = [
            lax.ppermute(to_half(first_part, qcols, heads_q), "seq", pairs(lead)).astype(jnp.float32)
        ]
        if rest_shifts:
            rest = cache_partials(
                cache_length, gathered, cache_keys, cache_values, qcols,
                len(rest_shifts) * own_count, len(rest_shifts) * own_count, rest_shifts, 1,
                seq_count, after=first_part,
            )
            for k, shift in enumerate(rest_shifts):
                piece = rest[k * own_count:(k + 1) * own_count]
                parts.append(
                    lax.ppermute(to_half(piece, qcols, heads_q), "seq", pairs(shift)).astype(
                        jnp.float32
                    )
                )
            remote = rest
        else:
            remote = first_part
        own = cache_partials(
            cache_length, new_queries, cache_keys, cache_values, qcols,
            own_count, own_count, (), group_size, seq_count, after=remote,
        )
        parts.append(own)
    else:
        partial = cache_partials(
            cache_length, gathered, cache_keys, cache_values, qcols,
            join_rows, min(join_rows, 256), (), 1, seq_count,
        )
        recv = lax.all_to_all(to_half(partial, qcols, heads_q), "seq", 0, 0, tiled=True)
        recv = recv.astype(jnp.float32)
        parts = [recv[j * own_count:(j + 1) * own_count] for j in range(seq_count)]
    part_mean = [p[:, :qcols] for p in parts]
    part_denom = [
        p[:, qcols:qcols + heads_q] + p[:, qcols + heads_q:qcols + 2 * heads_q] for p in parts
    ]
    part_max = [p[:, qcols + 2 * heads_q:qcols + 3 * heads_q] for p in parts]

    own_queries = new_queries.reshape(own_count, heads_kv, group_size, head_size)
    fresh_scores = (
        jnp.einsum(
            "cgrd,tgd->cgrt",
            own_queries,
            all_keys.reshape(join_rows, heads_kv, head_size),
            preferred_element_type=jnp.float32,
        )
        * score_scale
    )
    start_row = seq_rank * own_count
    own_positions = start_row + jnp.arange(own_count, dtype=jnp.int32)
    own_segments = lax.dynamic_slice_in_dim(segment_ids, start_row, own_count, 0)
    key_positions = jnp.arange(join_rows, dtype=jnp.int32)
    allowed = (key_positions[None, :] <= own_positions[:, None]) & (
        segment_ids[None, :] == own_segments[:, None]
    )
    allowed = allowed[:, None, None, :]
    fresh_max = jnp.max(jnp.where(allowed, fresh_scores, NEG_FILL), axis=-1)
    fresh_weights = jnp.exp(
        jnp.where(allowed, fresh_scores - fresh_max[..., None], NEG_FILL)
    ).astype(jnp.bfloat16)
    fresh_numer = jnp.einsum(
        "cgrt,tgd->cgrd",
        fresh_weights,
        all_values.reshape(join_rows, heads_kv, head_size),
        preferred_element_type=jnp.float32,
    ).reshape(own_count, qcols)
    fresh_denom = jnp.sum(fresh_weights.astype(jnp.float32), axis=-1).reshape(own_count, heads_q)
    fresh_max = fresh_max.reshape(own_count, heads_q)


    def spread(x):
        return jnp.broadcast_to(x[:, :, None], (own_count, heads_q, head_size)).reshape(
            own_count, qcols
        )

    own_mean, own_denom, own_max = part_mean[-1], part_denom[-1], part_max[-1]
    local_max = jnp.maximum(fresh_max, own_max)
    fresh_factor = jnp.exp(fresh_max - local_max)
    own_weight = jnp.exp(own_max - local_max) * own_denom
    local_numer = fresh_numer * spread(fresh_factor) + own_mean * spread(own_weight)
    local_denom = fresh_denom * fresh_factor + own_weight

    row_max = local_max
    for m in part_max[:-1]:
        row_max = jnp.maximum(row_max, m)
    local_factor = jnp.exp(local_max - row_max)
    total_numer = local_numer * spread(local_factor)
    total_denom = local_denom * local_factor
    for o_j, d_j, m_j in zip(part_mean[:-1], part_denom[:-1], part_max[:-1]):
        w_j = jnp.exp(m_j - row_max) * d_j
        total_numer = total_numer + o_j * spread(w_j)
        total_denom = total_denom + w_j
    attended = total_numer / spread(total_denom)
    return attended.astype(jnp.bfloat16)


def solution(mesh):
    placed = (
        P(("group", "seq"), "head"),
        P(("group", "seq"), "head"),
        P(("group", "seq"), "head"),
        P(("group", "seq"), "head"),
        P(("group", "seq"), "head"),
        P("group"),
        P("group"),
    )
    return jax.shard_map(
        on_device,
        mesh=mesh,
        in_specs=placed,
        out_specs=P(("group", "seq"), "head"),
        check_vma=False,
    )
```

```python
import functools

import jax
import jax.numpy as jnp
from jax import lax
from jax.experimental import pallas as pl
from jax.experimental.pallas import tpu as pltpu
from jax.sharding import PartitionSpec as P

HEAD_DIM = 128
SUB = 256
NEG_FILL = -1e30


def cache_kernel(seq_count, first, pieces, stack, len_ref, q_ref, k_ref, v_ref, *rest):
    out_ref = rest[-1]
    rank = lax.axis_index("seq")
    cache_rows = k_ref.shape[0]
    live = jnp.clip(len_ref[0] - rank * cache_rows, 0, cache_rows)
    rows = out_ref.shape[0]
    heads_q = (out_ref.shape[1] - 128) // HEAD_DIM
    heads_kv = k_ref.shape[1] // HEAD_DIM
    group = heads_q // heads_kv
    tiles = cache_rows // SUB
    scale = HEAD_DIM ** (-0.5)
    lane = lax.broadcasted_iota(jnp.int32, (rows, 128), 1)
    position = lax.broadcasted_iota(jnp.int32, (1, cache_rows), 1)
    extra = jnp.zeros((rows, 128), jnp.float32)

    def query_rows(h):
        cols = slice(h * HEAD_DIM, (h + 1) * HEAD_DIM)
        if pieces == 0:
            return q_ref[:, cols]
        piece = rows // pieces
        blocks = []
        for p in range(pieces):
            index = lax.rem(rank + first + p, seq_count)
            blocks.append(q_ref[pl.ds(pl.multiple_of(index * piece, piece), piece), cols])
        return jnp.concatenate(blocks, axis=0)

    keys_t = [k_ref[:, g * HEAD_DIM:(g + 1) * HEAD_DIM].T for g in range(heads_kv)]
    if stack > 1:
        units = [list(range(g * group, (g + 1) * group)) for g in range(heads_kv)]
    else:
        units = [[h] for h in range(heads_q)]
    for heads in units:
        g = heads[0] // group
        qx = jnp.concatenate([query_rows(h) for h in heads], axis=0)
        span = qx.shape[0]
        maxes, numers, denoms = [], [], []
        for b in range(tiles):
            kb = keys_t[g][:, b * SUB:(b + 1) * SUB]
            bias = jnp.where(position[:, b * SUB:(b + 1) * SUB] < live, 0.0, NEG_FILL)
            s = jnp.dot(qx, kb, preferred_element_type=jnp.float32) * scale + bias
            tm = jnp.max(s, axis=1, keepdims=True)
            w = jnp.exp(s - tm).astype(jnp.bfloat16)
            vb = v_ref[b * SUB:(b + 1) * SUB, g * HEAD_DIM:(g + 1) * HEAD_DIM]
            numers.append(jnp.dot(w, vb, preferred_element_type=jnp.float32))
            denoms.append(jnp.sum(w.astype(jnp.float32), axis=1, keepdims=True))
            maxes.append(tm)
        m = maxes[0]
        for tm in maxes[1:]:
            m = jnp.maximum(m, tm)
        top = jnp.floor(jnp.maximum(m, -60000.0) * 0.25 + 0.5) * 4.0
        numer = jnp.zeros((span, HEAD_DIM), jnp.float32)
        denom = jnp.zeros((span, 1), jnp.float32)
        for tm, nb, db in zip(maxes, numers, denoms):
            f = jnp.exp(tm - top)
            numer = numer + nb * f
            denom = denom + db * f
        mean = numer / jnp.where(denom > 0, denom, 1.0)
        ulp = jnp.exp2(jnp.floor(jnp.log2(jnp.where(denom > 0, denom, 1.0))) - 10.0)
        hi = jnp.where(denom > 0, jnp.round(denom / ulp) * ulp, 0.0)
        for i, h in enumerate(heads):
            rs = slice(i * rows, (i + 1) * rows)
            out_ref[:, h * HEAD_DIM:(h + 1) * HEAD_DIM] = mean[rs]
            extra = jnp.where(lane == h, hi[rs], extra)
            extra = jnp.where(lane == heads_q + h, denom[rs] - hi[rs], extra)
            extra = jnp.where(lane == 2 * heads_q + h, top[rs], extra)
    out_ref[:, heads_q * HEAD_DIM:] = extra


def to_half(part, qcols, heads_q):
    return part.astype(jnp.float16)


def cache_partials(cache_length, queries, keys, values, qcols, rows, block, first, pieces,
                   stack, seq_count, after=None):
    qrows, qcols_in = queries.shape
    cache_rows, kcols = keys.shape
    out_cols = qcols + 128
    heads_q = qcols // HEAD_DIM
    if pieces > 0 or block == qrows:
        q_spec = pl.BlockSpec((qrows, qcols), lambda i: (0, 0))
    else:
        q_spec = pl.BlockSpec((block, qcols), lambda i: (i, 0))
    in_specs = [
        pl.BlockSpec(memory_space=pltpu.SMEM),
        q_spec,
        pl.BlockSpec((cache_rows, kcols), lambda i: (0, 0)),
        pl.BlockSpec((cache_rows, kcols), lambda i: (0, 0)),
    ]
    operands = [cache_length, queries, keys, values]
    if after is not None:
        in_specs.append(pl.BlockSpec(memory_space=pl.ANY))
        operands.append(after)
    return pl.pallas_call(
        functools.partial(cache_kernel, seq_count, first, pieces, stack),
        grid=(rows // block,),
        in_specs=in_specs,
        out_specs=pl.BlockSpec((block, out_cols), lambda i: (i, 0)),
        out_shape=jax.ShapeDtypeStruct((rows, out_cols), jnp.float32),
        cost_estimate=pl.CostEstimate(
            flops=4 * rows * cache_rows * qcols,
            transcendentals=rows * cache_rows * heads_q,
            bytes_accessed=2 * (rows * qcols + 2 * cache_rows * kcols) + 4 * rows * out_cols,
        ),
    )(*operands)


def on_device(
    new_queries, new_keys, new_values, cache_keys, cache_values, segment_ids, cache_length
):
    head_size = HEAD_DIM
    own_count = new_queries.shape[0]
    join_rows = segment_ids.shape[0]
    cache_rows = cache_keys.shape[0]
    heads_kv = cache_keys.shape[1] // head_size
    heads_q = new_queries.shape[1] // head_size
    group_size = heads_q // heads_kv
    qcols = heads_q * head_size
    kcols = heads_kv * head_size
    seq_count = lax.axis_size("seq")
    seq_rank = lax.axis_index("seq")
    score_scale = head_size ** (-0.5)

    packed = jnp.concatenate([new_queries, new_keys, new_values], axis=1)
    gathered = lax.all_gather(packed, "seq", axis=0, tiled=True)
    all_keys = gathered[:, qcols:qcols + kcols]
    all_values = gathered[:, qcols + kcols:]

    if seq_count <= 8:
        remote = cache_partials(
            cache_length, gathered, cache_keys, cache_values, qcols,
            (seq_count - 1) * own_count, (seq_count - 1) * own_count, 1, seq_count - 1, 1,
            seq_count,
        )
        parts = []
        for shift in sorted(range(1, seq_count), key=lambda s: abs(2 * s - seq_count)):
            piece = remote[(shift - 1) * own_count:shift * own_count]
            parts.append(
                lax.ppermute(
                    to_half(piece, qcols, heads_q),
                    "seq",
                    [(i, (i + shift) % seq_count) for i in range(seq_count)],
                ).astype(jnp.float32)
            )
        own = cache_partials(
            cache_length, new_queries, cache_keys, cache_values, qcols,
            own_count, own_count, 0, 0, group_size, seq_count, after=remote,
        )
        parts.append(own)
    else:
        partial = cache_partials(
            cache_length, gathered, cache_keys, cache_values, qcols,
            join_rows, min(join_rows, 256), 0, 0, 1, seq_count,
        )
        recv = lax.all_to_all(to_half(partial, qcols, heads_q), "seq", 0, 0, tiled=True)
        recv = recv.astype(jnp.float32)
        parts = [recv[j * own_count:(j + 1) * own_count] for j in range(seq_count)]
    part_mean = [p[:, :qcols] for p in parts]
    part_denom = [
        p[:, qcols:qcols + heads_q] + p[:, qcols + heads_q:qcols + 2 * heads_q] for p in parts
    ]
    part_max = [p[:, qcols + 2 * heads_q:qcols + 3 * heads_q] for p in parts]

    own_queries = new_queries.reshape(own_count, heads_kv, group_size, head_size)
    fresh_scores = (
        jnp.einsum(
            "cgrd,tgd->cgrt",
            own_queries,
            all_keys.reshape(join_rows, heads_kv, head_size),
            preferred_element_type=jnp.float32,
        )
        * score_scale
    )
    start_row = seq_rank * own_count
    own_positions = start_row + jnp.arange(own_count, dtype=jnp.int32)
    own_segments = lax.dynamic_slice_in_dim(segment_ids, start_row, own_count, 0)
    key_positions = jnp.arange(join_rows, dtype=jnp.int32)
    allowed = (key_positions[None, :] <= own_positions[:, None]) & (
        segment_ids[None, :] == own_segments[:, None]
    )
    allowed = allowed[:, None, None, :]
    fresh_max = jnp.max(jnp.where(allowed, fresh_scores, NEG_FILL), axis=-1)
    fresh_weights = jnp.exp(
        jnp.where(allowed, fresh_scores - fresh_max[..., None], NEG_FILL)
    ).astype(jnp.bfloat16)
    fresh_numer = jnp.einsum(
        "cgrt,tgd->cgrd",
        fresh_weights,
        all_values.reshape(join_rows, heads_kv, head_size),
        preferred_element_type=jnp.float32,
    ).reshape(own_count, qcols)
    fresh_denom = jnp.sum(fresh_weights.astype(jnp.float32), axis=-1).reshape(own_count, heads_q)
    fresh_max = fresh_max.reshape(own_count, heads_q)


    def spread(x):
        return jnp.broadcast_to(x[:, :, None], (own_count, heads_q, head_size)).reshape(
            own_count, qcols
        )

    own_mean, own_denom, own_max = part_mean[-1], part_denom[-1], part_max[-1]
    local_max = jnp.maximum(fresh_max, own_max)
    fresh_factor = jnp.exp(fresh_max - local_max)
    own_weight = jnp.exp(own_max - local_max) * own_denom
    local_numer = fresh_numer * spread(fresh_factor) + own_mean * spread(own_weight)
    local_denom = fresh_denom * fresh_factor + own_weight

    row_max = local_max
    for m in part_max[:-1]:
        row_max = jnp.maximum(row_max, m)
    local_factor = jnp.exp(local_max - row_max)
    total_numer = local_numer * spread(local_factor)
    total_denom = local_denom * local_factor
    for o_j, d_j, m_j in zip(part_mean[:-1], part_denom[:-1], part_max[:-1]):
        w_j = jnp.exp(m_j - row_max) * d_j
        total_numer = total_numer + o_j * spread(w_j)
        total_denom = total_denom + w_j
    attended = total_numer / spread(total_denom)
    return attended.astype(jnp.bfloat16)


def solution(mesh):
    placed = (
        P(("group", "seq"), "head"),
        P(("group", "seq"), "head"),
        P(("group", "seq"), "head"),
        P(("group", "seq"), "head"),
        P(("group", "seq"), "head"),
        P("group"),
        P("group"),
    )
    return jax.shard_map(
        on_device,
        mesh=mesh,
        in_specs=placed,
        out_specs=P(("group", "seq"), "head"),
        check_vma=False,
    )
```

```python
import functools

import jax
import jax.numpy as jnp
from jax import lax
from jax.experimental import pallas as pl
from jax.experimental.pallas import tpu as pltpu
from jax.sharding import PartitionSpec as P

HEAD_DIM = 128
SUB = 256
NEG_FILL = -1e30


def cache_kernel(seq_count, first, pieces, stack, len_ref, q_ref, k_ref, v_ref, *rest):
    out_ref = rest[-1]
    rank = lax.axis_index("seq")
    cache_rows = k_ref.shape[0]
    live = jnp.clip(len_ref[0] - rank * cache_rows, 0, cache_rows)
    rows = out_ref.shape[0]
    heads_q = (out_ref.shape[1] - 128) // HEAD_DIM
    heads_kv = k_ref.shape[1] // HEAD_DIM
    group = heads_q // heads_kv
    tiles = cache_rows // SUB
    scale = HEAD_DIM ** (-0.5)
    lane = lax.broadcasted_iota(jnp.int32, (rows, 128), 1)
    position = lax.broadcasted_iota(jnp.int32, (1, cache_rows), 1)
    extra = jnp.zeros((rows, 128), jnp.float32)

    def query_rows(h):
        cols = slice(h * HEAD_DIM, (h + 1) * HEAD_DIM)
        if pieces == 0:
            return q_ref[:, cols]
        piece = rows // pieces
        blocks = []
        for p in range(pieces):
            index = lax.rem(rank + first + p, seq_count)
            blocks.append(q_ref[pl.ds(pl.multiple_of(index * piece, piece), piece), cols])
        return jnp.concatenate(blocks, axis=0)

    keys_t = [k_ref[:, g * HEAD_DIM:(g + 1) * HEAD_DIM].T for g in range(heads_kv)]
    if stack > 1:
        units = [list(range(g * group, (g + 1) * group)) for g in range(heads_kv)]
    else:
        units = [[h] for h in range(heads_q)]
    for heads in units:
        g = heads[0] // group
        qx = jnp.concatenate([query_rows(h) for h in heads], axis=0)
        span = qx.shape[0]
        maxes, numers, denoms = [], [], []
        for b in range(tiles):
            kb = keys_t[g][:, b * SUB:(b + 1) * SUB]
            bias = jnp.where(position[:, b * SUB:(b + 1) * SUB] < live, 0.0, NEG_FILL)
            s = jnp.dot(qx, kb, preferred_element_type=jnp.float32) * scale + bias
            tm = jnp.max(s, axis=1, keepdims=True)
            w = jnp.exp(s - tm).astype(jnp.bfloat16)
            vb = v_ref[b * SUB:(b + 1) * SUB, g * HEAD_DIM:(g + 1) * HEAD_DIM]
            numers.append(jnp.dot(w, vb, preferred_element_type=jnp.float32))
            denoms.append(jnp.sum(w.astype(jnp.float32), axis=1, keepdims=True))
            maxes.append(tm)
        m = maxes[0]
        for tm in maxes[1:]:
            m = jnp.maximum(m, tm)
        top = jnp.floor(jnp.maximum(m, -60000.0) * 0.25 + 0.5) * 4.0
        numer = jnp.zeros((span, HEAD_DIM), jnp.float32)
        denom = jnp.zeros((span, 1), jnp.float32)
        for tm, nb, db in zip(maxes, numers, denoms):
            f = jnp.exp(tm - top)
            numer = numer + nb * f
            denom = denom + db * f
        mean = numer / jnp.where(denom > 0, denom, 1.0)
        ulp = jnp.exp2(jnp.floor(jnp.log2(jnp.where(denom > 0, denom, 1.0))) - 10.0)
        hi = jnp.where(denom > 0, jnp.round(denom / ulp) * ulp, 0.0)
        for i, h in enumerate(heads):
            rs = slice(i * rows, (i + 1) * rows)
            out_ref[:, h * HEAD_DIM:(h + 1) * HEAD_DIM] = mean[rs]
            extra = jnp.where(lane == h, hi[rs], extra)
            extra = jnp.where(lane == heads_q + h, denom[rs] - hi[rs], extra)
            extra = jnp.where(lane == 2 * heads_q + h, top[rs], extra)
    out_ref[:, heads_q * HEAD_DIM:] = extra


def to_half(part, qcols, heads_q):
    return part.astype(jnp.float16)


def cache_partials(cache_length, queries, keys, values, qcols, rows, block, first, pieces,
                   stack, seq_count, after=None):
    qrows, qcols_in = queries.shape
    cache_rows, kcols = keys.shape
    out_cols = qcols + 128
    heads_q = qcols // HEAD_DIM
    if pieces > 0 or block == qrows:
        q_spec = pl.BlockSpec((qrows, qcols), lambda i: (0, 0))
    else:
        q_spec = pl.BlockSpec((block, qcols), lambda i: (i, 0))
    in_specs = [
        pl.BlockSpec(memory_space=pltpu.SMEM),
        q_spec,
        pl.BlockSpec((cache_rows, kcols), lambda i: (0, 0)),
        pl.BlockSpec((cache_rows, kcols), lambda i: (0, 0)),
    ]
    operands = [cache_length, queries, keys, values]
    if after is not None:
        in_specs.append(pl.BlockSpec(memory_space=pl.ANY))
        operands.append(after)
    return pl.pallas_call(
        functools.partial(cache_kernel, seq_count, first, pieces, stack),
        grid=(rows // block,),
        in_specs=in_specs,
        out_specs=pl.BlockSpec((block, out_cols), lambda i: (i, 0)),
        out_shape=jax.ShapeDtypeStruct((rows, out_cols), jnp.float32),
        cost_estimate=pl.CostEstimate(
            flops=4 * rows * cache_rows * qcols,
            transcendentals=rows * cache_rows * heads_q,
            bytes_accessed=2 * (rows * qcols + 2 * cache_rows * kcols) + 4 * rows * out_cols,
        ),
    )(*operands)


def on_device(
    new_queries, new_keys, new_values, cache_keys, cache_values, segment_ids, cache_length
):
    head_size = HEAD_DIM
    own_count = new_queries.shape[0]
    join_rows = segment_ids.shape[0]
    cache_rows = cache_keys.shape[0]
    heads_kv = cache_keys.shape[1] // head_size
    heads_q = new_queries.shape[1] // head_size
    group_size = heads_q // heads_kv
    qcols = heads_q * head_size
    kcols = heads_kv * head_size
    seq_count = lax.axis_size("seq")
    seq_rank = lax.axis_index("seq")
    score_scale = head_size ** (-0.5)

    packed = jnp.concatenate([new_queries, new_keys, new_values], axis=1)
    gathered = lax.all_gather(packed, "seq", axis=0, tiled=True)
    all_keys = gathered[:, qcols:qcols + kcols]
    all_values = gathered[:, qcols + kcols:]

    if seq_count <= 8:
        remote = cache_partials(
            cache_length, gathered, cache_keys, cache_values, qcols,
            (seq_count - 1) * own_count, (seq_count - 1) * own_count, 1, seq_count - 1, 1,
            seq_count,
        )
        parts = []
        for shift in sorted(range(1, seq_count), key=lambda s: (abs(2 * s - seq_count), -s)):
            piece = remote[(shift - 1) * own_count:shift * own_count]
            parts.append(
                lax.ppermute(
                    to_half(piece, qcols, heads_q),
                    "seq",
                    [(i, (i + shift) % seq_count) for i in range(seq_count)],
                ).astype(jnp.float32)
            )
        own = cache_partials(
            cache_length, new_queries, cache_keys, cache_values, qcols,
            own_count, own_count, 0, 0, group_size, seq_count, after=remote,
        )
        parts.append(own)
    else:
        partial = cache_partials(
            cache_length, gathered, cache_keys, cache_values, qcols,
            join_rows, min(join_rows, 256), 0, 0, 1, seq_count,
        )
        recv = lax.all_to_all(to_half(partial, qcols, heads_q), "seq", 0, 0, tiled=True)
        recv = recv.astype(jnp.float32)
        parts = [recv[j * own_count:(j + 1) * own_count] for j in range(seq_count)]
    part_mean = [p[:, :qcols] for p in parts]
    part_denom = [
        p[:, qcols:qcols + heads_q] + p[:, qcols + heads_q:qcols + 2 * heads_q] for p in parts
    ]
    part_max = [p[:, qcols + 2 * heads_q:qcols + 3 * heads_q] for p in parts]

    own_queries = new_queries.reshape(own_count, heads_kv, group_size, head_size)
    fresh_scores = (
        jnp.einsum(
            "cgrd,tgd->cgrt",
            own_queries,
            all_keys.reshape(join_rows, heads_kv, head_size),
            preferred_element_type=jnp.float32,
        )
        * score_scale
    )
    start_row = seq_rank * own_count
    own_positions = start_row + jnp.arange(own_count, dtype=jnp.int32)
    own_segments = lax.dynamic_slice_in_dim(segment_ids, start_row, own_count, 0)
    key_positions = jnp.arange(join_rows, dtype=jnp.int32)
    allowed = (key_positions[None, :] <= own_positions[:, None]) & (
        segment_ids[None, :] == own_segments[:, None]
    )
    allowed = allowed[:, None, None, :]
    fresh_max = jnp.max(jnp.where(allowed, fresh_scores, NEG_FILL), axis=-1)
    fresh_weights = jnp.exp(
        jnp.where(allowed, fresh_scores - fresh_max[..., None], NEG_FILL)
    ).astype(jnp.bfloat16)
    fresh_numer = jnp.einsum(
        "cgrt,tgd->cgrd",
        fresh_weights,
        all_values.reshape(join_rows, heads_kv, head_size),
        preferred_element_type=jnp.float32,
    ).reshape(own_count, qcols)
    fresh_denom = jnp.sum(fresh_weights.astype(jnp.float32), axis=-1).reshape(own_count, heads_q)
    fresh_max = fresh_max.reshape(own_count, heads_q)


    def spread(x):
        return jnp.broadcast_to(x[:, :, None], (own_count, heads_q, head_size)).reshape(
            own_count, qcols
        )

    own_mean, own_denom, own_max = part_mean[-1], part_denom[-1], part_max[-1]
    local_max = jnp.maximum(fresh_max, own_max)
    fresh_factor = jnp.exp(fresh_max - local_max)
    own_weight = jnp.exp(own_max - local_max) * own_denom
    local_numer = fresh_numer * spread(fresh_factor) + own_mean * spread(own_weight)
    local_denom = fresh_denom * fresh_factor + own_weight

    row_max = local_max
    for m in part_max[:-1]:
        row_max = jnp.maximum(row_max, m)
    local_factor = jnp.exp(local_max - row_max)
    total_numer = local_numer * spread(local_factor)
    total_denom = local_denom * local_factor
    for o_j, d_j, m_j in zip(part_mean[:-1], part_denom[:-1], part_max[:-1]):
        w_j = jnp.exp(m_j - row_max) * d_j
        total_numer = total_numer + o_j * spread(w_j)
        total_denom = total_denom + w_j
    attended = total_numer / spread(total_denom)
    return attended.astype(jnp.bfloat16)


def solution(mesh):
    placed = (
        P(("group", "seq"), "head"),
        P(("group", "seq"), "head"),
        P(("group", "seq"), "head"),
        P(("group", "seq"), "head"),
        P(("group", "seq"), "head"),
        P("group"),
        P("group"),
    )
    return jax.shard_map(
        on_device,
        mesh=mesh,
        in_specs=placed,
        out_specs=P(("group", "seq"), "head"),
        check_vma=False,
    )
```

```python
import functools

import jax
import jax.numpy as jnp
from jax import lax
from jax.experimental import pallas as pl
from jax.experimental.pallas import tpu as pltpu
from jax.sharding import PartitionSpec as P

HEAD_DIM = 128
SUB = 256
NEG_FILL = -1e30


def cache_kernel(seq_count, first, pieces, stack, len_ref, q_ref, k_ref, v_ref, *rest):
    out_ref = rest[-1]
    rank = lax.axis_index("seq")
    cache_rows = k_ref.shape[0]
    live = jnp.clip(len_ref[0] - rank * cache_rows, 0, cache_rows)
    rows = out_ref.shape[0]
    heads_q = (out_ref.shape[1] - 128) // HEAD_DIM
    heads_kv = k_ref.shape[1] // HEAD_DIM
    group = heads_q // heads_kv
    tiles = cache_rows // SUB
    scale = HEAD_DIM ** (-0.5)
    lane = lax.broadcasted_iota(jnp.int32, (rows, 128), 1)
    position = lax.broadcasted_iota(jnp.int32, (1, cache_rows), 1)
    extra = jnp.zeros((rows, 128), jnp.float32)

    def query_rows(h):
        cols = slice(h * HEAD_DIM, (h + 1) * HEAD_DIM)
        if pieces == 0:
            return q_ref[:, cols]
        piece = rows // pieces
        blocks = []
        for p in range(pieces):
            index = lax.rem(rank + first + p, seq_count)
            blocks.append(q_ref[pl.ds(pl.multiple_of(index * piece, piece), piece), cols])
        return jnp.concatenate(blocks, axis=0)

    keys_t = [k_ref[:, g * HEAD_DIM:(g + 1) * HEAD_DIM].T for g in range(heads_kv)]
    if stack > 1:
        units = [list(range(g * group, (g + 1) * group)) for g in range(heads_kv)]
    else:
        units = [[h] for h in range(heads_q)]
    for heads in units:
        g = heads[0] // group
        qx = jnp.concatenate([query_rows(h) for h in heads], axis=0)
        span = qx.shape[0]
        maxes, numers, denoms = [], [], []
        for b in range(tiles):
            kb = keys_t[g][:, b * SUB:(b + 1) * SUB]
            bias = jnp.where(position[:, b * SUB:(b + 1) * SUB] < live, 0.0, NEG_FILL)
            s = jnp.dot(qx, kb, preferred_element_type=jnp.float32) * scale + bias
            tm = jnp.max(s, axis=1, keepdims=True)
            w = jnp.exp(s - tm).astype(jnp.bfloat16)
            vb = v_ref[b * SUB:(b + 1) * SUB, g * HEAD_DIM:(g + 1) * HEAD_DIM]
            numers.append(jnp.dot(w, vb, preferred_element_type=jnp.float32))
            denoms.append(jnp.sum(w.astype(jnp.float32), axis=1, keepdims=True))
            maxes.append(tm)
        m = maxes[0]
        for tm in maxes[1:]:
            m = jnp.maximum(m, tm)
        top = jnp.floor(jnp.maximum(m, -60000.0) * 0.25 + 0.5) * 4.0
        numer = jnp.zeros((span, HEAD_DIM), jnp.float32)
        denom = jnp.zeros((span, 1), jnp.float32)
        for tm, nb, db in zip(maxes, numers, denoms):
            f = jnp.exp(tm - top)
            numer = numer + nb * f
            denom = denom + db * f
        mean = numer / jnp.where(denom > 0, denom, 1.0)
        ulp = jnp.exp2(jnp.floor(jnp.log2(jnp.where(denom > 0, denom, 1.0))) - 10.0)
        hi = jnp.where(denom > 0, jnp.round(denom / ulp) * ulp, 0.0)
        for i, h in enumerate(heads):
            rs = slice(i * rows, (i + 1) * rows)
            out_ref[:, h * HEAD_DIM:(h + 1) * HEAD_DIM] = mean[rs]
            extra = jnp.where(lane == h, hi[rs], extra)
            extra = jnp.where(lane == heads_q + h, denom[rs] - hi[rs], extra)
            extra = jnp.where(lane == 2 * heads_q + h, top[rs], extra)
    out_ref[:, heads_q * HEAD_DIM:] = extra


def to_half(part, qcols, heads_q):
    return part.astype(jnp.float16)


def cache_partials(cache_length, queries, keys, values, qcols, rows, block, first, pieces,
                   stack, seq_count, after=None):
    qrows, qcols_in = queries.shape
    cache_rows, kcols = keys.shape
    out_cols = qcols + 128
    heads_q = qcols // HEAD_DIM
    if pieces > 0 or block == qrows:
        q_spec = pl.BlockSpec((qrows, qcols), lambda i: (0, 0))
    else:
        q_spec = pl.BlockSpec((block, qcols), lambda i: (i, 0))
    in_specs = [
        pl.BlockSpec(memory_space=pltpu.SMEM),
        q_spec,
        pl.BlockSpec((cache_rows, kcols), lambda i: (0, 0)),
        pl.BlockSpec((cache_rows, kcols), lambda i: (0, 0)),
    ]
    operands = [cache_length, queries, keys, values]
    if after is not None:
        in_specs.append(pl.BlockSpec(memory_space=pl.ANY))
        operands.append(after)
    return pl.pallas_call(
        functools.partial(cache_kernel, seq_count, first, pieces, stack),
        grid=(rows // block,),
        in_specs=in_specs,
        out_specs=pl.BlockSpec((block, out_cols), lambda i: (i, 0)),
        out_shape=jax.ShapeDtypeStruct((rows, out_cols), jnp.float32),
        compiler_params=pltpu.CompilerParams(vmem_limit_bytes=16 * 1024 * 1024),
        cost_estimate=pl.CostEstimate(
            flops=4 * rows * cache_rows * qcols,
            transcendentals=rows * cache_rows * heads_q,
            bytes_accessed=2 * (rows * qcols + 2 * cache_rows * kcols) + 4 * rows * out_cols,
        ),
    )(*operands)


def on_device(
    new_queries, new_keys, new_values, cache_keys, cache_values, segment_ids, cache_length
):
    head_size = HEAD_DIM
    own_count = new_queries.shape[0]
    join_rows = segment_ids.shape[0]
    cache_rows = cache_keys.shape[0]
    heads_kv = cache_keys.shape[1] // head_size
    heads_q = new_queries.shape[1] // head_size
    group_size = heads_q // heads_kv
    qcols = heads_q * head_size
    kcols = heads_kv * head_size
    seq_count = lax.axis_size("seq")
    seq_rank = lax.axis_index("seq")
    score_scale = head_size ** (-0.5)

    packed = jnp.concatenate([new_queries, new_keys, new_values], axis=1)
    gathered = lax.all_gather(packed, "seq", axis=0, tiled=True)
    all_keys = gathered[:, qcols:qcols + kcols]
    all_values = gathered[:, qcols + kcols:]

    if seq_count <= 8:
        remote = cache_partials(
            cache_length, gathered, cache_keys, cache_values, qcols,
            (seq_count - 1) * own_count, (seq_count - 1) * own_count, 1, seq_count - 1, 1,
            seq_count,
        )
        parts = []
        for shift in sorted(range(1, seq_count), key=lambda s: (abs(2 * s - seq_count), -s)):
            piece = remote[(shift - 1) * own_count:shift * own_count]
            parts.append(
                lax.ppermute(
                    to_half(piece, qcols, heads_q),
                    "seq",
                    [(i, (i + shift) % seq_count) for i in range(seq_count)],
                ).astype(jnp.float32)
            )
        own = cache_partials(
            cache_length, new_queries, cache_keys, cache_values, qcols,
            own_count, own_count, 0, 0, group_size, seq_count, after=remote,
        )
        parts.append(own)
    else:
        partial = cache_partials(
            cache_length, gathered, cache_keys, cache_values, qcols,
            join_rows, min(join_rows, 256), 0, 0, 1, seq_count,
        )
        recv = lax.all_to_all(to_half(partial, qcols, heads_q), "seq", 0, 0, tiled=True)
        recv = recv.astype(jnp.float32)
        parts = [recv[j * own_count:(j + 1) * own_count] for j in range(seq_count)]
    part_mean = [p[:, :qcols] for p in parts]
    part_denom = [
        p[:, qcols:qcols + heads_q] + p[:, qcols + heads_q:qcols + 2 * heads_q] for p in parts
    ]
    part_max = [p[:, qcols + 2 * heads_q:qcols + 3 * heads_q] for p in parts]

    own_queries = new_queries.reshape(own_count, heads_kv, group_size, head_size)
    fresh_scores = (
        jnp.einsum(
            "cgrd,tgd->cgrt",
            own_queries,
            all_keys.reshape(join_rows, heads_kv, head_size),
            preferred_element_type=jnp.float32,
        )
        * score_scale
    )
    start_row = seq_rank * own_count
    own_positions = start_row + jnp.arange(own_count, dtype=jnp.int32)
    own_segments = lax.dynamic_slice_in_dim(segment_ids, start_row, own_count, 0)
    key_positions = jnp.arange(join_rows, dtype=jnp.int32)
    allowed = (key_positions[None, :] <= own_positions[:, None]) & (
        segment_ids[None, :] == own_segments[:, None]
    )
    allowed = allowed[:, None, None, :]
    fresh_max = jnp.max(jnp.where(allowed, fresh_scores, NEG_FILL), axis=-1)
    fresh_weights = jnp.exp(
        jnp.where(allowed, fresh_scores - fresh_max[..., None], NEG_FILL)
    ).astype(jnp.bfloat16)
    fresh_numer = jnp.einsum(
        "cgrt,tgd->cgrd",
        fresh_weights,
        all_values.reshape(join_rows, heads_kv, head_size),
        preferred_element_type=jnp.float32,
    ).reshape(own_count, qcols)
    fresh_denom = jnp.sum(fresh_weights.astype(jnp.float32), axis=-1).reshape(own_count, heads_q)
    fresh_max = fresh_max.reshape(own_count, heads_q)


    def spread(x):
        return jnp.broadcast_to(x[:, :, None], (own_count, heads_q, head_size)).reshape(
            own_count, qcols
        )

    own_mean, own_denom, own_max = part_mean[-1], part_denom[-1], part_max[-1]
    local_max = jnp.maximum(fresh_max, own_max)
    fresh_factor = jnp.exp(fresh_max - local_max)
    own_weight = jnp.exp(own_max - local_max) * own_denom
    local_numer = fresh_numer * spread(fresh_factor) + own_mean * spread(own_weight)
    local_denom = fresh_denom * fresh_factor + own_weight

    row_max = local_max
    for m in part_max[:-1]:
        row_max = jnp.maximum(row_max, m)
    local_factor = jnp.exp(local_max - row_max)
    total_numer = local_numer * spread(local_factor)
    total_denom = local_denom * local_factor
    for o_j, d_j, m_j in zip(part_mean[:-1], part_denom[:-1], part_max[:-1]):
        w_j = jnp.exp(m_j - row_max) * d_j
        total_numer = total_numer + o_j * spread(w_j)
        total_denom = total_denom + w_j
    attended = total_numer / spread(total_denom)
    return attended.astype(jnp.bfloat16)


def solution(mesh):
    placed = (
        P(("group", "seq"), "head"),
        P(("group", "seq"), "head"),
        P(("group", "seq"), "head"),
        P(("group", "seq"), "head"),
        P(("group", "seq"), "head"),
        P("group"),
        P("group"),
    )
    return jax.shard_map(
        on_device,
        mesh=mesh,
        in_specs=placed,
        out_specs=P(("group", "seq"), "head"),
        check_vma=False,
    )
```

```python
import functools

import jax
import jax.numpy as jnp
from jax import lax
from jax.experimental import pallas as pl
from jax.experimental.pallas import tpu as pltpu
from jax.sharding import PartitionSpec as P

HEAD_DIM = 128
SUB = 256
NEG_FILL = -1e30


def cache_kernel(seq_count, first, pieces, stack, len_ref, q_ref, k_ref, v_ref, *rest):
    out_ref = rest[-1]
    rank = lax.axis_index("seq")
    cache_rows = k_ref.shape[0]
    live = jnp.clip(len_ref[0] - rank * cache_rows, 0, cache_rows)
    rows = out_ref.shape[0]
    heads_q = (out_ref.shape[1] - 128) // HEAD_DIM
    heads_kv = k_ref.shape[1] // HEAD_DIM
    group = heads_q // heads_kv
    tiles = cache_rows // SUB
    scale = HEAD_DIM ** (-0.5)
    lane = lax.broadcasted_iota(jnp.int32, (rows, 128), 1)
    position = lax.broadcasted_iota(jnp.int32, (1, cache_rows), 1)
    extra = jnp.zeros((rows, 128), jnp.float32)

    def query_rows(h):
        cols = slice(h * HEAD_DIM, (h + 1) * HEAD_DIM)
        if pieces == 0:
            return q_ref[:, cols]
        piece = rows // pieces
        blocks = []
        for p in range(pieces):
            index = lax.rem(rank + first + p, seq_count)
            blocks.append(q_ref[pl.ds(pl.multiple_of(index * piece, piece), piece), cols])
        return jnp.concatenate(blocks, axis=0)

    keys_t = [k_ref[:, g * HEAD_DIM:(g + 1) * HEAD_DIM].T for g in range(heads_kv)]
    if stack > 1:
        units = [list(range(g * group, (g + 1) * group)) for g in range(heads_kv)]
    else:
        units = [[h] for h in range(heads_q)]
    for heads in units:
        g = heads[0] // group
        qx = jnp.concatenate([query_rows(h) for h in heads], axis=0)
        span = qx.shape[0]
        maxes, numers, denoms = [], [], []
        for b in range(tiles):
            kb = keys_t[g][:, b * SUB:(b + 1) * SUB]
            bias = jnp.where(position[:, b * SUB:(b + 1) * SUB] < live, 0.0, NEG_FILL)
            s = jnp.dot(qx, kb, preferred_element_type=jnp.float32) * scale + bias
            tm = jnp.max(s, axis=1, keepdims=True)
            w = jnp.exp(s - tm).astype(jnp.bfloat16)
            vb = v_ref[b * SUB:(b + 1) * SUB, g * HEAD_DIM:(g + 1) * HEAD_DIM]
            numers.append(jnp.dot(w, vb, preferred_element_type=jnp.float32))
            denoms.append(jnp.sum(w.astype(jnp.float32), axis=1, keepdims=True))
            maxes.append(tm)
        m = maxes[0]
        for tm in maxes[1:]:
            m = jnp.maximum(m, tm)
        top = jnp.floor(jnp.maximum(m, -60000.0) * 0.25 + 0.5) * 4.0
        numer = jnp.zeros((span, HEAD_DIM), jnp.float32)
        denom = jnp.zeros((span, 1), jnp.float32)
        for tm, nb, db in zip(maxes, numers, denoms):
            f = jnp.exp(tm - top)
            numer = numer + nb * f
            denom = denom + db * f
        mean = numer / jnp.where(denom > 0, denom, 1.0)
        ulp = jnp.exp2(jnp.floor(jnp.log2(jnp.where(denom > 0, denom, 1.0))) - 10.0)
        hi = jnp.where(denom > 0, jnp.round(denom / ulp) * ulp, 0.0)
        for i, h in enumerate(heads):
            rs = slice(i * rows, (i + 1) * rows)
            out_ref[:, h * HEAD_DIM:(h + 1) * HEAD_DIM] = mean[rs]
            extra = jnp.where(lane == h, hi[rs], extra)
            extra = jnp.where(lane == heads_q + h, denom[rs] - hi[rs], extra)
            extra = jnp.where(lane == 2 * heads_q + h, top[rs], extra)
    out_ref[:, heads_q * HEAD_DIM:] = extra


def to_half(part, qcols, heads_q):
    return part.astype(jnp.float16)


def cache_partials(cache_length, queries, keys, values, qcols, rows, block, first, pieces,
                   stack, seq_count, after=None):
    qrows, qcols_in = queries.shape
    cache_rows, kcols = keys.shape
    out_cols = qcols + 128
    heads_q = qcols // HEAD_DIM
    if pieces > 0 or block == qrows:
        q_spec = pl.BlockSpec((qrows, qcols), lambda i: (0, 0))
    else:
        q_spec = pl.BlockSpec((block, qcols), lambda i: (i, 0))
    in_specs = [
        pl.BlockSpec(memory_space=pltpu.SMEM),
        q_spec,
        pl.BlockSpec((cache_rows, kcols), lambda i: (0, 0)),
        pl.BlockSpec((cache_rows, kcols), lambda i: (0, 0)),
    ]
    operands = [cache_length, queries, keys, values]
    if after is not None:
        in_specs.append(pl.BlockSpec(memory_space=pl.ANY))
        operands.append(after)
    return pl.pallas_call(
        functools.partial(cache_kernel, seq_count, first, pieces, stack),
        grid=(rows // block,),
        in_specs=in_specs,
        out_specs=pl.BlockSpec((block, out_cols), lambda i: (i, 0)),
        out_shape=jax.ShapeDtypeStruct((rows, out_cols), jnp.float32),
        compiler_params=pltpu.CompilerParams(vmem_limit_bytes=8 * 1024 * 1024),
        cost_estimate=pl.CostEstimate(
            flops=4 * rows * cache_rows * qcols,
            transcendentals=rows * cache_rows * heads_q,
            bytes_accessed=2 * (rows * qcols + 2 * cache_rows * kcols) + 4 * rows * out_cols,
        ),
    )(*operands)


def on_device(
    new_queries, new_keys, new_values, cache_keys, cache_values, segment_ids, cache_length
):
    head_size = HEAD_DIM
    own_count = new_queries.shape[0]
    join_rows = segment_ids.shape[0]
    cache_rows = cache_keys.shape[0]
    heads_kv = cache_keys.shape[1] // head_size
    heads_q = new_queries.shape[1] // head_size
    group_size = heads_q // heads_kv
    qcols = heads_q * head_size
    kcols = heads_kv * head_size
    seq_count = lax.axis_size("seq")
    seq_rank = lax.axis_index("seq")
    score_scale = head_size ** (-0.5)

    packed = jnp.concatenate([new_queries, new_keys, new_values], axis=1)
    gathered = lax.all_gather(packed, "seq", axis=0, tiled=True)
    all_keys = gathered[:, qcols:qcols + kcols]
    all_values = gathered[:, qcols + kcols:]

    if seq_count <= 8:
        remote = cache_partials(
            cache_length, gathered, cache_keys, cache_values, qcols,
            (seq_count - 1) * own_count, (seq_count - 1) * own_count, 1, seq_count - 1, 1,
            seq_count,
        )
        parts = []
        for shift in sorted(range(1, seq_count), key=lambda s: (abs(2 * s - seq_count), -s)):
            piece = remote[(shift - 1) * own_count:shift * own_count]
            parts.append(
                lax.ppermute(
                    to_half(piece, qcols, heads_q),
                    "seq",
                    [(i, (i + shift) % seq_count) for i in range(seq_count)],
                ).astype(jnp.float32)
            )
        own = cache_partials(
            cache_length, new_queries, cache_keys, cache_values, qcols,
            own_count, own_count, 0, 0, group_size, seq_count, after=remote,
        )
        parts.append(own)
    else:
        partial = cache_partials(
            cache_length, gathered, cache_keys, cache_values, qcols,
            join_rows, min(join_rows, 256), 0, 0, 1, seq_count,
        )
        recv = lax.all_to_all(to_half(partial, qcols, heads_q), "seq", 0, 0, tiled=True)
        recv = recv.astype(jnp.float32)
        parts = [recv[j * own_count:(j + 1) * own_count] for j in range(seq_count)]
    part_mean = [p[:, :qcols] for p in parts]
    part_denom = [
        p[:, qcols:qcols + heads_q] + p[:, qcols + heads_q:qcols + 2 * heads_q] for p in parts
    ]
    part_max = [p[:, qcols + 2 * heads_q:qcols + 3 * heads_q] for p in parts]

    own_queries = new_queries.reshape(own_count, heads_kv, group_size, head_size)
    fresh_scores = (
        jnp.einsum(
            "cgrd,tgd->cgrt",
            own_queries,
            all_keys.reshape(join_rows, heads_kv, head_size),
            preferred_element_type=jnp.float32,
        )
        * score_scale
    )
    start_row = seq_rank * own_count
    own_positions = start_row + jnp.arange(own_count, dtype=jnp.int32)
    own_segments = lax.dynamic_slice_in_dim(segment_ids, start_row, own_count, 0)
    key_positions = jnp.arange(join_rows, dtype=jnp.int32)
    allowed = (key_positions[None, :] <= own_positions[:, None]) & (
        segment_ids[None, :] == own_segments[:, None]
    )
    allowed = allowed[:, None, None, :]
    fresh_max = jnp.max(jnp.where(allowed, fresh_scores, NEG_FILL), axis=-1)
    fresh_weights = jnp.exp(
        jnp.where(allowed, fresh_scores - fresh_max[..., None], NEG_FILL)
    ).astype(jnp.bfloat16)
    fresh_numer = jnp.einsum(
        "cgrt,tgd->cgrd",
        fresh_weights,
        all_values.reshape(join_rows, heads_kv, head_size),
        preferred_element_type=jnp.float32,
    ).reshape(own_count, qcols)
    fresh_denom = jnp.sum(fresh_weights.astype(jnp.float32), axis=-1).reshape(own_count, heads_q)
    fresh_max = fresh_max.reshape(own_count, heads_q)


    def spread(x):
        return jnp.broadcast_to(x[:, :, None], (own_count, heads_q, head_size)).reshape(
            own_count, qcols
        )

    own_mean, own_denom, own_max = part_mean[-1], part_denom[-1], part_max[-1]
    local_max = jnp.maximum(fresh_max, own_max)
    fresh_factor = jnp.exp(fresh_max - local_max)
    own_weight = jnp.exp(own_max - local_max) * own_denom
    local_numer = fresh_numer * spread(fresh_factor) + own_mean * spread(own_weight)
    local_denom = fresh_denom * fresh_factor + own_weight

    row_max = local_max
    for m in part_max[:-1]:
        row_max = jnp.maximum(row_max, m)
    local_factor = jnp.exp(local_max - row_max)
    total_numer = local_numer * spread(local_factor)
    total_denom = local_denom * local_factor
    for o_j, d_j, m_j in zip(part_mean[:-1], part_denom[:-1], part_max[:-1]):
        w_j = jnp.exp(m_j - row_max) * d_j
        total_numer = total_numer + o_j * spread(w_j)
        total_denom = total_denom + w_j
    attended = total_numer / spread(total_denom)
    return attended.astype(jnp.bfloat16)


def solution(mesh):
    placed = (
        P(("group", "seq"), "head"),
        P(("group", "seq"), "head"),
        P(("group", "seq"), "head"),
        P(("group", "seq"), "head"),
        P(("group", "seq"), "head"),
        P("group"),
        P("group"),
    )
    return jax.shard_map(
        on_device,
        mesh=mesh,
        in_specs=placed,
        out_specs=P(("group", "seq"), "head"),
        check_vma=False,
    )
```

```python
import functools

import jax
import jax.numpy as jnp
from jax import lax
from jax.experimental import pallas as pl
from jax.experimental.pallas import tpu as pltpu
from jax.sharding import PartitionSpec as P

HEAD_DIM = 128
SUB = 256
NEG_FILL = -1e30


def cache_kernel(seq_count, first, pieces, stack, len_ref, q_ref, k_ref, v_ref, *rest):
    out_ref = rest[-1]
    rank = lax.axis_index("seq")
    cache_rows = k_ref.shape[0]
    live = jnp.clip(len_ref[0] - rank * cache_rows, 0, cache_rows)
    rows = out_ref.shape[0]
    heads_q = (out_ref.shape[1] - 128) // HEAD_DIM
    heads_kv = k_ref.shape[1] // HEAD_DIM
    group = heads_q // heads_kv
    tiles = cache_rows // SUB
    scale = HEAD_DIM ** (-0.5)
    lane = lax.broadcasted_iota(jnp.int32, (rows, 128), 1)
    position = lax.broadcasted_iota(jnp.int32, (1, cache_rows), 1)
    extra = jnp.zeros((rows, 128), jnp.float32)

    def query_rows(h):
        cols = slice(h * HEAD_DIM, (h + 1) * HEAD_DIM)
        if pieces == 0:
            return q_ref[:, cols]
        piece = rows // pieces
        blocks = []
        for p in range(pieces):
            index = lax.rem(rank + first + p, seq_count)
            blocks.append(q_ref[pl.ds(pl.multiple_of(index * piece, piece), piece), cols])
        return jnp.concatenate(blocks, axis=0)

    keys_t = [k_ref[:, g * HEAD_DIM:(g + 1) * HEAD_DIM].T for g in range(heads_kv)]
    if stack > 1:
        units = [list(range(g * group, (g + 1) * group)) for g in range(heads_kv)]
    else:
        units = [[h] for h in range(heads_q)]
    for heads in units:
        g = heads[0] // group
        qx = jnp.concatenate([query_rows(h) for h in heads], axis=0)
        span = qx.shape[0]
        maxes, numers, denoms = [], [], []
        for b in range(tiles):
            kb = keys_t[g][:, b * SUB:(b + 1) * SUB]
            bias = jnp.where(position[:, b * SUB:(b + 1) * SUB] < live, 0.0, NEG_FILL)
            s = jnp.dot(qx, kb, preferred_element_type=jnp.float32) * scale + bias
            tm = jnp.max(s, axis=1, keepdims=True)
            w = jnp.exp(s - tm).astype(jnp.bfloat16)
            vb = v_ref[b * SUB:(b + 1) * SUB, g * HEAD_DIM:(g + 1) * HEAD_DIM]
            numers.append(jnp.dot(w, vb, preferred_element_type=jnp.float32))
            denoms.append(jnp.sum(w.astype(jnp.float32), axis=1, keepdims=True))
            maxes.append(tm)
        m = maxes[0]
        for tm in maxes[1:]:
            m = jnp.maximum(m, tm)
        top = jnp.floor(jnp.maximum(m, -60000.0) * 0.25 + 0.5) * 4.0
        numer = jnp.zeros((span, HEAD_DIM), jnp.float32)
        denom = jnp.zeros((span, 1), jnp.float32)
        for tm, nb, db in zip(maxes, numers, denoms):
            f = jnp.exp(tm - top)
            numer = numer + nb * f
            denom = denom + db * f
        mean = numer / jnp.where(denom > 0, denom, 1.0)
        ulp = jnp.exp2(jnp.floor(jnp.log2(jnp.where(denom > 0, denom, 1.0))) - 10.0)
        hi = jnp.where(denom > 0, jnp.round(denom / ulp) * ulp, 0.0)
        for i, h in enumerate(heads):
            rs = slice(i * rows, (i + 1) * rows)
            out_ref[:, h * HEAD_DIM:(h + 1) * HEAD_DIM] = mean[rs]
            extra = jnp.where(lane == h, hi[rs], extra)
            extra = jnp.where(lane == heads_q + h, denom[rs] - hi[rs], extra)
            extra = jnp.where(lane == 2 * heads_q + h, top[rs], extra)
    out_ref[:, heads_q * HEAD_DIM:] = extra


def to_half(part, qcols, heads_q):
    return part.astype(jnp.float16)


def cache_partials(cache_length, queries, keys, values, qcols, rows, block, first, pieces,
                   stack, seq_count, after=None):
    qrows, qcols_in = queries.shape
    cache_rows, kcols = keys.shape
    out_cols = qcols + 128
    heads_q = qcols // HEAD_DIM
    if pieces > 0 or block == qrows:
        q_spec = pl.BlockSpec((qrows, qcols), lambda i: (0, 0))
    else:
        q_spec = pl.BlockSpec((block, qcols), lambda i: (i, 0))
    in_specs = [
        pl.BlockSpec(memory_space=pltpu.SMEM),
        q_spec,
        pl.BlockSpec((cache_rows, kcols), lambda i: (0, 0)),
        pl.BlockSpec((cache_rows, kcols), lambda i: (0, 0)),
    ]
    operands = [cache_length, queries, keys, values]
    if after is not None:
        in_specs.append(pl.BlockSpec(memory_space=pl.ANY))
        operands.append(after)
    return pl.pallas_call(
        functools.partial(cache_kernel, seq_count, first, pieces, stack),
        grid=(rows // block,),
        in_specs=in_specs,
        out_specs=pl.BlockSpec((block, out_cols), lambda i: (i, 0)),
        out_shape=jax.ShapeDtypeStruct((rows, out_cols), jnp.float32),
        compiler_params=pltpu.CompilerParams(vmem_limit_bytes=16 * 1024 * 1024),
        cost_estimate=pl.CostEstimate(
            flops=4 * rows * cache_rows * qcols,
            transcendentals=rows * cache_rows * heads_q,
            bytes_accessed=2 * (rows * qcols + 2 * cache_rows * kcols) + 4 * rows * out_cols,
        ),
    )(*operands)


def on_device(
    new_queries, new_keys, new_values, cache_keys, cache_values, segment_ids, cache_length
):
    head_size = HEAD_DIM
    own_count = new_queries.shape[0]
    join_rows = segment_ids.shape[0]
    cache_rows = cache_keys.shape[0]
    heads_kv = cache_keys.shape[1] // head_size
    heads_q = new_queries.shape[1] // head_size
    group_size = heads_q // heads_kv
    qcols = heads_q * head_size
    kcols = heads_kv * head_size
    seq_count = lax.axis_size("seq")
    seq_rank = lax.axis_index("seq")
    score_scale = head_size ** (-0.5)

    packed = jnp.concatenate([new_queries, new_keys, new_values], axis=1)
    gathered = lax.all_gather(packed, "seq", axis=0, tiled=True)
    all_keys = gathered[:, qcols:qcols + kcols]
    all_values = gathered[:, qcols + kcols:]

    if seq_count <= 8:
        remote = cache_partials(
            cache_length, gathered, cache_keys, cache_values, qcols,
            (seq_count - 1) * own_count, (seq_count - 1) * own_count, 1, seq_count - 1, 1,
            seq_count,
        )
        parts = []
        for shift in sorted(range(1, seq_count), key=lambda s: (abs(2 * s - seq_count), -s)):
            piece = remote[(shift - 1) * own_count:shift * own_count]
            parts.append(
                lax.ppermute(
                    to_half(piece, qcols, heads_q),
                    "seq",
                    [(i, (i + shift) % seq_count) for i in range(seq_count)],
                )
            )
        own = cache_partials(
            cache_length, new_queries, cache_keys, cache_values, qcols,
            own_count, own_count, 0, 0, group_size, seq_count, after=remote,
        )
        parts.append(own)
    else:
        partial = cache_partials(
            cache_length, gathered, cache_keys, cache_values, qcols,
            join_rows, min(join_rows, 256), 0, 0, 1, seq_count,
        )
        recv = lax.all_to_all(to_half(partial, qcols, heads_q), "seq", 0, 0, tiled=True)
        recv = recv.astype(jnp.float32)
        parts = [recv[j * own_count:(j + 1) * own_count] for j in range(seq_count)]
    part_mean = [p[:, :qcols].astype(jnp.float32) for p in parts]
    part_denom = [
        p[:, qcols:qcols + heads_q].astype(jnp.float32)
        + p[:, qcols + heads_q:qcols + 2 * heads_q].astype(jnp.float32)
        for p in parts
    ]
    part_max = [p[:, qcols + 2 * heads_q:qcols + 3 * heads_q].astype(jnp.float32) for p in parts]

    own_queries = new_queries.reshape(own_count, heads_kv, group_size, head_size)
    fresh_scores = (
        jnp.einsum(
            "cgrd,tgd->cgrt",
            own_queries,
            all_keys.reshape(join_rows, heads_kv, head_size),
            preferred_element_type=jnp.float32,
        )
        * score_scale
    )
    start_row = seq_rank * own_count
    own_positions = start_row + jnp.arange(own_count, dtype=jnp.int32)
    own_segments = lax.dynamic_slice_in_dim(segment_ids, start_row, own_count, 0)
    key_positions = jnp.arange(join_rows, dtype=jnp.int32)
    allowed = (key_positions[None, :] <= own_positions[:, None]) & (
        segment_ids[None, :] == own_segments[:, None]
    )
    allowed = allowed[:, None, None, :]
    fresh_max = jnp.max(jnp.where(allowed, fresh_scores, NEG_FILL), axis=-1)
    fresh_weights = jnp.exp(
        jnp.where(allowed, fresh_scores - fresh_max[..., None], NEG_FILL)
    ).astype(jnp.bfloat16)
    fresh_numer = jnp.einsum(
        "cgrt,tgd->cgrd",
        fresh_weights,
        all_values.reshape(join_rows, heads_kv, head_size),
        preferred_element_type=jnp.float32,
    ).reshape(own_count, qcols)
    fresh_denom = jnp.sum(fresh_weights.astype(jnp.float32), axis=-1).reshape(own_count, heads_q)
    fresh_max = fresh_max.reshape(own_count, heads_q)


    def spread(x):
        return jnp.broadcast_to(x[:, :, None], (own_count, heads_q, head_size)).reshape(
            own_count, qcols
        )

    own_mean, own_denom, own_max = part_mean[-1], part_denom[-1], part_max[-1]
    local_max = jnp.maximum(fresh_max, own_max)
    fresh_factor = jnp.exp(fresh_max - local_max)
    own_weight = jnp.exp(own_max - local_max) * own_denom
    local_numer = fresh_numer * spread(fresh_factor) + own_mean * spread(own_weight)
    local_denom = fresh_denom * fresh_factor + own_weight

    row_max = local_max
    for m in part_max[:-1]:
        row_max = jnp.maximum(row_max, m)
    local_factor = jnp.exp(local_max - row_max)
    total_numer = local_numer * spread(local_factor)
    total_denom = local_denom * local_factor
    for o_j, d_j, m_j in zip(part_mean[:-1], part_denom[:-1], part_max[:-1]):
        w_j = jnp.exp(m_j - row_max) * d_j
        total_numer = total_numer + o_j * spread(w_j)
        total_denom = total_denom + w_j
    attended = total_numer / spread(total_denom)
    return attended.astype(jnp.bfloat16)


def solution(mesh):
    placed = (
        P(("group", "seq"), "head"),
        P(("group", "seq"), "head"),
        P(("group", "seq"), "head"),
        P(("group", "seq"), "head"),
        P(("group", "seq"), "head"),
        P("group"),
        P("group"),
    )
    return jax.shard_map(
        on_device,
        mesh=mesh,
        in_specs=placed,
        out_specs=P(("group", "seq"), "head"),
        check_vma=False,
    )
```
